128 devices in a mesh: req: 16 (over y, x), head: 8 (over z, core).
Axes of the slice: x: 4, y: 4, z: 4, core: 2. Of those that a mesh axis runs over, the one named last changes fastest.
Arguments:
- hidden_in: bfloat16 [4864, 3072], P('req', 'head'), may hold values from -6 to 6
- dec_query: bfloat16 [768, 3072], P('req', 'head'), may hold values from -5.5 to 5.5
- dec_key: bfloat16 [768, 3072], P('req', 'head'), may hold values from -6 to 6
- dec_value: bfloat16 [768, 3072], P('req', 'head'), may hold values from -6 to 6
- pre_query: bfloat16 [4096, 3072], P('req', 'head'), may hold values from -5.5 to 5.5
- pre_key: bfloat16 [4096, 3072], P('req', 'head'), may hold values from -6 to 6
- pre_value: bfloat16 [4096, 3072], P('req', 'head'), may hold values from -6 to 6
- cache_key: bfloat16 [32, 2048, 3072], P('req', None, 'head'), may hold values from -5.5 to 5.5
- cache_value: bfloat16 [32, 2048, 3072], P('req', None, 'head'), may hold values from -6 to 6
- group_of: int32 [768, 1], replicated, may hold values from 0 to 31; in each aligned block of 768 rows (0 to 767, 768 to 1535, ...) at most 48 rows name the same one
- cache_length: int32 [32], P('req'), may hold values from 256 to 2048, as said below
- stretch_start: int32 [16], P('req'), may hold values from 256 to 2048, as said below
- row_owner: int32 [4864, 1], P('req'), may hold values from 0 to 15; in each aligned block of 304 rows (0 to 303, 304 to 607, ...) at most 40 rows name the same one
- out_weight: bfloat16 [3072, 3072], P('head'), may hold values from -0.109375 to 0.109375
- norm_gain: float32 [3072], replicated, may hold values from 0.1 to 1.9
- gate_weight: bfloat16 [3072, 4096], P(None, 'head'), may hold values from -0.109375 to 0.109375
- up_weight: bfloat16 [3072, 4096], P(None, 'head'), may hold values from -0.109375 to 0.109375
- down_weight: bfloat16 [4096, 3072], P('head'), may hold values from -0.09375 to 0.09375
Outputs:
- layer_out: bfloat16 [10240, 3072], P(('req', 'head'))
The draws below stay inside these ranges and needn't reach their ends.
Inputs may be any that keep to these rules, and one draw needn't show every extreme that they name: `group_of`: at most 48 requests share a cache group, exactly 48 in some group; every group has a request. `cache_length`: some group has all 2048 rows valid. `stretch_start`: some stretch follows all 2048 cached rows. `row_owner`: among the 304 rows of one index of req at most 40 share an owner, exactly 40 on some index.
All inputs are finite; a program needn't handle non-finite values.
Results may differ from the reference program's by a relative error of at most 0.02.
Values may be sent and summed in bfloat16 or wider, within the bound.
No kernel may reach another device: no remote copies, remote signals or barrier semaphores. Data moves between devices by JAX's collectives and lax.ppermute only.
A program may use at most 128 MiB of HBM per device.

```python
import math
import jax
import jax.numpy as jnp
import numpy as np
from jax import lax

D = 3072
H = 32
HD = 96
FF_WIN = 4096
G_DEV = 2
REQ_DEV = 48
STRETCH = 256
L = 2048
BLOCKS = 8
OWNERS = 16
GROUPS = 32
REQS = 768
CAP = 48
STRETCHES = 16
ROWS = 304
SLOT = 40
OWNER_ROWS = 640
ALL_ROWS = 4864
OUT_ROWS = 10240
N_REQ = 16


def query_rows(key, salt, count):
    values_drawn = jnp.clip(jax.random.normal(jax.random.fold_in(key, salt), (count, D), jnp.float32), -5.5, 5.5)
    return values_drawn


def capped_lengths(key, salt, count):
    drawn = jax.random.randint(jax.random.fold_in(key, salt), (count,), max(2, L // 8), L + 1, dtype=jnp.int32)
    chosen_spot = jax.random.randint(jax.random.fold_in(key, salt + 1), (), 0, count, dtype=jnp.int32)
    return drawn.at[chosen_spot].set(L)


def draw_dec_query(key, part):
    return query_rows(key, 21, REQS).astype(jnp.bfloat16)


def draw_pre_query(key, part):
    return query_rows(key, 22, STRETCHES * STRETCH).astype(jnp.bfloat16)


def draw_cache_key(key, part):
    values_drawn = jnp.clip(jax.random.normal(jax.random.fold_in(key, 23), (GROUPS, L, D), jnp.float32), -5.5, 5.5)
    return values_drawn.astype(jnp.bfloat16)


def draw_cache_length(key, part):
    return capped_lengths(key, 31, GROUPS)


def draw_stretch_start(key, part):
    return capped_lengths(key, 41, STRETCHES)


def block_scale(key, dims, split, low, top_value):
    gain, own = 1.0, jax.random.fold_in(key, 6)
    for position, shards_of in split:
        heights = jnp.exp(jax.random.uniform(jax.random.fold_in(own, position), (shards_of,), jnp.float32, low / len(split), top_value / len(split)))
        gain = gain * jnp.repeat(heights, dims[position] // shards_of).reshape([-1 if axis == position else 1 for axis in range(len(dims))])
    return gain


def routed_block(stream_key, own, number, rows, number_of, top, reach, lean):
    order = jax.random.permutation(stream_key, number_of)
    crowded, common = load_shares(number_of, rows * top, reach, lean, True), load_shares(number_of, rows * top, reach, lean, False)
    places = jnp.arange(number_of)

    def named(sizes, offset_by):
        used = int((sizes > 0).sum())
        fixed = max(1, used // 4)
        moved = fixed + (places - fixed + offset_by * (used - fixed)) % max(1, number_of - fixed)
        return jnp.zeros((number_of,), jnp.int32).at[order[jnp.where(places < fixed, places, moved)]].set(jnp.asarray(sizes, jnp.int32))

    sizes = jnp.where(number % 4 == 0, named(crowded, number // 4), named(common, number - number // 4 - 1))
    mixed = jax.random.permutation(jax.random.fold_in(own, 3), number_of)
    source_of, receiver = mixed[0:number_of // 2 * 2:2], mixed[1:number_of // 2 * 2:2]
    margin = jnp.minimum(sizes[source_of] - 1, reach - sizes[receiver]) // 2
    margin = jnp.where((source_of == order[0]) | (receiver == order[0]) | (sizes[receiver] == 0), 0, jnp.maximum(margin, 0))
    moved = jax.random.randint(jax.random.fold_in(own, 4), (number_of // 2,), 0, 1 << 20) % (margin + 1)
    sizes = sizes.at[source_of].add(-moved).at[receiver].add(moved)
    labels = jnp.searchsorted(jnp.cumsum(sizes), jnp.arange(rows * top), side="right").astype(jnp.int32)
    grid = labels.reshape(top, rows).T
    grid = grid[jax.random.permutation(jax.random.fold_in(own, 1), rows)]
    offset_by = jax.random.randint(jax.random.fold_in(own, 2), (rows, 1), 0, top)
    return jnp.take_along_axis(grid, (jnp.arange(top)[None, :] + offset_by) % top, axis=1)


def load_shares(count, total, reach, skew, full):
    loads = [(1 << 20) // math.isqrt(standing ** skew) + 1 for standing in range(1, count + 1)]
    largest = reach if full else min(reach, max(-(-total // count), total * loads[0] // sum(loads)))
    least = 1 if total - largest >= count - 1 else 0
    given, spare = [largest] + [least] * (count - 1), total - largest - least * (count - 1)
    while spare > 0:
        movable = [i for i in range(1, count) if given[i] < largest] or [i for i in range(1, count) if given[i] < reach]
        whole, left = sum([loads[i] for i in movable]), spare
        for i in movable:
            addition = min(reach - given[i], max(1, left * loads[i] // whole), spare)
            given[i] = given[i] + addition
            spare = spare - addition
    return np.array(given)


def noise(key, dims, deviation, reach, cuts=(), held_as=jnp.bfloat16):
    values = jax.random.normal(key, dims, jnp.float32) * deviation
    if len(cuts) > 0:
        values = block_scale(key, dims, cuts, -0.22, 0.18) * values
    return jnp.clip(values, min=-reach, max=reach).astype(held_as)


def setup_inputs(seed: int = 0) -> dict:
    arg_keys = jax.random.split(jax.random.key(seed), 19)
    hidden_in = noise(arg_keys[0], (ALL_ROWS, D), 1.0, 6.0, ((0, 16), (1, 8)))
    dec_query = draw_dec_query(jax.random.fold_in(arg_keys[18], 71), 0)
    dec_key = noise(arg_keys[2], (REQS, D), 1.5, 6.0, ((0, 16), (1, 8)))
    dec_value = noise(arg_keys[3], (REQS, D), 1.0, 6.0, ((0, 16), (1, 8)))
    pre_query = draw_pre_query(jax.random.fold_in(arg_keys[18], 71), 0)
    pre_key = noise(arg_keys[5], (STRETCHES * STRETCH, D), 1.0, 6.0, ((0, 16), (1, 8)))
    pre_value = noise(arg_keys[6], (STRETCHES * STRETCH, D), 1.0, 6.0, ((0, 16), (1, 8)))
    cache_key = draw_cache_key(jax.random.fold_in(arg_keys[18], 71), 0)
    cache_value = noise(arg_keys[8], (GROUPS, L, D), 1.0, 6.0, ((0, 16), (2, 8)))
    group_of_keys = jax.random.split(jax.random.fold_in(arg_keys[9], 1), REQS // REQS)
    group_of_turns = jax.random.permutation(jax.random.fold_in(arg_keys[9], 3), REQS // REQS)
    group_of = jax.vmap(lambda own, number: routed_block(jax.random.fold_in(arg_keys[9], 2), own, number, REQS, GROUPS, 1, CAP, 2))(group_of_keys, group_of_turns).reshape((REQS, 1))
    cache_length = draw_cache_length(jax.random.fold_in(arg_keys[18], 71), 0)
    stretch_start = draw_stretch_start(jax.random.fold_in(arg_keys[18], 71), 0)
    row_owner_keys = jax.random.split(jax.random.fold_in(arg_keys[12], 1), ALL_ROWS // ROWS)
    row_owner_turns = jax.random.permutation(jax.random.fold_in(arg_keys[12], 3), ALL_ROWS // ROWS)
    row_owner = jax.vmap(lambda own, number: routed_block(jax.random.fold_in(arg_keys[12], 2), own, number, ROWS, OWNERS, 1, SLOT, 1))(row_owner_keys, row_owner_turns).reshape((ALL_ROWS, 1))
    out_weight = noise(arg_keys[13], (D, D), D ** -0.5, 0.109375, ((0, 8),))
    norm_gain = jnp.clip(1.0 + 0.18 * jax.random.normal(arg_keys[14], (D,), jnp.float32), 0.1, 1.9)
    gate_weight = noise(arg_keys[15], (D, FF_WIN), D ** -0.5, 0.109375, ((1, 8),))
    up_weight = noise(arg_keys[16], (D, FF_WIN), D ** -0.5, 0.109375, ((1, 8),))
    down_weight = noise(arg_keys[17], (FF_WIN, D), FF_WIN ** -0.5, 0.09375, ((0, 8),))
    return {"hidden_in": hidden_in, "dec_query": dec_query, "dec_key": dec_key, "dec_value": dec_value, "pre_query": pre_query, "pre_key": pre_key, "pre_value": pre_value, "cache_key": cache_key, "cache_value": cache_value, "group_of": group_of, "cache_length": cache_length, "stretch_start": stretch_start, "row_owner": row_owner, "out_weight": out_weight, "norm_gain": norm_gain, "gate_weight": gate_weight, "up_weight": up_weight, "down_weight": down_weight}


def rounded_softmax(scores):
    highest = lax.optimization_barrier(jnp.max(scores, axis=-1, keepdims=True))
    raised = jnp.exp(scores - highest)
    weights = (raised / lax.optimization_barrier(jnp.sum(raised, axis=-1, keepdims=True))).astype(jnp.bfloat16)
    weights = lax.optimization_barrier(weights)
    return weights.astype(jnp.float32)

def reference(hidden_in, dec_query, dec_key, dec_value, pre_query, pre_key, pre_value, cache_key, cache_value, group_of, cache_length, stretch_start, row_owner, out_weight, norm_gain, gate_weight, up_weight, down_weight):
    factor = 1.0 / math.sqrt(HD)
    positions = jnp.arange(L)

    def decode_one(record):
        one_query, own_key, own_value, which_group = record
        keys_cache = lax.dynamic_index_in_dim(cache_key, which_group, 0, keepdims=False).astype(jnp.float32).reshape(L, H, HD)
        values_cache = lax.dynamic_index_in_dim(cache_value, which_group, 0, keepdims=False).astype(jnp.float32).reshape(L, H, HD)
        heads_q = one_query.astype(jnp.float32).reshape(H, HD)
        cache_scores = jnp.einsum('hd,khd->hk', heads_q, keys_cache) * factor
        own_scores = lax.optimization_barrier(jnp.sum(heads_q * own_key.astype(jnp.float32).reshape(H, HD), axis=-1)) * factor
        valid_rows = lax.dynamic_index_in_dim(cache_length, which_group, 0, keepdims=False)
        cache_scores = jnp.where((positions < valid_rows)[None, :], cache_scores, -jnp.inf)
        scores = jnp.concatenate([cache_scores, own_scores[:, None]], axis=1)
        weights = rounded_softmax(scores)
        blended = jnp.einsum('hk,khd->hd', weights[:, :L], values_cache) + weights[:, L:] * own_value.astype(jnp.float32).reshape(H, HD)
        return blended.reshape(D).astype(jnp.bfloat16)
    dec_attn = lax.map(decode_one, (dec_query, dec_key, dec_value, group_of[:, 0]))
    columns = jnp.arange(L + STRETCH)
    row_numbers = jnp.arange(STRETCH)

    def prefill_one(record):
        stretch_q, stretch_k, stretch_v, prefix_rows, which_group = record
        keys_all = jnp.concatenate([lax.dynamic_index_in_dim(cache_key, which_group, 0, keepdims=False), stretch_k], axis=0)
        values_all = jnp.concatenate([lax.dynamic_index_in_dim(cache_value, which_group, 0, keepdims=False), stretch_v], axis=0)
        keys_all = keys_all.astype(jnp.float32).reshape(L + STRETCH, H, HD)
        values_all = values_all.astype(jnp.float32).reshape(L + STRETCH, H, HD)
        heads_q = stretch_q.astype(jnp.float32).reshape(STRETCH, H, HD)
        scores = jnp.einsum('qhd,khd->hqk', heads_q, keys_all) * factor
        allowed = jnp.where(columns[None, :] < L, columns[None, :] < prefix_rows, columns[None, :] - L <= row_numbers[:, None])
        scores = jnp.where(allowed[None], scores, -jnp.inf)
        weights = rounded_softmax(scores)
        blended = jnp.einsum('hqk,khd->qhd', weights, values_all)
        return blended.reshape(STRETCH, D).astype(jnp.bfloat16)
    stretch_groups = (jnp.arange(STRETCHES) * G_DEV).astype(jnp.int32)
    pre_attn = lax.map(prefill_one, (pre_query.reshape(STRETCHES, STRETCH, D), pre_key.reshape(STRETCHES, STRETCH, D), pre_value.reshape(STRETCHES, STRETCH, D), stretch_start, stretch_groups))
    attn_rows = jnp.concatenate([dec_attn.reshape(N_REQ, REQ_DEV, D), pre_attn.reshape(N_REQ, STRETCH, D)], axis=1).reshape(ALL_ROWS, D)
    block_width = D // BLOCKS
    summed = jnp.zeros((ALL_ROWS, D), jnp.float32)
    for blocknum in range(BLOCKS):
        first_col = blocknum * block_width
        partial_value = jnp.dot(attn_rows[:, first_col:first_col + block_width], out_weight[first_col:first_col + block_width], preferred_element_type=jnp.float32)
        partial_value = partial_value.at[:, first_col:first_col + block_width].add(hidden_in[:, first_col:first_col + block_width].astype(jnp.float32))
        rounded = lax.optimization_barrier(partial_value.astype(jnp.bfloat16))
        summed = summed + rounded.astype(jnp.float32)
    residual = summed.astype(jnp.bfloat16)
    residual_wide = residual.astype(jnp.float32)
    squares = lax.optimization_barrier(jnp.mean(jnp.square(residual_wide), axis=-1, keepdims=True))
    normed = (residual_wide * lax.rsqrt(squares + 1e-05) * norm_gain.astype(jnp.float32)).astype(jnp.bfloat16)
    gate_act = jnp.dot(normed, gate_weight, preferred_element_type=jnp.float32)
    up_act = jnp.dot(normed, up_weight, preferred_element_type=jnp.float32)
    hidden = (jax.nn.silu(gate_act) * up_act).astype(jnp.bfloat16)
    ff_width = FF_WIN // BLOCKS
    down_sum = jnp.zeros((ALL_ROWS, D), jnp.float32)
    for blocknum in range(BLOCKS):
        first_unit = blocknum * ff_width
        partial_value = jnp.dot(hidden[:, first_unit:first_unit + ff_width], down_weight[first_unit:first_unit + ff_width], preferred_element_type=jnp.float32)
        rounded = lax.optimization_barrier(partial_value.astype(jnp.bfloat16))
        down_sum = down_sum + rounded.astype(jnp.float32)
    out_rows = (residual_wide + down_sum).astype(jnp.bfloat16)
    owners = row_owner[:, 0].reshape(N_REQ, ROWS)
    onehot = (owners[:, :, None] == jnp.arange(N_REQ, dtype=jnp.int32)[None, None, :]).astype(jnp.int32)
    before = lax.optimization_barrier(jnp.sum((jnp.cumsum(onehot, axis=1) - 1) * onehot, axis=2))
    sources = jnp.arange(N_REQ, dtype=jnp.int32)[:, None]
    destination = (owners * OWNER_ROWS + sources * SLOT + before).reshape(ALL_ROWS).astype(jnp.int32)
    layer_out = jnp.zeros((OUT_ROWS, D), jnp.bfloat16).at[destination].set(out_rows)
    return layer_out
```

```python
import math

import jax
import jax.numpy as jnp
from jax import lax
from jax.sharding import PartitionSpec as P

HD = 96
CAP = 48


eps_norm = 1e-05


def head_split(matrix):
    return matrix.reshape(matrix.shape[0], matrix.shape[1] // HD, HD)


def softmax_rows(scores, allowed):
    masked = jnp.where(allowed, scores, -jnp.inf)
    highest = jnp.max(masked, axis=-1, keepdims=True)
    raised = jnp.exp(masked - highest)
    return (raised / jnp.sum(raised, axis=-1, keepdims=True)).astype(jnp.bfloat16)


def rank_within(onehot, axis):
    return jnp.sum((jnp.cumsum(onehot, axis=axis) - 1) * onehot, axis=-1)


def on_device(
    hidden_in,
    dec_query,
    dec_key,
    dec_value,
    pre_query,
    pre_key,
    pre_value,
    cache_key,
    cache_value,
    group_of,
    cache_length,
    stretch_start,
    row_owner,
    out_weight,
    norm_gain,
    gate_weight,
    up_weight,
    down_weight,
):
    factor = 1.0 / math.sqrt(HD)
    width_here = dec_query.shape[1]
    req_count = lax.axis_size("req")
    head_count = lax.axis_size("head")
    me = lax.axis_index("req")
    groups_here = cache_key.shape[0]
    length_cache = cache_key.shape[1]
    per_home = dec_query.shape[0]
    members = group_of[:, 0]
    total_reqs = members.shape[0]

    holder_of = members // groups_here
    holder_hot = (holder_of[:, None] == jnp.arange(req_count, dtype=jnp.int32)[None, :]).astype(jnp.int32)
    rank_all = rank_within(holder_hot.reshape(req_count, per_home, req_count), 1).reshape(total_reqs)
    slot_of = (jnp.arange(total_reqs, dtype=jnp.int32) // per_home) * per_home + rank_all

    my_holder = lax.dynamic_slice_in_dim(holder_of, me * per_home, per_home)
    my_rank = lax.dynamic_slice_in_dim(rank_all, me * per_home, per_home)
    my_slot = my_holder * per_home + my_rank
    packer = (
        my_slot[None, :] == jnp.arange(req_count * per_home, dtype=jnp.int32)[:, None]
    ).astype(jnp.bfloat16)
    stacked_in = jnp.concatenate([dec_query, dec_key, dec_value], axis=1)
    outgoing_q = jnp.dot(packer, stacked_in, preferred_element_type=jnp.float32).astype(jnp.bfloat16)
    arrived_q = lax.all_to_all(outgoing_q, "req", split_axis=0, concat_axis=0, tiled=True)

    first_group = me * groups_here
    wanted = first_group + jnp.arange(groups_here, dtype=jnp.int32)
    belongs = (members[None, :] == wanted[:, None]).astype(jnp.int32)
    ranking = jnp.cumsum(belongs, axis=1) - 1
    places = jnp.arange(CAP, dtype=jnp.int32)
    chosen = ((belongs[:, None, :] == 1) & (ranking[:, None, :] == places[None, :, None])).reshape(
        groups_here * CAP, total_reqs
    )
    chosen_slot = jnp.sum(jnp.where(chosen, slot_of[None, :], 0), axis=1)
    chosen_any = jnp.any(chosen, axis=1)
    chooser = chosen_any[:, None] & (
        chosen_slot[:, None] == jnp.arange(req_count * per_home, dtype=jnp.int32)[None, :]
    )
    picked = jnp.dot(
        chooser.astype(jnp.bfloat16), arrived_q, preferred_element_type=jnp.float32
    ).astype(jnp.bfloat16)
    positions = jnp.arange(length_cache)
    results = []
    for group_pos in range(groups_here):
        rows_block = picked[group_pos * CAP : (group_pos + 1) * CAP]
        picked_q = head_split(rows_block[:, :width_here])
        picked_k = head_split(rows_block[:, width_here : 2 * width_here])
        picked_v = head_split(rows_block[:, 2 * width_here :])
        cache_scores = (
            jnp.einsum(
                "qhd,khd->hqk",
                picked_q,
                head_split(cache_key[group_pos]),
                preferred_element_type=jnp.float32,
            )
            * factor
        )
        own_scores = (
            jnp.sum(picked_q.astype(jnp.float32) * picked_k.astype(jnp.float32), axis=-1).T * factor
        )
        scores = jnp.concatenate([cache_scores, own_scores[:, :, None]], axis=-1)
        allowed = jnp.concatenate([positions < cache_length[group_pos], jnp.ones((1,), bool)])[
            None, None, :
        ]
        weights = softmax_rows(scores, allowed)
        blended = jnp.einsum(
            "hqk,khd->qhd",
            weights[:, :, :length_cache],
            head_split(cache_value[group_pos]),
            preferred_element_type=jnp.float32,
        )
        blended = blended + weights[:, :, length_cache].astype(jnp.float32).T[
            :, :, None
        ] * picked_v.astype(jnp.float32)
        results.append(blended.reshape(CAP, width_here))
    stacked = jnp.concatenate(results, axis=0).astype(jnp.bfloat16)
    going_back = jnp.dot(
        chooser.astype(jnp.bfloat16).T, stacked, preferred_element_type=jnp.float32
    ).astype(jnp.bfloat16)
    came_back = lax.all_to_all(going_back, "req", split_axis=0, concat_axis=0, tiled=True)
    dec_out = jnp.dot(packer.T, came_back, preferred_element_type=jnp.float32).astype(jnp.bfloat16)

    stretch_len = pre_query.shape[0]
    key_rows = jnp.concatenate([cache_key[0], pre_key], axis=0)
    value_rows = jnp.concatenate([cache_value[0], pre_value], axis=0)
    columns = jnp.arange(length_cache + stretch_len)
    row_numbers = jnp.arange(stretch_len)
    allowed_pre = jnp.where(
        columns[None, :] < length_cache,
        columns[None, :] < stretch_start[0],
        columns[None, :] - length_cache <= row_numbers[:, None],
    )
    pre_scores = (
        jnp.einsum(
            "qhd,khd->hqk",
            head_split(pre_query),
            head_split(key_rows),
            preferred_element_type=jnp.float32,
        )
        * factor
    )
    pre_weights = softmax_rows(pre_scores, allowed_pre[None])
    pre_mixed = jnp.einsum(
        "hqk,khd->qhd", pre_weights, head_split(value_rows), preferred_element_type=jnp.float32
    )
    pre_out = pre_mixed.reshape(stretch_len, width_here).astype(jnp.bfloat16)
    attn_rows = jnp.concatenate([dec_out, pre_out], axis=0)
    projected = jnp.dot(attn_rows, out_weight, preferred_element_type=jnp.float32)
    head_me = lax.axis_index("head")
    col_start = head_me * width_here
    own_cols = lax.dynamic_slice_in_dim(projected, col_start, width_here, 1) + hidden_in.astype(
        jnp.float32
    )
    contribution = lax.dynamic_update_slice_in_dim(projected, own_cols, col_start, 1)
    residual = lax.psum(contribution.astype(jnp.bfloat16), "head")

    residual_wide = residual.astype(jnp.float32)
    squares = jnp.mean(jnp.square(residual_wide), axis=-1, keepdims=True)
    normed = (residual_wide * lax.rsqrt(squares + eps_norm) * norm_gain).astype(jnp.bfloat16)
    gate_act = jnp.dot(normed, gate_weight, preferred_element_type=jnp.float32)
    up_act = jnp.dot(normed, up_weight, preferred_element_type=jnp.float32)
    hidden = (jax.nn.silu(gate_act) * up_act).astype(jnp.bfloat16)
    down_part = jnp.dot(hidden, down_weight, preferred_element_type=jnp.float32).astype(jnp.bfloat16)
    down_cols = lax.psum_scatter(down_part, "head", scatter_dimension=1, tiled=True)
    own_residual = lax.dynamic_slice_in_dim(residual_wide, col_start, width_here, 1)
    out_cols = (own_residual + down_cols.astype(jnp.float32)).astype(jnp.bfloat16)

    row_count = residual.shape[0]
    slot_rows = 8 * ((2 * row_count + 8 * req_count - 1) // (8 * req_count))
    owners = row_owner[:, 0]
    onehot_owner = (owners[:, None] == jnp.arange(req_count, dtype=jnp.int32)[None, :]).astype(
        jnp.int32
    )
    before = rank_within(onehot_owner, 0)
    target = owners * slot_rows + before
    placing = (
        target[None, :] == jnp.arange(req_count * slot_rows, dtype=jnp.int32)[:, None]
    ).astype(jnp.bfloat16)
    outgoing = jnp.dot(placing, out_cols, preferred_element_type=jnp.float32).astype(jnp.bfloat16)
    arrived = lax.all_to_all(outgoing, "req", split_axis=0, concat_axis=0, tiled=True)
    return lax.all_to_all(arrived, "head", split_axis=0, concat_axis=1, tiled=True)


def solution(mesh):
    placed = (
        P("req", "head"),
        P("req", "head"),
        P("req", "head"),
        P("req", "head"),
        P("req", "head"),
        P("req", "head"),
        P("req", "head"),
        P("req", None, "head"),
        P("req", None, "head"),
        P(),
        P("req"),
        P("req"),
        P("req", None),
        P("head", None),
        P(),
        P(None, "head"),
        P(None, "head"),
        P("head", None),
    )
    return jax.shard_map(
        on_device, mesh=mesh, in_specs=placed, out_specs=P(("req", "head"), None), check_vma=False
    )
```

```python
import math

import jax
import jax.numpy as jnp
from jax import lax
from jax.sharding import PartitionSpec as P

HD = 96
CAP = 48


eps_norm = 1e-05


def head_split(matrix):
    return matrix.reshape(matrix.shape[0], matrix.shape[1] // HD, HD)


def softmax_rows(scores, allowed):
    masked = jnp.where(allowed, scores, -jnp.inf)
    highest = jnp.max(masked, axis=-1, keepdims=True)
    raised = jnp.exp(masked - highest)
    return (raised / jnp.sum(raised, axis=-1, keepdims=True)).astype(jnp.bfloat16)


def rank_within(onehot, axis):
    return jnp.sum((jnp.cumsum(onehot, axis=axis) - 1) * onehot, axis=-1)


def pair_then_z_scatter(x):
    rows, cols = x.shape
    n = lax.axis_size("head")
    ring = n // 2
    h = lax.axis_index("head")
    zc = h // 2
    core = h % 2
    blocks = x.reshape(rows, ring, 2, cols // n)
    mine = lax.dynamic_index_in_dim(blocks, core, 2, keepdims=False)
    other = lax.dynamic_index_in_dim(blocks, 1 - core, 2, keepdims=False)
    got = lax.ppermute(other, "head", [(i, i ^ 1) for i in range(n)])
    pair_sum = (mine.astype(jnp.float32) + got.astype(jnp.float32)).astype(jnp.bfloat16)
    acc = lax.dynamic_index_in_dim(pair_sum, zc, 1, keepdims=False).astype(jnp.float32)
    for d in range(1, ring):
        perm = [(i, ((i // 2 + d) % ring) * 2 + i % 2) for i in range(n)]
        piece = lax.dynamic_index_in_dim(pair_sum, (zc + d) % ring, 1, keepdims=False)
        acc = acc + lax.ppermute(piece, "head", perm).astype(jnp.float32)
    return acc


def z_then_pair_gather(y):
    rows, width = y.shape
    n = lax.axis_size("head")
    ring = n // 2
    h = lax.axis_index("head")
    zc = h // 2
    core = h % 2
    parts = [y]
    for d in range(1, ring):
        perm = [(i, ((i // 2 + d) % ring) * 2 + i % 2) for i in range(n)]
        parts.append(lax.ppermute(y, "head", perm))
    stacked = jnp.stack(parts, 0)
    in_order = jnp.stack(
        [lax.dynamic_index_in_dim(stacked, (zc - zz) % ring, 0, keepdims=False) for zz in range(ring)], 1
    )
    got = lax.ppermute(in_order, "head", [(i, i ^ 1) for i in range(n)])
    first = jnp.where(core == 0, in_order, got)
    second = jnp.where(core == 0, got, in_order)
    return jnp.stack([first, second], 2).reshape(rows, ring * 2 * width)


def on_device(
    hidden_in,
    dec_query,
    dec_key,
    dec_value,
    pre_query,
    pre_key,
    pre_value,
    cache_key,
    cache_value,
    group_of,
    cache_length,
    stretch_start,
    row_owner,
    out_weight,
    norm_gain,
    gate_weight,
    up_weight,
    down_weight,
):
    factor = 1.0 / math.sqrt(HD)
    width_here = dec_query.shape[1]
    req_count = lax.axis_size("req")
    head_count = lax.axis_size("head")
    me = lax.axis_index("req")
    groups_here = cache_key.shape[0]
    length_cache = cache_key.shape[1]
    per_home = dec_query.shape[0]
    members = group_of[:, 0]
    total_reqs = members.shape[0]

    holder_of = members // groups_here
    holder_hot = (holder_of[:, None] == jnp.arange(req_count, dtype=jnp.int32)[None, :]).astype(jnp.int32)
    rank_all = rank_within(holder_hot.reshape(req_count, per_home, req_count), 1).reshape(total_reqs)
    slot_of = (jnp.arange(total_reqs, dtype=jnp.int32) // per_home) * per_home + rank_all

    my_holder = lax.dynamic_slice_in_dim(holder_of, me * per_home, per_home)
    my_rank = lax.dynamic_slice_in_dim(rank_all, me * per_home, per_home)
    my_slot = my_holder * per_home + my_rank
    packer = (
        my_slot[None, :] == jnp.arange(req_count * per_home, dtype=jnp.int32)[:, None]
    ).astype(jnp.bfloat16)
    stacked_in = jnp.concatenate([dec_query, dec_key, dec_value], axis=1)
    outgoing_q = jnp.dot(packer, stacked_in, preferred_element_type=jnp.float32).astype(jnp.bfloat16)
    arrived_q = lax.all_to_all(outgoing_q, "req", split_axis=0, concat_axis=0, tiled=True)

    first_group = me * groups_here
    wanted = first_group + jnp.arange(groups_here, dtype=jnp.int32)
    belongs = (members[None, :] == wanted[:, None]).astype(jnp.int32)
    ranking = jnp.cumsum(belongs, axis=1) - 1
    places = jnp.arange(CAP, dtype=jnp.int32)
    chosen = ((belongs[:, None, :] == 1) & (ranking[:, None, :] == places[None, :, None])).reshape(
        groups_here * CAP, total_reqs
    )
    chosen_slot = jnp.sum(jnp.where(chosen, slot_of[None, :], 0), axis=1)
    chosen_any = jnp.any(chosen, axis=1)
    chooser = chosen_any[:, None] & (
        chosen_slot[:, None] == jnp.arange(req_count * per_home, dtype=jnp.int32)[None, :]
    )
    picked = jnp.dot(
        chooser.astype(jnp.bfloat16), arrived_q, preferred_element_type=jnp.float32
    ).astype(jnp.bfloat16)
    positions = jnp.arange(length_cache)
    results = []
    for group_pos in range(groups_here):
        rows_block = picked[group_pos * CAP : (group_pos + 1) * CAP]
        picked_q = head_split(rows_block[:, :width_here])
        picked_k = head_split(rows_block[:, width_here : 2 * width_here])
        picked_v = head_split(rows_block[:, 2 * width_here :])
        cache_scores = (
            jnp.einsum(
                "qhd,khd->hqk",
                picked_q,
                head_split(cache_key[group_pos]),
                preferred_element_type=jnp.float32,
            )
            * factor
        )
        own_scores = (
            jnp.sum(picked_q.astype(jnp.float32) * picked_k.astype(jnp.float32), axis=-1).T * factor
        )
        scores = jnp.concatenate([cache_scores, own_scores[:, :, None]], axis=-1)
        allowed = jnp.concatenate([positions < cache_length[group_pos], jnp.ones((1,), bool)])[
            None, None, :
        ]
        weights = softmax_rows(scores, allowed)
        blended = jnp.einsum(
            "hqk,khd->qhd",
            weights[:, :, :length_cache],
            head_split(cache_value[group_pos]),
            preferred_element_type=jnp.float32,
        )
        blended = blended + weights[:, :, length_cache].astype(jnp.float32).T[
            :, :, None
        ] * picked_v.astype(jnp.float32)
        results.append(blended.reshape(CAP, width_here))
    stacked = jnp.concatenate(results, axis=0).astype(jnp.bfloat16)
    going_back = jnp.dot(
        chooser.astype(jnp.bfloat16).T, stacked, preferred_element_type=jnp.float32
    ).astype(jnp.bfloat16)
    came_back = lax.all_to_all(going_back, "req", split_axis=0, concat_axis=0, tiled=True)
    dec_out = jnp.dot(packer.T, came_back, preferred_element_type=jnp.float32).astype(jnp.bfloat16)

    stretch_len = pre_query.shape[0]
    key_rows = jnp.concatenate([cache_key[0], pre_key], axis=0)
    value_rows = jnp.concatenate([cache_value[0], pre_value], axis=0)
    columns = jnp.arange(length_cache + stretch_len)
    row_numbers = jnp.arange(stretch_len)
    allowed_pre = jnp.where(
        columns[None, :] < length_cache,
        columns[None, :] < stretch_start[0],
        columns[None, :] - length_cache <= row_numbers[:, None],
    )
    pre_scores = (
        jnp.einsum(
            "qhd,khd->hqk",
            head_split(pre_query),
            head_split(key_rows),
            preferred_element_type=jnp.float32,
        )
        * factor
    )
    pre_weights = softmax_rows(pre_scores, allowed_pre[None])
    pre_mixed = jnp.einsum(
        "hqk,khd->qhd", pre_weights, head_split(value_rows), preferred_element_type=jnp.float32
    )
    pre_out = pre_mixed.reshape(stretch_len, width_here).astype(jnp.bfloat16)
    attn_rows = jnp.concatenate([dec_out, pre_out], axis=0)
    projected = jnp.dot(attn_rows, out_weight, preferred_element_type=jnp.float32)
    head_me = lax.axis_index("head")
    col_start = head_me * width_here
    own_cols = lax.dynamic_slice_in_dim(projected, col_start, width_here, 1) + hidden_in.astype(
        jnp.float32
    )
    contribution = lax.dynamic_update_slice_in_dim(projected, own_cols, col_start, 1)
    own_residual = pair_then_z_scatter(contribution.astype(jnp.bfloat16))
    residual = z_then_pair_gather(own_residual.astype(jnp.bfloat16))

    residual_wide = residual.astype(jnp.float32)
    squares = jnp.mean(jnp.square(residual_wide), axis=-1, keepdims=True)
    normed = (residual_wide * lax.rsqrt(squares + eps_norm) * norm_gain).astype(jnp.bfloat16)
    gate_act = jnp.dot(normed, gate_weight, preferred_element_type=jnp.float32)
    up_act = jnp.dot(normed, up_weight, preferred_element_type=jnp.float32)
    hidden = (jax.nn.silu(gate_act) * up_act).astype(jnp.bfloat16)
    down_part = jnp.dot(hidden, down_weight, preferred_element_type=jnp.float32).astype(jnp.bfloat16)
    down_cols = pair_then_z_scatter(down_part)
    own_wide = own_residual.astype(jnp.bfloat16).astype(jnp.float32)
    out_cols = (own_wide + down_cols).astype(jnp.bfloat16)

    row_count = residual.shape[0]
    slot_rows = 8 * ((2 * row_count + 8 * req_count - 1) // (8 * req_count))
    owners = row_owner[:, 0]
    onehot_owner = (owners[:, None] == jnp.arange(req_count, dtype=jnp.int32)[None, :]).astype(
        jnp.int32
    )
    before = rank_within(onehot_owner, 0)
    target = owners * slot_rows + before
    placing = (
        target[None, :] == jnp.arange(req_count * slot_rows, dtype=jnp.int32)[:, None]
    ).astype(jnp.bfloat16)
    outgoing = jnp.dot(placing, out_cols, preferred_element_type=jnp.float32).astype(jnp.bfloat16)
    arrived = lax.all_to_all(outgoing, "req", split_axis=0, concat_axis=0, tiled=True)
    return lax.all_to_all(arrived, "head", split_axis=0, concat_axis=1, tiled=True)


def solution(mesh):
    placed = (
        P("req", "head"),
        P("req", "head"),
        P("req", "head"),
        P("req", "head"),
        P("req", "head"),
        P("req", "head"),
        P("req", "head"),
        P("req", None, "head"),
        P("req", None, "head"),
        P(),
        P("req"),
        P("req"),
        P("req", None),
        P("head", None),
        P(),
        P(None, "head"),
        P(None, "head"),
        P("head", None),
    )
    return jax.shard_map(
        on_device, mesh=mesh, in_specs=placed, out_specs=P(("req", "head"), None), check_vma=False
    )
```

```python
import math

import jax
import jax.numpy as jnp
from jax import lax
from jax.sharding import PartitionSpec as P

HD = 96
CAP = 48


eps_norm = 1e-05


def head_split(matrix):
    return matrix.reshape(matrix.shape[0], matrix.shape[1] // HD, HD)


def softmax_rows(scores, allowed):
    masked = jnp.where(allowed, scores, -jnp.inf)
    highest = jnp.max(masked, axis=-1, keepdims=True)
    raised = jnp.exp(masked - highest)
    return (raised / jnp.sum(raised, axis=-1, keepdims=True)).astype(jnp.bfloat16)


def rank_within(onehot, axis):
    return jnp.sum((jnp.cumsum(onehot, axis=axis) - 1) * onehot, axis=-1)


def pair_then_z_scatter(x):
    rows, cols = x.shape
    n = lax.axis_size("head")
    ring = n // 2
    width = cols // n
    h = lax.axis_index("head")
    zc = h // 2
    on_first = h % 2 == 0
    even = jnp.concatenate([x[:, (2 * z) * width : (2 * z + 1) * width] for z in range(ring)], 1)
    odd = jnp.concatenate([x[:, (2 * z + 1) * width : (2 * z + 2) * width] for z in range(ring)], 1)
    mine = jnp.where(on_first, even, odd)
    other = jnp.where(on_first, odd, even)
    got = lax.ppermute(other, "head", [(i, i ^ 1) for i in range(n)])
    pair_sum = (mine.astype(jnp.float32) + got.astype(jnp.float32)).astype(jnp.bfloat16)
    acc = lax.dynamic_slice_in_dim(pair_sum, zc * width, width, 1).astype(jnp.float32)
    for d in range(1, ring):
        perm = [(i, ((i // 2 + d) % ring) * 2 + i % 2) for i in range(n)]
        piece = lax.dynamic_slice_in_dim(pair_sum, ((zc + d) % ring) * width, width, 1)
        acc = acc + lax.ppermute(piece, "head", perm).astype(jnp.float32)
    return acc


def z_then_pair_gather(y):
    rows, width = y.shape
    n = lax.axis_size("head")
    ring = n // 2
    h = lax.axis_index("head")
    zc = h // 2
    on_first = h % 2 == 0
    parts = [y]
    for d in range(1, ring):
        perm = [(i, ((i // 2 + d) % ring) * 2 + i % 2) for i in range(n)]
        parts.append(lax.ppermute(y, "head", perm))
    stacked = jnp.stack(parts, 0)
    in_order = jnp.concatenate(
        [lax.dynamic_index_in_dim(stacked, (zc - zz) % ring, 0, keepdims=False) for zz in range(ring)], 1
    )
    got = lax.ppermute(in_order, "head", [(i, i ^ 1) for i in range(n)])
    pieces = []
    for z in range(ring):
        mine_z = in_order[:, z * width : (z + 1) * width]
        got_z = got[:, z * width : (z + 1) * width]
        pieces.append(jnp.where(on_first, mine_z, got_z))
        pieces.append(jnp.where(on_first, got_z, mine_z))
    return jnp.concatenate(pieces, 1)


def on_device(
    hidden_in,
    dec_query,
    dec_key,
    dec_value,
    pre_query,
    pre_key,
    pre_value,
    cache_key,
    cache_value,
    group_of,
    cache_length,
    stretch_start,
    row_owner,
    out_weight,
    norm_gain,
    gate_weight,
    up_weight,
    down_weight,
):
    factor = 1.0 / math.sqrt(HD)
    width_here = dec_query.shape[1]
    req_count = lax.axis_size("req")
    head_count = lax.axis_size("head")
    me = lax.axis_index("req")
    groups_here = cache_key.shape[0]
    length_cache = cache_key.shape[1]
    per_home = dec_query.shape[0]
    members = group_of[:, 0]
    total_reqs = members.shape[0]

    holder_of = members // groups_here
    holder_hot = (holder_of[:, None] == jnp.arange(req_count, dtype=jnp.int32)[None, :]).astype(jnp.int32)
    rank_all = rank_within(holder_hot.reshape(req_count, per_home, req_count), 1).reshape(total_reqs)
    slot_of = (jnp.arange(total_reqs, dtype=jnp.int32) // per_home) * per_home + rank_all

    my_holder = lax.dynamic_slice_in_dim(holder_of, me * per_home, per_home)
    my_rank = lax.dynamic_slice_in_dim(rank_all, me * per_home, per_home)
    my_slot = my_holder * per_home + my_rank
    packer = (
        my_slot[None, :] == jnp.arange(req_count * per_home, dtype=jnp.int32)[:, None]
    ).astype(jnp.bfloat16)
    stacked_in = jnp.concatenate([dec_query, dec_key, dec_value], axis=1)
    outgoing_q = jnp.dot(packer, stacked_in, preferred_element_type=jnp.float32).astype(jnp.bfloat16)
    arrived_q = lax.all_to_all(outgoing_q, "req", split_axis=0, concat_axis=0, tiled=True)

    first_group = me * groups_here
    wanted = first_group + jnp.arange(groups_here, dtype=jnp.int32)
    belongs = (members[None, :] == wanted[:, None]).astype(jnp.int32)
    ranking = jnp.cumsum(belongs, axis=1) - 1
    places = jnp.arange(CAP, dtype=jnp.int32)
    chosen = ((belongs[:, None, :] == 1) & (ranking[:, None, :] == places[None, :, None])).reshape(
        groups_here * CAP, total_reqs
    )
    chosen_slot = jnp.sum(jnp.where(chosen, slot_of[None, :], 0), axis=1)
    chosen_any = jnp.any(chosen, axis=1)
    chooser = chosen_any[:, None] & (
        chosen_slot[:, None] == jnp.arange(req_count * per_home, dtype=jnp.int32)[None, :]
    )
    picked = jnp.dot(
        chooser.astype(jnp.bfloat16), arrived_q, preferred_element_type=jnp.float32
    ).astype(jnp.bfloat16)
    positions = jnp.arange(length_cache)
    results = []
    for group_pos in range(groups_here):
        rows_block = picked[group_pos * CAP : (group_pos + 1) * CAP]
        picked_q = head_split(rows_block[:, :width_here])
        picked_k = head_split(rows_block[:, width_here : 2 * width_here])
        picked_v = head_split(rows_block[:, 2 * width_here :])
        cache_scores = (
            jnp.einsum(
                "qhd,khd->hqk",
                picked_q,
                head_split(cache_key[group_pos]),
                preferred_element_type=jnp.float32,
            )
            * factor
        )
        own_scores = (
            jnp.sum(picked_q.astype(jnp.float32) * picked_k.astype(jnp.float32), axis=-1).T * factor
        )
        scores = jnp.concatenate([cache_scores, own_scores[:, :, None]], axis=-1)
        allowed = jnp.concatenate([positions < cache_length[group_pos], jnp.ones((1,), bool)])[
            None, None, :
        ]
        weights = softmax_rows(scores, allowed)
        blended = jnp.einsum(
            "hqk,khd->qhd",
            weights[:, :, :length_cache],
            head_split(cache_value[group_pos]),
            preferred_element_type=jnp.float32,
        )
        blended = blended + weights[:, :, length_cache].astype(jnp.float32).T[
            :, :, None
        ] * picked_v.astype(jnp.float32)
        results.append(blended.reshape(CAP, width_here))
    stacked = jnp.concatenate(results, axis=0).astype(jnp.bfloat16)
    going_back = jnp.dot(
        chooser.astype(jnp.bfloat16).T, stacked, preferred_element_type=jnp.float32
    ).astype(jnp.bfloat16)
    came_back = lax.all_to_all(going_back, "req", split_axis=0, concat_axis=0, tiled=True)
    dec_out = jnp.dot(packer.T, came_back, preferred_element_type=jnp.float32).astype(jnp.bfloat16)

    stretch_len = pre_query.shape[0]
    key_rows = jnp.concatenate([cache_key[0], pre_key], axis=0)
    value_rows = jnp.concatenate([cache_value[0], pre_value], axis=0)
    columns = jnp.arange(length_cache + stretch_len)
    row_numbers = jnp.arange(stretch_len)
    allowed_pre = jnp.where(
        columns[None, :] < length_cache,
        columns[None, :] < stretch_start[0],
        columns[None, :] - length_cache <= row_numbers[:, None],
    )
    pre_scores = (
        jnp.einsum(
            "qhd,khd->hqk",
            head_split(pre_query),
            head_split(key_rows),
            preferred_element_type=jnp.float32,
        )
        * factor
    )
    pre_weights = softmax_rows(pre_scores, allowed_pre[None])
    pre_mixed = jnp.einsum(
        "hqk,khd->qhd", pre_weights, head_split(value_rows), preferred_element_type=jnp.float32
    )
    pre_out = pre_mixed.reshape(stretch_len, width_here).astype(jnp.bfloat16)
    attn_rows = jnp.concatenate([dec_out, pre_out], axis=0)
    projected = jnp.dot(attn_rows, out_weight, preferred_element_type=jnp.float32)
    head_me = lax.axis_index("head")
    col_start = head_me * width_here
    own_cols = lax.dynamic_slice_in_dim(projected, col_start, width_here, 1) + hidden_in.astype(
        jnp.float32
    )
    contribution = lax.dynamic_update_slice_in_dim(projected, own_cols, col_start, 1)
    own_residual = pair_then_z_scatter(contribution.astype(jnp.bfloat16))
    residual = z_then_pair_gather(own_residual.astype(jnp.bfloat16))

    residual_wide = residual.astype(jnp.float32)
    squares = jnp.mean(jnp.square(residual_wide), axis=-1, keepdims=True)
    normed = (residual_wide * lax.rsqrt(squares + eps_norm) * norm_gain).astype(jnp.bfloat16)
    gate_act = jnp.dot(normed, gate_weight, preferred_element_type=jnp.float32)
    up_act = jnp.dot(normed, up_weight, preferred_element_type=jnp.float32)
    hidden = (jax.nn.silu(gate_act) * up_act).astype(jnp.bfloat16)
    down_part = jnp.dot(hidden, down_weight, preferred_element_type=jnp.float32).astype(jnp.bfloat16)
    down_cols = pair_then_z_scatter(down_part)
    own_wide = own_residual.astype(jnp.bfloat16).astype(jnp.float32)
    out_cols = (own_wide + down_cols).astype(jnp.bfloat16)

    row_count = residual.shape[0]
    slot_rows = 8 * ((2 * row_count + 8 * req_count - 1) // (8 * req_count))
    owners = row_owner[:, 0]
    onehot_owner = (owners[:, None] == jnp.arange(req_count, dtype=jnp.int32)[None, :]).astype(
        jnp.int32
    )
    before = rank_within(onehot_owner, 0)
    target = owners * slot_rows + before
    placing = (
        target[None, :] == jnp.arange(req_count * slot_rows, dtype=jnp.int32)[:, None]
    ).astype(jnp.bfloat16)
    outgoing = jnp.dot(placing, out_cols, preferred_element_type=jnp.float32).astype(jnp.bfloat16)
    arrived = lax.all_to_all(outgoing, "req", split_axis=0, concat_axis=0, tiled=True)
    return lax.all_to_all(arrived, "head", split_axis=0, concat_axis=1, tiled=True)


def solution(mesh):
    placed = (
        P("req", "head"),
        P("req", "head"),
        P("req", "head"),
        P("req", "head"),
        P("req", "head"),
        P("req", "head"),
        P("req", "head"),
        P("req", None, "head"),
        P("req", None, "head"),
        P(),
        P("req"),
        P("req"),
        P("req", None),
        P("head", None),
        P(),
        P(None, "head"),
        P(None, "head"),
        P("head", None),
    )
    return jax.shard_map(
        on_device, mesh=mesh, in_specs=placed, out_specs=P(("req", "head"), None), check_vma=False
    )
```

```python
import math

import jax
import jax.numpy as jnp
from jax import lax
from jax.sharding import PartitionSpec as P

HD = 96
CAP = 48


eps_norm = 1e-05


def rank_within(onehot, axis):
    return jnp.sum((jnp.cumsum(onehot, axis=axis) - 1) * onehot, axis=-1)


def pair_then_z_scatter(x):
    rows, cols = x.shape
    n = lax.axis_size("head")
    ring = n // 2
    width = cols // n
    h = lax.axis_index("head")
    zc = h // 2
    on_first = h % 2 == 0
    even = jnp.concatenate([x[:, (2 * z) * width : (2 * z + 1) * width] for z in range(ring)], 1)
    odd = jnp.concatenate([x[:, (2 * z + 1) * width : (2 * z + 2) * width] for z in range(ring)], 1)
    mine = jnp.where(on_first, even, odd)
    other = jnp.where(on_first, odd, even)
    got = lax.ppermute(other, "head", [(i, i ^ 1) for i in range(n)])
    pair_sum = (mine.astype(jnp.float32) + got.astype(jnp.float32)).astype(jnp.bfloat16)
    acc = lax.dynamic_slice_in_dim(pair_sum, zc * width, width, 1).astype(jnp.float32)
    for d in range(1, ring):
        perm = [(i, ((i // 2 + d) % ring) * 2 + i % 2) for i in range(n)]
        piece = lax.dynamic_slice_in_dim(pair_sum, ((zc + d) % ring) * width, width, 1)
        acc = acc + lax.ppermute(piece, "head", perm).astype(jnp.float32)
    return acc


def z_then_pair_gather(y):
    rows, width = y.shape
    n = lax.axis_size("head")
    ring = n // 2
    h = lax.axis_index("head")
    zc = h // 2
    on_first = h % 2 == 0
    parts = [y]
    for d in range(1, ring):
        perm = [(i, ((i // 2 + d) % ring) * 2 + i % 2) for i in range(n)]
        parts.append(lax.ppermute(y, "head", perm))
    stacked = jnp.stack(parts, 0)
    in_order = jnp.concatenate(
        [lax.dynamic_index_in_dim(stacked, (zc - zz) % ring, 0, keepdims=False) for zz in range(ring)], 1
    )
    got = lax.ppermute(in_order, "head", [(i, i ^ 1) for i in range(n)])
    pieces = []
    for z in range(ring):
        mine_z = in_order[:, z * width : (z + 1) * width]
        got_z = got[:, z * width : (z + 1) * width]
        pieces.append(jnp.where(on_first, mine_z, got_z))
        pieces.append(jnp.where(on_first, got_z, mine_z))
    return jnp.concatenate(pieces, 1)


def on_device(
    hidden_in,
    dec_query,
    dec_key,
    dec_value,
    pre_query,
    pre_key,
    pre_value,
    cache_key,
    cache_value,
    group_of,
    cache_length,
    stretch_start,
    row_owner,
    out_weight,
    norm_gain,
    gate_weight,
    up_weight,
    down_weight,
):
    factor = 1.0 / math.sqrt(HD)
    width_here = dec_query.shape[1]
    req_count = lax.axis_size("req")
    head_count = lax.axis_size("head")
    me = lax.axis_index("req")
    groups_here = cache_key.shape[0]
    length_cache = cache_key.shape[1]
    per_home = dec_query.shape[0]
    members = group_of[:, 0]
    total_reqs = members.shape[0]

    holder_of = members // groups_here
    holder_hot = (holder_of[:, None] == jnp.arange(req_count, dtype=jnp.int32)[None, :]).astype(jnp.int32)
    rank_all = rank_within(holder_hot.reshape(req_count, per_home, req_count), 1).reshape(total_reqs)
    slot_of = (jnp.arange(total_reqs, dtype=jnp.int32) // per_home) * per_home + rank_all

    my_holder = lax.dynamic_slice_in_dim(holder_of, me * per_home, per_home)
    my_rank = lax.dynamic_slice_in_dim(rank_all, me * per_home, per_home)
    my_slot = my_holder * per_home + my_rank
    packer = (
        my_slot[None, :] == jnp.arange(req_count * per_home, dtype=jnp.int32)[:, None]
    ).astype(jnp.bfloat16)
    stacked_in = jnp.concatenate([dec_query, dec_key, dec_value], axis=1)
    outgoing_q = jnp.dot(packer, stacked_in, preferred_element_type=jnp.float32).astype(jnp.bfloat16)
    arrived_q = lax.all_to_all(outgoing_q, "req", split_axis=0, concat_axis=0, tiled=True)

    first_group = me * groups_here
    wanted = first_group + jnp.arange(groups_here, dtype=jnp.int32)
    belongs = (members[None, :] == wanted[:, None]).astype(jnp.int32)
    ranking = jnp.cumsum(belongs, axis=1) - 1
    places = jnp.arange(CAP, dtype=jnp.int32)
    chosen = ((belongs[:, None, :] == 1) & (ranking[:, None, :] == places[None, :, None])).reshape(
        groups_here * CAP, total_reqs
    )
    chosen_slot = jnp.sum(jnp.where(chosen, slot_of[None, :], 0), axis=1)
    chosen_any = jnp.any(chosen, axis=1)
    chooser = chosen_any[:, None] & (
        chosen_slot[:, None] == jnp.arange(req_count * per_home, dtype=jnp.int32)[None, :]
    )
    picked = jnp.dot(
        chooser.astype(jnp.bfloat16), arrived_q, preferred_element_type=jnp.float32
    ).astype(jnp.bfloat16)
    heads_here = width_here // HD
    head_mask = (jnp.arange(width_here) // HD)[None, :] == jnp.arange(heads_here)[:, None]
    positions = jnp.arange(length_cache)
    results = []
    for group_pos in range(groups_here):
        rows_block = picked[group_pos * CAP : (group_pos + 1) * CAP]
        q_rows = rows_block[:, :width_here]
        k_own = rows_block[:, width_here : 2 * width_here]
        v_own = rows_block[:, 2 * width_here :]
        q_stack = jnp.where(head_mask[:, None, :], q_rows[None], 0).reshape(heads_here * CAP, width_here)
        cache_scores = lax.dot_general(
            q_stack, cache_key[group_pos], (((1,), (1,)), ((), ())), preferred_element_type=jnp.float32
        ) * factor
        own_prod = q_rows.astype(jnp.float32) * k_own.astype(jnp.float32)
        own_scores = (
            jnp.sum(jnp.where(head_mask[:, None, :], own_prod[None], 0.0), axis=-1).reshape(heads_here * CAP, 1)
            * factor
        )
        valid = (positions < cache_length[group_pos])[None, :]
        cache_scores = jnp.where(valid, cache_scores, -jnp.inf)
        highest = jnp.maximum(jnp.max(cache_scores, axis=-1, keepdims=True), own_scores)
        raised = jnp.exp(cache_scores - highest)
        raised_own = jnp.exp(own_scores - highest)
        total = jnp.sum(raised, axis=-1, keepdims=True) + raised_own
        weights = (raised / total).astype(jnp.bfloat16)
        weight_own = (raised_own / total).astype(jnp.bfloat16).astype(jnp.float32)
        mixed = jnp.dot(weights, cache_value[group_pos], preferred_element_type=jnp.float32)
        mixed = mixed + weight_own * v_own.astype(jnp.float32)[None].repeat(heads_here, 0).reshape(
            heads_here * CAP, width_here
        )
        blended = jnp.sum(
            jnp.where(head_mask[:, None, :], mixed.reshape(heads_here, CAP, width_here), 0.0), axis=0
        )
        results.append(blended)
    stacked = jnp.concatenate(results, axis=0).astype(jnp.bfloat16)
    going_back = jnp.dot(
        chooser.astype(jnp.bfloat16).T, stacked, preferred_element_type=jnp.float32
    ).astype(jnp.bfloat16)
    came_back = lax.all_to_all(going_back, "req", split_axis=0, concat_axis=0, tiled=True)
    dec_out = jnp.dot(packer.T, came_back, preferred_element_type=jnp.float32).astype(jnp.bfloat16)

    stretch_len = pre_query.shape[0]
    row_numbers = jnp.arange(stretch_len)
    pre_stack = jnp.where(head_mask[:, None, :], pre_query[None], 0).reshape(heads_here * stretch_len, width_here)
    dims = (((1,), (1,)), ((), ()))
    cache_part = lax.dot_general(pre_stack, cache_key[0], dims, preferred_element_type=jnp.float32) * factor
    self_part = lax.dot_general(pre_stack, pre_key, dims, preferred_element_type=jnp.float32) * factor
    cache_part = jnp.where((positions < stretch_start[0])[None, :], cache_part, -jnp.inf)
    causal = (row_numbers[None, :] <= row_numbers[:, None])[None]
    self_part = jnp.where(causal, self_part.reshape(heads_here, stretch_len, stretch_len), -jnp.inf).reshape(
        heads_here * stretch_len, stretch_len
    )
    highest = jnp.maximum(
        jnp.max(cache_part, axis=-1, keepdims=True), jnp.max(self_part, axis=-1, keepdims=True)
    )
    raised_cache = jnp.exp(cache_part - highest)
    raised_self = jnp.exp(self_part - highest)
    total = jnp.sum(raised_cache, axis=-1, keepdims=True) + jnp.sum(raised_self, axis=-1, keepdims=True)
    pre_mixed = jnp.dot(
        (raised_cache / total).astype(jnp.bfloat16), cache_value[0], preferred_element_type=jnp.float32
    ) + jnp.dot((raised_self / total).astype(jnp.bfloat16), pre_value, preferred_element_type=jnp.float32)
    pre_out = jnp.sum(
        jnp.where(head_mask[:, None, :], pre_mixed.reshape(heads_here, stretch_len, width_here), 0.0), axis=0
    ).astype(jnp.bfloat16)
    attn_rows = jnp.concatenate([dec_out, pre_out], axis=0)
    projected = jnp.dot(attn_rows, out_weight, preferred_element_type=jnp.float32)
    head_me = lax.axis_index("head")
    col_start = head_me * width_here
    own_cols = lax.dynamic_slice_in_dim(projected, col_start, width_here, 1) + hidden_in.astype(
        jnp.float32
    )
    contribution = lax.dynamic_update_slice_in_dim(projected, own_cols, col_start, 1)
    own_residual = pair_then_z_scatter(contribution.astype(jnp.bfloat16))
    residual = z_then_pair_gather(own_residual.astype(jnp.bfloat16))

    residual_wide = residual.astype(jnp.float32)
    squares = jnp.mean(jnp.square(residual_wide), axis=-1, keepdims=True)
    normed = (residual_wide * lax.rsqrt(squares + eps_norm) * norm_gain).astype(jnp.bfloat16)
    gate_act = jnp.dot(normed, gate_weight, preferred_element_type=jnp.float32)
    up_act = jnp.dot(normed, up_weight, preferred_element_type=jnp.float32)
    hidden = (jax.nn.silu(gate_act) * up_act).astype(jnp.bfloat16)
    down_part = jnp.dot(hidden, down_weight, preferred_element_type=jnp.float32).astype(jnp.bfloat16)
    down_cols = pair_then_z_scatter(down_part)
    own_wide = own_residual.astype(jnp.bfloat16).astype(jnp.float32)
    out_cols = (own_wide + down_cols).astype(jnp.bfloat16)

    row_count = residual.shape[0]
    slot_rows = 8 * ((2 * row_count + 8 * req_count - 1) // (8 * req_count))
    owners = row_owner[:, 0]
    onehot_owner = (owners[:, None] == jnp.arange(req_count, dtype=jnp.int32)[None, :]).astype(
        jnp.int32
    )
    before = rank_within(onehot_owner, 0)
    target = owners * slot_rows + before
    placing = (
        target[None, :] == jnp.arange(req_count * slot_rows, dtype=jnp.int32)[:, None]
    ).astype(jnp.bfloat16)
    outgoing = jnp.dot(placing, out_cols, preferred_element_type=jnp.float32).astype(jnp.bfloat16)
    arrived = lax.all_to_all(outgoing, "req", split_axis=0, concat_axis=0, tiled=True)
    return lax.all_to_all(arrived, "head", split_axis=0, concat_axis=1, tiled=True)


def solution(mesh):
    placed = (
        P("req", "head"),
        P("req", "head"),
        P("req", "head"),
        P("req", "head"),
        P("req", "head"),
        P("req", "head"),
        P("req", "head"),
        P("req", None, "head"),
        P("req", None, "head"),
        P(),
        P("req"),
        P("req"),
        P("req", None),
        P("head", None),
        P(),
        P(None, "head"),
        P(None, "head"),
        P("head", None),
    )
    return jax.shard_map(
        on_device, mesh=mesh, in_specs=placed, out_specs=P(("req", "head"), None), check_vma=False
    )
```

```python
import math

import jax
import jax.numpy as jnp
from jax import lax
from jax.sharding import PartitionSpec as P

HD = 96
CAP = 48


eps_norm = 1e-05


def rank_within(onehot, axis):
    return jnp.sum((jnp.cumsum(onehot, axis=axis) - 1) * onehot, axis=-1)


def pair_then_z_scatter(x):
    rows, cols = x.shape
    n = lax.axis_size("head")
    ring = n // 2
    width = cols // n
    h = lax.axis_index("head")
    zc = h // 2
    on_first = h % 2 == 0
    even = jnp.concatenate([x[:, (2 * z) * width : (2 * z + 1) * width] for z in range(ring)], 1)
    odd = jnp.concatenate([x[:, (2 * z + 1) * width : (2 * z + 2) * width] for z in range(ring)], 1)
    mine = jnp.where(on_first, even, odd)
    other = jnp.where(on_first, odd, even)
    got = lax.ppermute(other, "head", [(i, i ^ 1) for i in range(n)])
    pair_sum = (mine.astype(jnp.float32) + got.astype(jnp.float32)).astype(jnp.bfloat16)
    acc = lax.dynamic_slice_in_dim(pair_sum, zc * width, width, 1).astype(jnp.float32)
    for d in range(1, ring):
        perm = [(i, ((i // 2 + d) % ring) * 2 + i % 2) for i in range(n)]
        piece = lax.dynamic_slice_in_dim(pair_sum, ((zc + d) % ring) * width, width, 1)
        acc = acc + lax.ppermute(piece, "head", perm).astype(jnp.float32)
    return acc


def z_then_pair_gather(y):
    rows, width = y.shape
    n = lax.axis_size("head")
    ring = n // 2
    h = lax.axis_index("head")
    zc = h // 2
    on_first = h % 2 == 0
    parts = [y]
    for d in range(1, ring):
        perm = [(i, ((i // 2 + d) % ring) * 2 + i % 2) for i in range(n)]
        parts.append(lax.ppermute(y, "head", perm))
    stacked = jnp.stack(parts, 0)
    in_order = jnp.concatenate(
        [lax.dynamic_index_in_dim(stacked, (zc - zz) % ring, 0, keepdims=False) for zz in range(ring)], 1
    )
    got = lax.ppermute(in_order, "head", [(i, i ^ 1) for i in range(n)])
    pieces = []
    for z in range(ring):
        mine_z = in_order[:, z * width : (z + 1) * width]
        got_z = got[:, z * width : (z + 1) * width]
        pieces.append(jnp.where(on_first, mine_z, got_z))
        pieces.append(jnp.where(on_first, got_z, mine_z))
    return jnp.concatenate(pieces, 1)


def on_device(
    hidden_in,
    dec_query,
    dec_key,
    dec_value,
    pre_query,
    pre_key,
    pre_value,
    cache_key,
    cache_value,
    group_of,
    cache_length,
    stretch_start,
    row_owner,
    out_weight,
    norm_gain,
    gate_weight,
    up_weight,
    down_weight,
):
    factor = 1.0 / math.sqrt(HD)
    width_here = dec_query.shape[1]
    req_count = lax.axis_size("req")
    head_count = lax.axis_size("head")
    me = lax.axis_index("req")
    groups_here = cache_key.shape[0]
    length_cache = cache_key.shape[1]
    per_home = dec_query.shape[0]
    members = group_of[:, 0]
    total_reqs = members.shape[0]

    holder_of = members // groups_here
    holder_hot = (holder_of[:, None] == jnp.arange(req_count, dtype=jnp.int32)[None, :]).astype(jnp.int32)
    rank_all = rank_within(holder_hot.reshape(req_count, per_home, req_count), 1).reshape(total_reqs)
    slot_of = (jnp.arange(total_reqs, dtype=jnp.int32) // per_home) * per_home + rank_all

    my_holder = lax.dynamic_slice_in_dim(holder_of, me * per_home, per_home)
    my_rank = lax.dynamic_slice_in_dim(rank_all, me * per_home, per_home)
    my_slot = my_holder * per_home + my_rank
    packer = (
        my_slot[None, :] == jnp.arange(req_count * per_home, dtype=jnp.int32)[:, None]
    ).astype(jnp.bfloat16)
    stacked_in = jnp.concatenate([dec_query, dec_key, dec_value], axis=1)
    outgoing_q = jnp.dot(packer, stacked_in, preferred_element_type=jnp.float32).astype(jnp.bfloat16)
    arrived_q = lax.all_to_all(outgoing_q, "req", split_axis=0, concat_axis=0, tiled=True)

    first_group = me * groups_here
    wanted = first_group + jnp.arange(groups_here, dtype=jnp.int32)
    belongs = (members[None, :] == wanted[:, None]).astype(jnp.int32)
    ranking = jnp.cumsum(belongs, axis=1) - 1
    places = jnp.arange(CAP, dtype=jnp.int32)
    chosen = ((belongs[:, None, :] == 1) & (ranking[:, None, :] == places[None, :, None])).reshape(
        groups_here * CAP, total_reqs
    )
    chosen_slot = jnp.sum(jnp.where(chosen, slot_of[None, :], 0), axis=1)
    chosen_any = jnp.any(chosen, axis=1)
    chooser = chosen_any[:, None] & (
        chosen_slot[:, None] == jnp.arange(req_count * per_home, dtype=jnp.int32)[None, :]
    )
    picked = jnp.dot(
        chooser.astype(jnp.bfloat16), arrived_q, preferred_element_type=jnp.float32
    ).astype(jnp.bfloat16)
    heads_here = width_here // HD
    head_mask = (jnp.arange(width_here) // HD)[None, :] == jnp.arange(heads_here)[:, None]
    positions = jnp.arange(length_cache)
    results = []
    for group_pos in range(groups_here):
        rows_block = picked[group_pos * CAP : (group_pos + 1) * CAP]
        q_rows = rows_block[:, :width_here]
        k_own = rows_block[:, width_here : 2 * width_here]
        v_own = rows_block[:, 2 * width_here :]
        q_stack = jnp.where(head_mask[:, None, :], q_rows[None], 0).reshape(heads_here * CAP, width_here)
        cache_scores = lax.dot_general(
            q_stack, cache_key[group_pos], (((1,), (1,)), ((), ())), preferred_element_type=jnp.float32
        ) * factor
        own_prod = q_rows.astype(jnp.float32) * k_own.astype(jnp.float32)
        own_scores = (
            jnp.sum(jnp.where(head_mask[:, None, :], own_prod[None], 0.0), axis=-1).reshape(heads_here * CAP, 1)
            * factor
        )
        valid = (positions < cache_length[group_pos])[None, :]
        cache_scores = jnp.where(valid, cache_scores, -jnp.inf)
        highest = jnp.maximum(jnp.max(cache_scores, axis=-1, keepdims=True), own_scores)
        raised = jnp.exp(cache_scores - highest)
        raised_own = jnp.exp(own_scores - highest)
        total = jnp.sum(raised, axis=-1, keepdims=True) + raised_own
        weights = (raised / total).astype(jnp.bfloat16)
        weight_own = (raised_own / total).astype(jnp.bfloat16).astype(jnp.float32)
        mixed = jnp.dot(weights, cache_value[group_pos], preferred_element_type=jnp.float32)
        mixed = mixed + weight_own * v_own.astype(jnp.float32)[None].repeat(heads_here, 0).reshape(
            heads_here * CAP, width_here
        )
        blended = jnp.sum(
            jnp.where(head_mask[:, None, :], mixed.reshape(heads_here, CAP, width_here), 0.0), axis=0
        )
        results.append(blended)
    stacked = jnp.concatenate(results, axis=0).astype(jnp.bfloat16)
    going_back = jnp.dot(
        chooser.astype(jnp.bfloat16).T, stacked, preferred_element_type=jnp.float32
    ).astype(jnp.bfloat16)
    came_back = lax.all_to_all(going_back, "req", split_axis=0, concat_axis=0, tiled=True)
    dec_out = jnp.dot(packer.T, came_back, preferred_element_type=jnp.float32).astype(jnp.bfloat16)

    stretch_len = pre_query.shape[0]
    row_numbers = jnp.arange(stretch_len)
    pre_stack = jnp.where(head_mask[:, None, :], pre_query[None], 0).reshape(heads_here * stretch_len, width_here)
    dims = (((1,), (1,)), ((), ()))
    cache_part = lax.dot_general(pre_stack, cache_key[0], dims, preferred_element_type=jnp.float32) * factor
    self_part = lax.dot_general(pre_stack, pre_key, dims, preferred_element_type=jnp.float32) * factor
    cache_part = jnp.where((positions < stretch_start[0])[None, :], cache_part, -jnp.inf)
    causal = (row_numbers[None, :] <= row_numbers[:, None])[None]
    self_part = jnp.where(causal, self_part.reshape(heads_here, stretch_len, stretch_len), -jnp.inf).reshape(
        heads_here * stretch_len, stretch_len
    )
    highest = jnp.maximum(
        jnp.max(cache_part, axis=-1, keepdims=True), jnp.max(self_part, axis=-1, keepdims=True)
    )
    raised_cache = jnp.exp(cache_part - highest)
    raised_self = jnp.exp(self_part - highest)
    total = jnp.sum(raised_cache, axis=-1, keepdims=True) + jnp.sum(raised_self, axis=-1, keepdims=True)
    pre_mixed = jnp.dot(
        (raised_cache / total).astype(jnp.bfloat16), cache_value[0], preferred_element_type=jnp.float32
    ) + jnp.dot((raised_self / total).astype(jnp.bfloat16), pre_value, preferred_element_type=jnp.float32)
    pre_out = jnp.sum(
        jnp.where(head_mask[:, None, :], pre_mixed.reshape(heads_here, stretch_len, width_here), 0.0), axis=0
    ).astype(jnp.bfloat16)
    head_me = lax.axis_index("head")
    col_start = head_me * width_here

    def feed_forward(attn_chunk, hidden_chunk):
        projected = jnp.dot(attn_chunk, out_weight, preferred_element_type=jnp.float32)
        own_cols = lax.dynamic_slice_in_dim(projected, col_start, width_here, 1) + hidden_chunk.astype(
            jnp.float32
        )
        contribution = lax.dynamic_update_slice_in_dim(projected, own_cols, col_start, 1)
        own_residual = pair_then_z_scatter(contribution.astype(jnp.bfloat16)).astype(jnp.bfloat16)
        residual = z_then_pair_gather(own_residual)
        residual_wide = residual.astype(jnp.float32)
        squares = jnp.mean(jnp.square(residual_wide), axis=-1, keepdims=True)
        normed = (residual_wide * lax.rsqrt(squares + eps_norm) * norm_gain).astype(jnp.bfloat16)
        gate_act = jnp.dot(normed, gate_weight, preferred_element_type=jnp.float32)
        up_act = jnp.dot(normed, up_weight, preferred_element_type=jnp.float32)
        hidden = (jax.nn.silu(gate_act) * up_act).astype(jnp.bfloat16)
        down_part = jnp.dot(hidden, down_weight, preferred_element_type=jnp.float32).astype(jnp.bfloat16)
        down_cols = pair_then_z_scatter(down_part)
        return (own_residual.astype(jnp.float32) + down_cols).astype(jnp.bfloat16)

    pre_cols = feed_forward(pre_out, hidden_in[per_home:])
    dec_cols = feed_forward(dec_out, hidden_in[:per_home])
    out_cols = jnp.concatenate([dec_cols, pre_cols], axis=0)

    row_count = hidden_in.shape[0]
    slot_rows = 8 * ((2 * row_count + 8 * req_count - 1) // (8 * req_count))
    owners = row_owner[:, 0]
    onehot_owner = (owners[:, None] == jnp.arange(req_count, dtype=jnp.int32)[None, :]).astype(
        jnp.int32
    )
    before = rank_within(onehot_owner, 0)
    target = owners * slot_rows + before
    placing = (
        target[None, :] == jnp.arange(req_count * slot_rows, dtype=jnp.int32)[:, None]
    ).astype(jnp.bfloat16)
    outgoing = jnp.dot(placing, out_cols, preferred_element_type=jnp.float32).astype(jnp.bfloat16)
    arrived = lax.all_to_all(outgoing, "req", split_axis=0, concat_axis=0, tiled=True)
    return lax.all_to_all(arrived, "head", split_axis=0, concat_axis=1, tiled=True)


def solution(mesh):
    placed = (
        P("req", "head"),
        P("req", "head"),
        P("req", "head"),
        P("req", "head"),
        P("req", "head"),
        P("req", "head"),
        P("req", "head"),
        P("req", None, "head"),
        P("req", None, "head"),
        P(),
        P("req"),
        P("req"),
        P("req", None),
        P("head", None),
        P(),
        P(None, "head"),
        P(None, "head"),
        P("head", None),
    )
    return jax.shard_map(
        on_device, mesh=mesh, in_specs=placed, out_specs=P(("req", "head"), None), check_vma=False
    )
```

```python
import math

import jax
import jax.numpy as jnp
from jax import lax
from jax.sharding import PartitionSpec as P

HD = 96
CAP = 48


eps_norm = 1e-05


def rank_within(onehot, axis):
    return jnp.sum((jnp.cumsum(onehot, axis=axis) - 1) * onehot, axis=-1)


def pair_then_z_scatter(x):
    rows, cols = x.shape
    n = lax.axis_size("head")
    ring = n // 2
    width = cols // n
    h = lax.axis_index("head")
    zc = h // 2
    on_first = h % 2 == 0
    even = jnp.concatenate([x[:, (2 * z) * width : (2 * z + 1) * width] for z in range(ring)], 1)
    odd = jnp.concatenate([x[:, (2 * z + 1) * width : (2 * z + 2) * width] for z in range(ring)], 1)
    mine = jnp.where(on_first, even, odd)
    other = jnp.where(on_first, odd, even)
    got = lax.ppermute(other, "head", [(i, i ^ 1) for i in range(n)])
    pair_sum = (mine.astype(jnp.float32) + got.astype(jnp.float32)).astype(jnp.bfloat16)
    acc = lax.dynamic_slice_in_dim(pair_sum, zc * width, width, 1).astype(jnp.float32)
    for d in range(1, ring):
        perm = [(i, ((i // 2 + d) % ring) * 2 + i % 2) for i in range(n)]
        piece = lax.dynamic_slice_in_dim(pair_sum, ((zc + d) % ring) * width, width, 1)
        acc = acc + lax.ppermute(piece, "head", perm).astype(jnp.float32)
    return acc


def z_then_pair_gather(y):
    rows, width = y.shape
    n = lax.axis_size("head")
    ring = n // 2
    h = lax.axis_index("head")
    zc = h // 2
    on_first = h % 2 == 0
    parts = [y]
    for d in range(1, ring):
        perm = [(i, ((i // 2 + d) % ring) * 2 + i % 2) for i in range(n)]
        parts.append(lax.ppermute(y, "head", perm))
    stacked = jnp.stack(parts, 0)
    in_order = jnp.concatenate(
        [lax.dynamic_index_in_dim(stacked, (zc - zz) % ring, 0, keepdims=False) for zz in range(ring)], 1
    )
    got = lax.ppermute(in_order, "head", [(i, i ^ 1) for i in range(n)])
    pieces = []
    for z in range(ring):
        mine_z = in_order[:, z * width : (z + 1) * width]
        got_z = got[:, z * width : (z + 1) * width]
        pieces.append(jnp.where(on_first, mine_z, got_z))
        pieces.append(jnp.where(on_first, got_z, mine_z))
    return jnp.concatenate(pieces, 1)


def on_device(
    hidden_in,
    dec_query,
    dec_key,
    dec_value,
    pre_query,
    pre_key,
    pre_value,
    cache_key,
    cache_value,
    group_of,
    cache_length,
    stretch_start,
    row_owner,
    out_weight,
    norm_gain,
    gate_weight,
    up_weight,
    down_weight,
):
    factor = 1.0 / math.sqrt(HD)
    width_here = dec_query.shape[1]
    req_count = lax.axis_size("req")
    head_count = lax.axis_size("head")
    me = lax.axis_index("req")
    groups_here = cache_key.shape[0]
    length_cache = cache_key.shape[1]
    per_home = dec_query.shape[0]
    members = group_of[:, 0]
    total_reqs = members.shape[0]

    holder_of = members // groups_here
    holder_hot = (holder_of[:, None] == jnp.arange(req_count, dtype=jnp.int32)[None, :]).astype(jnp.int32)
    rank_all = rank_within(holder_hot.reshape(req_count, per_home, req_count), 1).reshape(total_reqs)
    slot_of = (jnp.arange(total_reqs, dtype=jnp.int32) // per_home) * per_home + rank_all

    my_holder = lax.dynamic_slice_in_dim(holder_of, me * per_home, per_home)
    my_rank = lax.dynamic_slice_in_dim(rank_all, me * per_home, per_home)
    my_slot = my_holder * per_home + my_rank
    packer = (
        my_slot[None, :] == jnp.arange(req_count * per_home, dtype=jnp.int32)[:, None]
    ).astype(jnp.bfloat16)
    stacked_in = jnp.concatenate([dec_query, dec_key, dec_value], axis=1)
    outgoing_q = jnp.dot(packer, stacked_in, preferred_element_type=jnp.float32).astype(jnp.bfloat16)
    outgoing_q, pre_query, pre_key, pre_value = lax.optimization_barrier(
        (outgoing_q, pre_query, pre_key, pre_value)
    )
    arrived_q = lax.all_to_all(outgoing_q, "req", split_axis=0, concat_axis=0, tiled=True)

    first_group = me * groups_here
    wanted = first_group + jnp.arange(groups_here, dtype=jnp.int32)
    belongs = (members[None, :] == wanted[:, None]).astype(jnp.int32)
    ranking = jnp.cumsum(belongs, axis=1) - 1
    places = jnp.arange(CAP, dtype=jnp.int32)
    chosen = ((belongs[:, None, :] == 1) & (ranking[:, None, :] == places[None, :, None])).reshape(
        groups_here * CAP, total_reqs
    )
    chosen_slot = jnp.sum(jnp.where(chosen, slot_of[None, :], 0), axis=1)
    chosen_any = jnp.any(chosen, axis=1)
    chooser = chosen_any[:, None] & (
        chosen_slot[:, None] == jnp.arange(req_count * per_home, dtype=jnp.int32)[None, :]
    )
    picked = jnp.dot(
        chooser.astype(jnp.bfloat16), arrived_q, preferred_element_type=jnp.float32
    ).astype(jnp.bfloat16)
    heads_here = width_here // HD
    head_mask = (jnp.arange(width_here) // HD)[None, :] == jnp.arange(heads_here)[:, None]
    positions = jnp.arange(length_cache)
    results = []
    for group_pos in range(groups_here):
        rows_block = picked[group_pos * CAP : (group_pos + 1) * CAP]
        q_rows = rows_block[:, :width_here]
        k_own = rows_block[:, width_here : 2 * width_here]
        v_own = rows_block[:, 2 * width_here :]
        q_stack = jnp.where(head_mask[:, None, :], q_rows[None], 0).reshape(heads_here * CAP, width_here)
        cache_scores = lax.dot_general(
            q_stack, cache_key[group_pos], (((1,), (1,)), ((), ())), preferred_element_type=jnp.float32
        ) * factor
        own_prod = q_rows.astype(jnp.float32) * k_own.astype(jnp.float32)
        own_scores = (
            jnp.sum(jnp.where(head_mask[:, None, :], own_prod[None], 0.0), axis=-1).reshape(heads_here * CAP, 1)
            * factor
        )
        valid = (positions < cache_length[group_pos])[None, :]
        cache_scores = jnp.where(valid, cache_scores, -jnp.inf)
        highest = jnp.maximum(jnp.max(cache_scores, axis=-1, keepdims=True), own_scores)
        raised = jnp.exp(cache_scores - highest)
        raised_own = jnp.exp(own_scores - highest)
        total = jnp.sum(raised, axis=-1, keepdims=True) + raised_own
        weights = (raised / total).astype(jnp.bfloat16)
        weight_own = (raised_own / total).astype(jnp.bfloat16).astype(jnp.float32)
        mixed = jnp.dot(weights, cache_value[group_pos], preferred_element_type=jnp.float32)
        mixed = mixed + weight_own * v_own.astype(jnp.float32)[None].repeat(heads_here, 0).reshape(
            heads_here * CAP, width_here
        )
        blended = jnp.sum(
            jnp.where(head_mask[:, None, :], mixed.reshape(heads_here, CAP, width_here), 0.0), axis=0
        )
        results.append(blended)
    stacked = jnp.concatenate(results, axis=0).astype(jnp.bfloat16)
    going_back = jnp.dot(
        chooser.astype(jnp.bfloat16).T, stacked, preferred_element_type=jnp.float32
    ).astype(jnp.bfloat16)
    came_back = lax.all_to_all(going_back, "req", split_axis=0, concat_axis=0, tiled=True)
    dec_out = jnp.dot(packer.T, came_back, preferred_element_type=jnp.float32).astype(jnp.bfloat16)

    stretch_len = pre_query.shape[0]
    row_numbers = jnp.arange(stretch_len)
    pre_stack = jnp.where(head_mask[:, None, :], pre_query[None], 0).reshape(heads_here * stretch_len, width_here)
    dims = (((1,), (1,)), ((), ()))
    cache_part = lax.dot_general(pre_stack, cache_key[0], dims, preferred_element_type=jnp.float32) * factor
    self_part = lax.dot_general(pre_stack, pre_key, dims, preferred_element_type=jnp.float32) * factor
    cache_part = jnp.where((positions < stretch_start[0])[None, :], cache_part, -jnp.inf)
    causal = (row_numbers[None, :] <= row_numbers[:, None])[None]
    self_part = jnp.where(causal, self_part.reshape(heads_here, stretch_len, stretch_len), -jnp.inf).reshape(
        heads_here * stretch_len, stretch_len
    )
    highest = jnp.maximum(
        jnp.max(cache_part, axis=-1, keepdims=True), jnp.max(self_part, axis=-1, keepdims=True)
    )
    raised_cache = jnp.exp(cache_part - highest)
    raised_self = jnp.exp(self_part - highest)
    total = jnp.sum(raised_cache, axis=-1, keepdims=True) + jnp.sum(raised_self, axis=-1, keepdims=True)
    pre_mixed = jnp.dot(
        (raised_cache / total).astype(jnp.bfloat16), cache_value[0], preferred_element_type=jnp.float32
    ) + jnp.dot((raised_self / total).astype(jnp.bfloat16), pre_value, preferred_element_type=jnp.float32)
    pre_out = jnp.sum(
        jnp.where(head_mask[:, None, :], pre_mixed.reshape(heads_here, stretch_len, width_here), 0.0), axis=0
    ).astype(jnp.bfloat16)
    head_me = lax.axis_index("head")
    col_start = head_me * width_here

    def feed_forward(attn_chunk, hidden_chunk):
        projected = jnp.dot(attn_chunk, out_weight, preferred_element_type=jnp.float32)
        own_cols = lax.dynamic_slice_in_dim(projected, col_start, width_here, 1) + hidden_chunk.astype(
            jnp.float32
        )
        contribution = lax.dynamic_update_slice_in_dim(projected, own_cols, col_start, 1)
        own_residual = pair_then_z_scatter(contribution.astype(jnp.bfloat16)).astype(jnp.bfloat16)
        residual = z_then_pair_gather(own_residual)
        residual_wide = residual.astype(jnp.float32)
        squares = jnp.mean(jnp.square(residual_wide), axis=-1, keepdims=True)
        normed = (residual_wide * lax.rsqrt(squares + eps_norm) * norm_gain).astype(jnp.bfloat16)
        gate_act = jnp.dot(normed, gate_weight, preferred_element_type=jnp.float32)
        up_act = jnp.dot(normed, up_weight, preferred_element_type=jnp.float32)
        hidden = (jax.nn.silu(gate_act) * up_act).astype(jnp.bfloat16)
        down_part = jnp.dot(hidden, down_weight, preferred_element_type=jnp.float32).astype(jnp.bfloat16)
        down_cols = pair_then_z_scatter(down_part)
        return (own_residual.astype(jnp.float32) + down_cols).astype(jnp.bfloat16)

    pre_cols = feed_forward(pre_out, hidden_in[per_home:])
    dec_cols = feed_forward(dec_out, hidden_in[:per_home])
    out_cols = jnp.concatenate([dec_cols, pre_cols], axis=0)

    row_count = hidden_in.shape[0]
    slot_rows = 8 * ((2 * row_count + 8 * req_count - 1) // (8 * req_count))
    owners = row_owner[:, 0]
    onehot_owner = (owners[:, None] == jnp.arange(req_count, dtype=jnp.int32)[None, :]).astype(
        jnp.int32
    )
    before = rank_within(onehot_owner, 0)
    target = owners * slot_rows + before
    placing = (
        target[None, :] == jnp.arange(req_count * slot_rows, dtype=jnp.int32)[:, None]
    ).astype(jnp.bfloat16)
    outgoing = jnp.dot(placing, out_cols, preferred_element_type=jnp.float32).astype(jnp.bfloat16)
    arrived = lax.all_to_all(outgoing, "req", split_axis=0, concat_axis=0, tiled=True)
    return lax.all_to_all(arrived, "head", split_axis=0, concat_axis=1, tiled=True)


def solution(mesh):
    placed = (
        P("req", "head"),
        P("req", "head"),
        P("req", "head"),
        P("req", "head"),
        P("req", "head"),
        P("req", "head"),
        P("req", "head"),
        P("req", None, "head"),
        P("req", None, "head"),
        P(),
        P("req"),
        P("req"),
        P("req", None),
        P("head", None),
        P(),
        P(None, "head"),
        P(None, "head"),
        P("head", None),
    )
    return jax.shard_map(
        on_device, mesh=mesh, in_specs=placed, out_specs=P(("req", "head"), None), check_vma=False
    )
```

```python
import math

import jax
import jax.numpy as jnp
from jax import lax
from jax.sharding import PartitionSpec as P

HD = 96
CAP = 48


eps_norm = 1e-05


def rank_within(onehot, axis):
    return jnp.sum((jnp.cumsum(onehot, axis=axis) - 1) * onehot, axis=-1)


def pair_then_z_scatter(x):
    rows, cols = x.shape
    n = lax.axis_size("head")
    ring = n // 2
    width = cols // n
    h = lax.axis_index("head")
    zc = h // 2
    on_first = h % 2 == 0
    even = jnp.concatenate([x[:, (2 * z) * width : (2 * z + 1) * width] for z in range(ring)], 1)
    odd = jnp.concatenate([x[:, (2 * z + 1) * width : (2 * z + 2) * width] for z in range(ring)], 1)
    mine = jnp.where(on_first, even, odd)
    other = jnp.where(on_first, odd, even)
    got = lax.ppermute(other, "head", [(i, i ^ 1) for i in range(n)])
    pair_sum = (mine.astype(jnp.float32) + got.astype(jnp.float32)).astype(jnp.bfloat16)
    acc = lax.dynamic_slice_in_dim(pair_sum, zc * width, width, 1).astype(jnp.float32)
    for d in range(1, ring):
        perm = [(i, ((i // 2 + d) % ring) * 2 + i % 2) for i in range(n)]
        piece = lax.dynamic_slice_in_dim(pair_sum, ((zc + d) % ring) * width, width, 1)
        acc = acc + lax.ppermute(piece, "head", perm).astype(jnp.float32)
    return acc


def z_then_pair_gather(y):
    rows, width = y.shape
    n = lax.axis_size("head")
    ring = n // 2
    h = lax.axis_index("head")
    zc = h // 2
    on_first = h % 2 == 0
    parts = [y]
    for d in range(1, ring):
        perm = [(i, ((i // 2 + d) % ring) * 2 + i % 2) for i in range(n)]
        parts.append(lax.ppermute(y, "head", perm))
    stacked = jnp.stack(parts, 0)
    in_order = jnp.concatenate(
        [lax.dynamic_index_in_dim(stacked, (zc - zz) % ring, 0, keepdims=False) for zz in range(ring)], 1
    )
    got = lax.ppermute(in_order, "head", [(i, i ^ 1) for i in range(n)])
    pieces = []
    for z in range(ring):
        mine_z = in_order[:, z * width : (z + 1) * width]
        got_z = got[:, z * width : (z + 1) * width]
        pieces.append(jnp.where(on_first, mine_z, got_z))
        pieces.append(jnp.where(on_first, got_z, mine_z))
    return jnp.concatenate(pieces, 1)


def on_device(
    hidden_in,
    dec_query,
    dec_key,
    dec_value,
    pre_query,
    pre_key,
    pre_value,
    cache_key,
    cache_value,
    group_of,
    cache_length,
    stretch_start,
    row_owner,
    out_weight,
    norm_gain,
    gate_weight,
    up_weight,
    down_weight,
):
    factor = 1.0 / math.sqrt(HD)
    width_here = dec_query.shape[1]
    req_count = lax.axis_size("req")
    head_count = lax.axis_size("head")
    me = lax.axis_index("req")
    groups_here = cache_key.shape[0]
    length_cache = cache_key.shape[1]
    per_home = dec_query.shape[0]
    members = group_of[:, 0]
    total_reqs = members.shape[0]

    holder_of = members // groups_here
    holder_hot = (holder_of[:, None] == jnp.arange(req_count, dtype=jnp.int32)[None, :]).astype(jnp.int32)
    rank_all = rank_within(holder_hot.reshape(req_count, per_home, req_count), 1).reshape(total_reqs)
    slot_of = (jnp.arange(total_reqs, dtype=jnp.int32) // per_home) * per_home + rank_all

    my_holder = lax.dynamic_slice_in_dim(holder_of, me * per_home, per_home)
    my_rank = lax.dynamic_slice_in_dim(rank_all, me * per_home, per_home)
    my_slot = my_holder * per_home + my_rank
    packer = (
        my_slot[None, :] == jnp.arange(req_count * per_home, dtype=jnp.int32)[:, None]
    ).astype(jnp.bfloat16)
    outgoing_q = jnp.dot(packer, dec_query, preferred_element_type=jnp.float32).astype(jnp.bfloat16)
    arrived_q = lax.all_to_all(outgoing_q, "req", split_axis=0, concat_axis=0, tiled=True)

    first_group = me * groups_here
    wanted = first_group + jnp.arange(groups_here, dtype=jnp.int32)
    belongs = (members[None, :] == wanted[:, None]).astype(jnp.int32)
    ranking = jnp.cumsum(belongs, axis=1) - 1
    places = jnp.arange(CAP, dtype=jnp.int32)
    chosen = ((belongs[:, None, :] == 1) & (ranking[:, None, :] == places[None, :, None])).reshape(
        groups_here * CAP, total_reqs
    )
    chosen_slot = jnp.sum(jnp.where(chosen, slot_of[None, :], 0), axis=1)
    chosen_any = jnp.any(chosen, axis=1)
    chooser = chosen_any[:, None] & (
        chosen_slot[:, None] == jnp.arange(req_count * per_home, dtype=jnp.int32)[None, :]
    )
    picked = jnp.dot(
        chooser.astype(jnp.bfloat16), arrived_q, preferred_element_type=jnp.float32
    ).astype(jnp.bfloat16)
    heads_here = width_here // HD
    head_mask = (jnp.arange(width_here) // HD)[None, :] == jnp.arange(heads_here)[:, None]
    positions = jnp.arange(length_cache)
    results = []
    pad_cols = 128
    for group_pos in range(groups_here):
        q_rows = picked[group_pos * CAP : (group_pos + 1) * CAP]
        q_stack = jnp.where(head_mask[:, None, :], q_rows[None], 0).reshape(heads_here * CAP, width_here)
        cache_scores = lax.dot_general(
            q_stack, cache_key[group_pos], (((1,), (1,)), ((), ())), preferred_element_type=jnp.float32
        ) * factor
        valid = (positions < cache_length[group_pos])[None, :]
        cache_scores = jnp.where(valid, cache_scores, -jnp.inf)
        highest = jnp.max(cache_scores, axis=-1, keepdims=True)
        raised = jnp.exp(cache_scores - highest)
        total = jnp.sum(raised, axis=-1, keepdims=True)
        weights = (raised / total).astype(jnp.bfloat16)
        mixed = jnp.dot(weights, cache_value[group_pos], preferred_element_type=jnp.float32)
        blended = jnp.sum(
            jnp.where(head_mask[:, None, :], mixed.reshape(heads_here, CAP, width_here), 0.0), axis=0
        )
        spread = (highest + jnp.log(total)).reshape(heads_here, CAP).T
        spread_hi = spread.astype(jnp.bfloat16)
        spread_lo = (spread - spread_hi.astype(jnp.float32)).astype(jnp.bfloat16)
        tail = jnp.zeros((CAP, pad_cols - 2 * heads_here), jnp.bfloat16)
        results.append(
            jnp.concatenate([blended.astype(jnp.bfloat16), spread_hi, spread_lo, tail], axis=1)
        )
    stacked = jnp.concatenate(results, axis=0)
    going_back = jnp.dot(
        chooser.astype(jnp.bfloat16).T, stacked, preferred_element_type=jnp.float32
    ).astype(jnp.bfloat16)
    came_back = lax.all_to_all(going_back, "req", split_axis=0, concat_axis=0, tiled=True)
    dec_back = jnp.dot(packer.T, came_back, preferred_element_type=jnp.float32)
    cache_mix = dec_back[:, :width_here]
    cache_spread = (
        dec_back[:, width_here : width_here + heads_here]
        + dec_back[:, width_here + heads_here : width_here + 2 * heads_here]
    )
    own_prod = dec_query.astype(jnp.float32) * dec_key.astype(jnp.float32)
    own_scores = jnp.sum(jnp.where(head_mask[:, None, :], own_prod[None], 0.0), axis=-1).T * factor
    top = jnp.maximum(cache_spread, own_scores)
    part_cache = jnp.exp(cache_spread - top)
    part_own = jnp.exp(own_scores - top)
    share_own = part_own / (part_cache + part_own)
    share_cols = jnp.sum(jnp.where(head_mask[:, None, :], share_own.T[:, :, None], 0.0), axis=0)
    dec_out = (
        (1.0 - share_cols) * cache_mix + share_cols * dec_value.astype(jnp.float32)
    ).astype(jnp.bfloat16)

    stretch_len = pre_query.shape[0]
    row_numbers = jnp.arange(stretch_len)
    pre_stack = jnp.where(head_mask[:, None, :], pre_query[None], 0).reshape(heads_here * stretch_len, width_here)
    dims = (((1,), (1,)), ((), ()))
    cache_part = lax.dot_general(pre_stack, cache_key[0], dims, preferred_element_type=jnp.float32) * factor
    self_part = lax.dot_general(pre_stack, pre_key, dims, preferred_element_type=jnp.float32) * factor
    cache_part = jnp.where((positions < stretch_start[0])[None, :], cache_part, -jnp.inf)
    causal = (row_numbers[None, :] <= row_numbers[:, None])[None]
    self_part = jnp.where(causal, self_part.reshape(heads_here, stretch_len, stretch_len), -jnp.inf).reshape(
        heads_here * stretch_len, stretch_len
    )
    highest = jnp.maximum(
        jnp.max(cache_part, axis=-1, keepdims=True), jnp.max(self_part, axis=-1, keepdims=True)
    )
    raised_cache = jnp.exp(cache_part - highest)
    raised_self = jnp.exp(self_part - highest)
    total = jnp.sum(raised_cache, axis=-1, keepdims=True) + jnp.sum(raised_self, axis=-1, keepdims=True)
    pre_mixed = jnp.dot(
        (raised_cache / total).astype(jnp.bfloat16), cache_value[0], preferred_element_type=jnp.float32
    ) + jnp.dot((raised_self / total).astype(jnp.bfloat16), pre_value, preferred_element_type=jnp.float32)
    pre_out = jnp.sum(
        jnp.where(head_mask[:, None, :], pre_mixed.reshape(heads_here, stretch_len, width_here), 0.0), axis=0
    ).astype(jnp.bfloat16)
    attn_rows = jnp.concatenate([dec_out, pre_out], axis=0)
    projected = jnp.dot(attn_rows, out_weight, preferred_element_type=jnp.float32)
    head_me = lax.axis_index("head")
    col_start = head_me * width_here
    own_cols = lax.dynamic_slice_in_dim(projected, col_start, width_here, 1) + hidden_in.astype(
        jnp.float32
    )
    contribution = lax.dynamic_update_slice_in_dim(projected, own_cols, col_start, 1)
    own_residual = pair_then_z_scatter(contribution.astype(jnp.bfloat16))
    residual = z_then_pair_gather(own_residual.astype(jnp.bfloat16))

    residual_wide = residual.astype(jnp.float32)
    squares = jnp.mean(jnp.square(residual_wide), axis=-1, keepdims=True)
    normed = (residual_wide * lax.rsqrt(squares + eps_norm) * norm_gain).astype(jnp.bfloat16)
    gate_act = jnp.dot(normed, gate_weight, preferred_element_type=jnp.float32)
    up_act = jnp.dot(normed, up_weight, preferred_element_type=jnp.float32)
    hidden = (jax.nn.silu(gate_act) * up_act).astype(jnp.bfloat16)
    down_part = jnp.dot(hidden, down_weight, preferred_element_type=jnp.float32).astype(jnp.bfloat16)
    down_cols = pair_then_z_scatter(down_part)
    own_wide = own_residual.astype(jnp.bfloat16).astype(jnp.float32)
    out_cols = (own_wide + down_cols).astype(jnp.bfloat16)

    row_count = residual.shape[0]
    slot_rows = 8 * ((2 * row_count + 8 * req_count - 1) // (8 * req_count))
    owners = row_owner[:, 0]
    onehot_owner = (owners[:, None] == jnp.arange(req_count, dtype=jnp.int32)[None, :]).astype(
        jnp.int32
    )
    before = rank_within(onehot_owner, 0)
    target = owners * slot_rows + before
    placing = (
        target[None, :] == jnp.arange(req_count * slot_rows, dtype=jnp.int32)[:, None]
    ).astype(jnp.bfloat16)
    outgoing = jnp.dot(placing, out_cols, preferred_element_type=jnp.float32).astype(jnp.bfloat16)
    arrived = lax.all_to_all(outgoing, "req", split_axis=0, concat_axis=0, tiled=True)
    return lax.all_to_all(arrived, "head", split_axis=0, concat_axis=1, tiled=True)


def solution(mesh):
    placed = (
        P("req", "head"),
        P("req", "head"),
        P("req", "head"),
        P("req", "head"),
        P("req", "head"),
        P("req", "head"),
        P("req", "head"),
        P("req", None, "head"),
        P("req", None, "head"),
        P(),
        P("req"),
        P("req"),
        P("req", None),
        P("head", None),
        P(),
        P(None, "head"),
        P(None, "head"),
        P("head", None),
    )
    return jax.shard_map(
        on_device, mesh=mesh, in_specs=placed, out_specs=P(("req", "head"), None), check_vma=False
    )
```

```python
import math

import jax
import jax.numpy as jnp
from jax import lax
from jax.sharding import PartitionSpec as P

HD = 96
CAP = 48


eps_norm = 1e-05


def rank_within(onehot, axis):
    return jnp.sum((jnp.cumsum(onehot, axis=axis) - 1) * onehot, axis=-1)


def pair_then_z_scatter(x):
    rows, cols = x.shape
    n = lax.axis_size("head")
    ring = n // 2
    width = cols // n
    h = lax.axis_index("head")
    zc = h // 2
    on_first = h % 2 == 0
    even = jnp.concatenate([x[:, (2 * z) * width : (2 * z + 1) * width] for z in range(ring)], 1)
    odd = jnp.concatenate([x[:, (2 * z + 1) * width : (2 * z + 2) * width] for z in range(ring)], 1)
    mine = jnp.where(on_first, even, odd)
    other = jnp.where(on_first, odd, even)
    got = lax.ppermute(other, "head", [(i, i ^ 1) for i in range(n)])
    pair_sum = (mine.astype(jnp.float32) + got.astype(jnp.float32)).astype(jnp.bfloat16)
    acc = lax.dynamic_slice_in_dim(pair_sum, zc * width, width, 1).astype(jnp.float32)
    for d in range(1, ring):
        perm = [(i, ((i // 2 + d) % ring) * 2 + i % 2) for i in range(n)]
        piece = lax.dynamic_slice_in_dim(pair_sum, ((zc + d) % ring) * width, width, 1)
        acc = acc + lax.ppermute(piece, "head", perm).astype(jnp.float32)
    return acc


def z_then_pair_gather(y):
    rows, width = y.shape
    n = lax.axis_size("head")
    ring = n // 2
    h = lax.axis_index("head")
    zc = h // 2
    on_first = h % 2 == 0
    parts = [y]
    for d in range(1, ring):
        perm = [(i, ((i // 2 + d) % ring) * 2 + i % 2) for i in range(n)]
        parts.append(lax.ppermute(y, "head", perm))
    stacked = jnp.stack(parts, 0)
    in_order = jnp.concatenate(
        [lax.dynamic_index_in_dim(stacked, (zc - zz) % ring, 0, keepdims=False) for zz in range(ring)], 1
    )
    got = lax.ppermute(in_order, "head", [(i, i ^ 1) for i in range(n)])
    pieces = []
    for z in range(ring):
        mine_z = in_order[:, z * width : (z + 1) * width]
        got_z = got[:, z * width : (z + 1) * width]
        pieces.append(jnp.where(on_first, mine_z, got_z))
        pieces.append(jnp.where(on_first, got_z, mine_z))
    return jnp.concatenate(pieces, 1)


def on_device(
    hidden_in,
    dec_query,
    dec_key,
    dec_value,
    pre_query,
    pre_key,
    pre_value,
    cache_key,
    cache_value,
    group_of,
    cache_length,
    stretch_start,
    row_owner,
    out_weight,
    norm_gain,
    gate_weight,
    up_weight,
    down_weight,
):
    factor = 1.0 / math.sqrt(HD)
    width_here = dec_query.shape[1]
    req_count = lax.axis_size("req")
    head_count = lax.axis_size("head")
    me = lax.axis_index("req")
    groups_here = cache_key.shape[0]
    length_cache = cache_key.shape[1]
    per_home = dec_query.shape[0]
    members = group_of[:, 0]
    total_reqs = members.shape[0]

    holder_of = members // groups_here
    holder_hot = (holder_of[:, None] == jnp.arange(req_count, dtype=jnp.int32)[None, :]).astype(jnp.int32)
    rank_all = rank_within(holder_hot.reshape(req_count, per_home, req_count), 1).reshape(total_reqs)
    slot_of = (jnp.arange(total_reqs, dtype=jnp.int32) // per_home) * per_home + rank_all

    my_holder = lax.dynamic_slice_in_dim(holder_of, me * per_home, per_home)
    my_rank = lax.dynamic_slice_in_dim(rank_all, me * per_home, per_home)
    my_slot = my_holder * per_home + my_rank
    packer = (
        my_slot[None, :] == jnp.arange(req_count * per_home, dtype=jnp.int32)[:, None]
    ).astype(jnp.bfloat16)
    outgoing_q = jnp.dot(packer, dec_query, preferred_element_type=jnp.float32).astype(jnp.bfloat16)
    arrived_q = lax.all_to_all(outgoing_q, "req", split_axis=0, concat_axis=0, tiled=True)

    first_group = me * groups_here
    wanted = first_group + jnp.arange(groups_here, dtype=jnp.int32)
    belongs = (members[None, :] == wanted[:, None]).astype(jnp.int32)
    ranking = jnp.cumsum(belongs, axis=1) - 1
    places = jnp.arange(CAP, dtype=jnp.int32)
    chosen = ((belongs[:, None, :] == 1) & (ranking[:, None, :] == places[None, :, None])).reshape(
        groups_here * CAP, total_reqs
    )
    chosen_slot = jnp.sum(jnp.where(chosen, slot_of[None, :], 0), axis=1)
    chosen_any = jnp.any(chosen, axis=1)
    chooser = chosen_any[:, None] & (
        chosen_slot[:, None] == jnp.arange(req_count * per_home, dtype=jnp.int32)[None, :]
    )
    picked = jnp.dot(
        chooser.astype(jnp.bfloat16), arrived_q, preferred_element_type=jnp.float32
    ).astype(jnp.bfloat16)
    heads_here = width_here // HD
    head_mask = (jnp.arange(width_here) // HD)[None, :] == jnp.arange(heads_here)[:, None]
    positions = jnp.arange(length_cache)
    results = []
    pad_cols = 128
    for group_pos in range(groups_here):
        q_rows = picked[group_pos * CAP : (group_pos + 1) * CAP]
        q_stack = jnp.where(head_mask[:, None, :], q_rows[None], 0).reshape(heads_here * CAP, width_here)
        cache_scores = lax.dot_general(
            q_stack, cache_key[group_pos], (((1,), (1,)), ((), ())), preferred_element_type=jnp.float32
        ) * factor
        valid = (positions < cache_length[group_pos])[None, :]
        cache_scores = jnp.where(valid, cache_scores, -jnp.inf)
        highest = jnp.max(cache_scores, axis=-1, keepdims=True)
        raised = jnp.exp(cache_scores - highest)
        total = jnp.sum(raised, axis=-1, keepdims=True)
        weights = (raised / total).astype(jnp.bfloat16)
        mixed = jnp.dot(weights, cache_value[group_pos], preferred_element_type=jnp.float32)
        blended = jnp.sum(
            jnp.where(head_mask[:, None, :], mixed.reshape(heads_here, CAP, width_here), 0.0), axis=0
        )
        spread = (highest + jnp.log(total)).reshape(heads_here, CAP).T
        spread_hi = spread.astype(jnp.bfloat16)
        spread_lo = (spread - spread_hi.astype(jnp.float32)).astype(jnp.bfloat16)
        tail = jnp.zeros((CAP, pad_cols - 2 * heads_here), jnp.bfloat16)
        results.append(
            jnp.concatenate([blended.astype(jnp.bfloat16), spread_hi, spread_lo, tail], axis=1)
        )
    stacked = jnp.concatenate(results, axis=0)
    going_back = jnp.dot(
        chooser.astype(jnp.bfloat16).T, stacked, preferred_element_type=jnp.float32
    ).astype(jnp.bfloat16)
    came_back = lax.all_to_all(going_back, "req", split_axis=0, concat_axis=0, tiled=True)
    dec_back = jnp.dot(packer.T, came_back, preferred_element_type=jnp.float32)
    cache_mix = dec_back[:, :width_here]
    cache_spread = (
        dec_back[:, width_here : width_here + heads_here]
        + dec_back[:, width_here + heads_here : width_here + 2 * heads_here]
    )
    own_prod = dec_query.astype(jnp.float32) * dec_key.astype(jnp.float32)
    own_scores = jnp.sum(jnp.where(head_mask[:, None, :], own_prod[None], 0.0), axis=-1).T * factor
    top = jnp.maximum(cache_spread, own_scores)
    part_cache = jnp.exp(cache_spread - top)
    part_own = jnp.exp(own_scores - top)
    share_own = part_own / (part_cache + part_own)
    share_cols = jnp.sum(jnp.where(head_mask[:, None, :], share_own.T[:, :, None], 0.0), axis=0)
    dec_out = (
        (1.0 - share_cols) * cache_mix + share_cols * dec_value.astype(jnp.float32)
    ).astype(jnp.bfloat16)

    stretch_len = pre_query.shape[0]
    row_numbers = jnp.arange(stretch_len)
    pre_stack = jnp.where(head_mask[:, None, :], pre_query[None], 0).reshape(heads_here * stretch_len, width_here)
    dims = (((1,), (1,)), ((), ()))
    cache_part = lax.dot_general(pre_stack, cache_key[0], dims, preferred_element_type=jnp.float32) * factor
    self_part = lax.dot_general(pre_stack, pre_key, dims, preferred_element_type=jnp.float32) * factor
    cache_part = jnp.where((positions < stretch_start[0])[None, :], cache_part, -jnp.inf)
    causal = (row_numbers[None, :] <= row_numbers[:, None])[None]
    self_part = jnp.where(causal, self_part.reshape(heads_here, stretch_len, stretch_len), -jnp.inf).reshape(
        heads_here * stretch_len, stretch_len
    )
    highest = jnp.maximum(
        jnp.max(cache_part, axis=-1, keepdims=True), jnp.max(self_part, axis=-1, keepdims=True)
    )
    raised_cache = jnp.exp(cache_part - highest)
    raised_self = jnp.exp(self_part - highest)
    total = jnp.sum(raised_cache, axis=-1, keepdims=True) + jnp.sum(raised_self, axis=-1, keepdims=True)
    pre_mixed = jnp.dot(
        (raised_cache / total).astype(jnp.bfloat16), cache_value[0], preferred_element_type=jnp.float32
    ) + jnp.dot((raised_self / total).astype(jnp.bfloat16), pre_value, preferred_element_type=jnp.float32)
    pre_out = jnp.sum(
        jnp.where(head_mask[:, None, :], pre_mixed.reshape(heads_here, stretch_len, width_here), 0.0), axis=0
    ).astype(jnp.bfloat16)
    dec_out, pre_out = lax.optimization_barrier((dec_out, pre_out))
    attn_rows = jnp.concatenate([dec_out, pre_out], axis=0)
    head_me = lax.axis_index("head")
    col_start = head_me * width_here

    def feed_forward(attn_chunk, hidden_chunk):
        projected = jnp.dot(attn_chunk, out_weight, preferred_element_type=jnp.float32)
        own_cols = lax.dynamic_slice_in_dim(projected, col_start, width_here, 1) + hidden_chunk.astype(
            jnp.float32
        )
        contribution = lax.dynamic_update_slice_in_dim(projected, own_cols, col_start, 1)
        own_residual = pair_then_z_scatter(contribution.astype(jnp.bfloat16)).astype(jnp.bfloat16)
        residual = z_then_pair_gather(own_residual)
        residual_wide = residual.astype(jnp.float32)
        squares = jnp.mean(jnp.square(residual_wide), axis=-1, keepdims=True)
        normed = (residual_wide * lax.rsqrt(squares + eps_norm) * norm_gain).astype(jnp.bfloat16)
        gate_act = jnp.dot(normed, gate_weight, preferred_element_type=jnp.float32)
        up_act = jnp.dot(normed, up_weight, preferred_element_type=jnp.float32)
        hidden = (jax.nn.silu(gate_act) * up_act).astype(jnp.bfloat16)
        down_part = jnp.dot(hidden, down_weight, preferred_element_type=jnp.float32).astype(jnp.bfloat16)
        down_cols = pair_then_z_scatter(down_part)
        return (own_residual.astype(jnp.float32) + down_cols).astype(jnp.bfloat16)

    row_count = hidden_in.shape[0]
    half = row_count // 2
    out_cols = jnp.concatenate(
        [
            feed_forward(attn_rows[:half], hidden_in[:half]),
            feed_forward(attn_rows[half:], hidden_in[half:]),
        ],
        axis=0,
    )

    slot_rows = 8 * ((2 * row_count + 8 * req_count - 1) // (8 * req_count))
    owners = row_owner[:, 0]
    onehot_owner = (owners[:, None] == jnp.arange(req_count, dtype=jnp.int32)[None, :]).astype(
        jnp.int32
    )
    before = rank_within(onehot_owner, 0)
    target = owners * slot_rows + before
    placing = (
        target[None, :] == jnp.arange(req_count * slot_rows, dtype=jnp.int32)[:, None]
    ).astype(jnp.bfloat16)
    outgoing = jnp.dot(placing, out_cols, preferred_element_type=jnp.float32).astype(jnp.bfloat16)
    arrived = lax.all_to_all(outgoing, "req", split_axis=0, concat_axis=0, tiled=True)
    return lax.all_to_all(arrived, "head", split_axis=0, concat_axis=1, tiled=True)


def solution(mesh):
    placed = (
        P("req", "head"),
        P("req", "head"),
        P("req", "head"),
        P("req", "head"),
        P("req", "head"),
        P("req", "head"),
        P("req", "head"),
        P("req", None, "head"),
        P("req", None, "head"),
        P(),
        P("req"),
        P("req"),
        P("req", None),
        P("head", None),
        P(),
        P(None, "head"),
        P(None, "head"),
        P("head", None),
    )
    return jax.shard_map(
        on_device, mesh=mesh, in_specs=placed, out_specs=P(("req", "head"), None), check_vma=False
    )
```

```python
import math

import jax
import jax.numpy as jnp
from jax import lax
from jax.sharding import PartitionSpec as P

HD = 96
CAP = 48


eps_norm = 1e-05


def rank_within(onehot, axis):
    return jnp.sum((jnp.cumsum(onehot, axis=axis) - 1) * onehot, axis=-1)


def pair_then_z_scatter(x):
    rows, cols = x.shape
    n = lax.axis_size("head")
    ring = n // 2
    width = cols // n
    h = lax.axis_index("head")
    zc = h // 2
    on_first = h % 2 == 0
    even = jnp.concatenate([x[:, (2 * z) * width : (2 * z + 1) * width] for z in range(ring)], 1)
    odd = jnp.concatenate([x[:, (2 * z + 1) * width : (2 * z + 2) * width] for z in range(ring)], 1)
    mine = jnp.where(on_first, even, odd)
    other = jnp.where(on_first, odd, even)
    got = lax.ppermute(other, "head", [(i, i ^ 1) for i in range(n)])
    pair_sum = (mine.astype(jnp.float32) + got.astype(jnp.float32)).astype(jnp.bfloat16)
    acc = lax.dynamic_slice_in_dim(pair_sum, zc * width, width, 1).astype(jnp.float32)
    for d in range(1, ring):
        perm = [(i, ((i // 2 + d) % ring) * 2 + i % 2) for i in range(n)]
        piece = lax.dynamic_slice_in_dim(pair_sum, ((zc + d) % ring) * width, width, 1)
        acc = acc + lax.ppermute(piece, "head", perm).astype(jnp.float32)
    return acc


def z_then_pair_gather(y):
    rows, width = y.shape
    n = lax.axis_size("head")
    ring = n // 2
    h = lax.axis_index("head")
    zc = h // 2
    on_first = h % 2 == 0
    parts = [y]
    for d in range(1, ring):
        perm = [(i, ((i // 2 + d) % ring) * 2 + i % 2) for i in range(n)]
        parts.append(lax.ppermute(y, "head", perm))
    stacked = jnp.stack(parts, 0)
    in_order = jnp.concatenate(
        [lax.dynamic_index_in_dim(stacked, (zc - zz) % ring, 0, keepdims=False) for zz in range(ring)], 1
    )
    got = lax.ppermute(in_order, "head", [(i, i ^ 1) for i in range(n)])
    pieces = []
    for z in range(ring):
        mine_z = in_order[:, z * width : (z + 1) * width]
        got_z = got[:, z * width : (z + 1) * width]
        pieces.append(jnp.where(on_first, mine_z, got_z))
        pieces.append(jnp.where(on_first, got_z, mine_z))
    return jnp.concatenate(pieces, 1)


def on_device(
    hidden_in,
    dec_query,
    dec_key,
    dec_value,
    pre_query,
    pre_key,
    pre_value,
    cache_key,
    cache_value,
    group_of,
    cache_length,
    stretch_start,
    row_owner,
    out_weight,
    norm_gain,
    gate_weight,
    up_weight,
    down_weight,
):
    factor = 1.0 / math.sqrt(HD)
    width_here = dec_query.shape[1]
    req_count = lax.axis_size("req")
    head_count = lax.axis_size("head")
    me = lax.axis_index("req")
    groups_here = cache_key.shape[0]
    length_cache = cache_key.shape[1]
    per_home = dec_query.shape[0]
    members = group_of[:, 0]
    total_reqs = members.shape[0]

    holder_of = members // groups_here
    holder_hot = (holder_of[:, None] == jnp.arange(req_count, dtype=jnp.int32)[None, :]).astype(jnp.int32)
    rank_all = rank_within(holder_hot.reshape(req_count, per_home, req_count), 1).reshape(total_reqs)
    slot_of = (jnp.arange(total_reqs, dtype=jnp.int32) // per_home) * per_home + rank_all

    my_holder = lax.dynamic_slice_in_dim(holder_of, me * per_home, per_home)
    my_rank = lax.dynamic_slice_in_dim(rank_all, me * per_home, per_home)
    my_slot = my_holder * per_home + my_rank
    packer = (
        my_slot[None, :] == jnp.arange(req_count * per_home, dtype=jnp.int32)[:, None]
    ).astype(jnp.bfloat16)
    outgoing_q = jnp.dot(packer, dec_query, preferred_element_type=jnp.float32).astype(jnp.bfloat16)
    arrived_q = lax.all_to_all(outgoing_q, "req", split_axis=0, concat_axis=0, tiled=True)

    first_group = me * groups_here
    wanted = first_group + jnp.arange(groups_here, dtype=jnp.int32)
    belongs = (members[None, :] == wanted[:, None]).astype(jnp.int32)
    ranking = jnp.cumsum(belongs, axis=1) - 1
    places = jnp.arange(CAP, dtype=jnp.int32)
    chosen = ((belongs[:, None, :] == 1) & (ranking[:, None, :] == places[None, :, None])).reshape(
        groups_here * CAP, total_reqs
    )
    chosen_slot = jnp.sum(jnp.where(chosen, slot_of[None, :], 0), axis=1)
    chosen_any = jnp.any(chosen, axis=1)
    chooser = chosen_any[:, None] & (
        chosen_slot[:, None] == jnp.arange(req_count * per_home, dtype=jnp.int32)[None, :]
    )
    picked = jnp.dot(
        chooser.astype(jnp.bfloat16), arrived_q, preferred_element_type=jnp.float32
    ).astype(jnp.bfloat16)
    heads_here = width_here // HD
    head_mask = (jnp.arange(width_here) // HD)[None, :] == jnp.arange(heads_here)[:, None]
    positions = jnp.arange(length_cache)
    results = []
    pad_cols = 128
    for group_pos in range(groups_here):
        q_rows = picked[group_pos * CAP : (group_pos + 1) * CAP]
        q_stack = jnp.where(head_mask[:, None, :], q_rows[None], 0).reshape(heads_here * CAP, width_here)
        cache_scores = lax.dot_general(
            q_stack, cache_key[group_pos], (((1,), (1,)), ((), ())), preferred_element_type=jnp.float32
        ) * factor
        valid = (positions < cache_length[group_pos])[None, :]
        cache_scores = jnp.where(valid, cache_scores, -jnp.inf)
        highest = jnp.max(cache_scores, axis=-1, keepdims=True)
        raised = jnp.exp(cache_scores - highest)
        total = jnp.sum(raised, axis=-1, keepdims=True)
        weights = (raised / total).astype(jnp.bfloat16)
        mixed = jnp.dot(weights, cache_value[group_pos], preferred_element_type=jnp.float32)
        blended = jnp.sum(
            jnp.where(head_mask[:, None, :], mixed.reshape(heads_here, CAP, width_here), 0.0), axis=0
        )
        spread = (highest + jnp.log(total)).reshape(heads_here, CAP).T
        spread_hi = spread.astype(jnp.bfloat16)
        spread_lo = (spread - spread_hi.astype(jnp.float32)).astype(jnp.bfloat16)
        tail = jnp.zeros((CAP, pad_cols - 2 * heads_here), jnp.bfloat16)
        results.append(
            jnp.concatenate([blended.astype(jnp.bfloat16), spread_hi, spread_lo, tail], axis=1)
        )
    stacked = jnp.concatenate(results, axis=0)
    going_back = jnp.dot(
        chooser.astype(jnp.bfloat16).T, stacked, preferred_element_type=jnp.float32
    ).astype(jnp.bfloat16)
    came_back = lax.all_to_all(going_back, "req", split_axis=0, concat_axis=0, tiled=True)
    dec_back = jnp.dot(packer.T, came_back, preferred_element_type=jnp.float32)
    cache_mix = dec_back[:, :width_here]
    cache_spread = (
        dec_back[:, width_here : width_here + heads_here]
        + dec_back[:, width_here + heads_here : width_here + 2 * heads_here]
    )
    own_prod = dec_query.astype(jnp.float32) * dec_key.astype(jnp.float32)
    own_scores = jnp.sum(jnp.where(head_mask[:, None, :], own_prod[None], 0.0), axis=-1).T * factor
    top = jnp.maximum(cache_spread, own_scores)
    part_cache = jnp.exp(cache_spread - top)
    part_own = jnp.exp(own_scores - top)
    share_own = part_own / (part_cache + part_own)
    share_cols = jnp.sum(jnp.where(head_mask[:, None, :], share_own.T[:, :, None], 0.0), axis=0)
    dec_out = (
        (1.0 - share_cols) * cache_mix + share_cols * dec_value.astype(jnp.float32)
    ).astype(jnp.bfloat16)

    stretch_len = pre_query.shape[0]
    row_numbers = jnp.arange(stretch_len)
    pre_stack = jnp.where(head_mask[:, None, :], pre_query[None], 0).reshape(heads_here * stretch_len, width_here)
    dims = (((1,), (1,)), ((), ()))
    cache_part = lax.dot_general(pre_stack, cache_key[0], dims, preferred_element_type=jnp.float32) * factor
    self_part = lax.dot_general(pre_stack, pre_key, dims, preferred_element_type=jnp.float32) * factor
    cache_part = jnp.where((positions < stretch_start[0])[None, :], cache_part, -jnp.inf)
    causal = (row_numbers[None, :] <= row_numbers[:, None])[None]
    self_part = jnp.where(causal, self_part.reshape(heads_here, stretch_len, stretch_len), -jnp.inf).reshape(
        heads_here * stretch_len, stretch_len
    )
    highest = jnp.maximum(
        jnp.max(cache_part, axis=-1, keepdims=True), jnp.max(self_part, axis=-1, keepdims=True)
    )
    raised_cache = jnp.exp(cache_part - highest)
    raised_self = jnp.exp(self_part - highest)
    total = jnp.sum(raised_cache, axis=-1, keepdims=True) + jnp.sum(raised_self, axis=-1, keepdims=True)
    pre_mixed = jnp.dot(
        (raised_cache / total).astype(jnp.bfloat16), cache_value[0], preferred_element_type=jnp.float32
    ) + jnp.dot((raised_self / total).astype(jnp.bfloat16), pre_value, preferred_element_type=jnp.float32)
    pre_out = jnp.sum(
        jnp.where(head_mask[:, None, :], pre_mixed.reshape(heads_here, stretch_len, width_here), 0.0), axis=0
    ).astype(jnp.bfloat16)
    head_me = lax.axis_index("head")
    col_start = head_me * width_here

    def project(attn_chunk, hidden_chunk):
        projected = jnp.dot(attn_chunk, out_weight, preferred_element_type=jnp.float32)
        own_cols = lax.dynamic_slice_in_dim(projected, col_start, width_here, 1) + hidden_chunk.astype(
            jnp.float32
        )
        return lax.dynamic_update_slice_in_dim(projected, own_cols, col_start, 1).astype(jnp.bfloat16)

    pre_contribution = project(pre_out, hidden_in[per_home:])
    dec_out, pre_contribution = lax.optimization_barrier((dec_out, pre_contribution))
    contribution_rows = jnp.concatenate([project(dec_out, hidden_in[:per_home]), pre_contribution], axis=0)

    def feed_forward(contribution):
        own_residual = pair_then_z_scatter(contribution).astype(jnp.bfloat16)
        residual = z_then_pair_gather(own_residual)
        residual_wide = residual.astype(jnp.float32)
        squares = jnp.mean(jnp.square(residual_wide), axis=-1, keepdims=True)
        normed = (residual_wide * lax.rsqrt(squares + eps_norm) * norm_gain).astype(jnp.bfloat16)
        gate_act = jnp.dot(normed, gate_weight, preferred_element_type=jnp.float32)
        up_act = jnp.dot(normed, up_weight, preferred_element_type=jnp.float32)
        hidden = (jax.nn.silu(gate_act) * up_act).astype(jnp.bfloat16)
        down_part = jnp.dot(hidden, down_weight, preferred_element_type=jnp.float32).astype(jnp.bfloat16)
        down_cols = pair_then_z_scatter(down_part)
        return (own_residual.astype(jnp.float32) + down_cols).astype(jnp.bfloat16)

    row_count = hidden_in.shape[0]
    half = row_count // 2
    out_cols = jnp.concatenate(
        [
            feed_forward(contribution_rows[:half]),
            feed_forward(contribution_rows[half:]),
        ],
        axis=0,
    )

    slot_rows = 8 * ((2 * row_count + 8 * req_count - 1) // (8 * req_count))
    owners = row_owner[:, 0]
    onehot_owner = (owners[:, None] == jnp.arange(req_count, dtype=jnp.int32)[None, :]).astype(
        jnp.int32
    )
    before = rank_within(onehot_owner, 0)
    target = owners * slot_rows + before
    placing = (
        target[None, :] == jnp.arange(req_count * slot_rows, dtype=jnp.int32)[:, None]
    ).astype(jnp.bfloat16)
    outgoing = jnp.dot(placing, out_cols, preferred_element_type=jnp.float32).astype(jnp.bfloat16)
    arrived = lax.all_to_all(outgoing, "req", split_axis=0, concat_axis=0, tiled=True)
    return lax.all_to_all(arrived, "head", split_axis=0, concat_axis=1, tiled=True)


def solution(mesh):
    placed = (
        P("req", "head"),
        P("req", "head"),
        P("req", "head"),
        P("req", "head"),
        P("req", "head"),
        P("req", "head"),
        P("req", "head"),
        P("req", None, "head"),
        P("req", None, "head"),
        P(),
        P("req"),
        P("req"),
        P("req", None),
        P("head", None),
        P(),
        P(None, "head"),
        P(None, "head"),
        P("head", None),
    )
    return jax.shard_map(
        on_device, mesh=mesh, in_specs=placed, out_specs=P(("req", "head"), None), check_vma=False
    )
```

```python
import math

import jax
import jax.numpy as jnp
from jax import lax
from jax.sharding import PartitionSpec as P

HD = 96
CAP = 48


eps_norm = 1e-05


def rank_within(onehot, axis):
    return jnp.sum((jnp.cumsum(onehot, axis=axis) - 1) * onehot, axis=-1)


def pair_then_z_scatter(x):
    rows, cols = x.shape
    n = lax.axis_size("head")
    ring = n // 2
    width = cols // n
    h = lax.axis_index("head")
    zc = h // 2
    on_first = h % 2 == 0
    even = jnp.concatenate([x[:, (2 * z) * width : (2 * z + 1) * width] for z in range(ring)], 1)
    odd = jnp.concatenate([x[:, (2 * z + 1) * width : (2 * z + 2) * width] for z in range(ring)], 1)
    mine = jnp.where(on_first, even, odd)
    other = jnp.where(on_first, odd, even)
    got = lax.ppermute(other, "head", [(i, i ^ 1) for i in range(n)])
    pair_sum = (mine.astype(jnp.float32) + got.astype(jnp.float32)).astype(jnp.bfloat16)
    acc = lax.dynamic_slice_in_dim(pair_sum, zc * width, width, 1).astype(jnp.float32)
    for d in range(1, ring):
        perm = [(i, ((i // 2 + d) % ring) * 2 + i % 2) for i in range(n)]
        piece = lax.dynamic_slice_in_dim(pair_sum, ((zc + d) % ring) * width, width, 1)
        acc = acc + lax.ppermute(piece, "head", perm).astype(jnp.float32)
    return acc


def z_then_pair_gather(y):
    rows, width = y.shape
    n = lax.axis_size("head")
    ring = n // 2
    h = lax.axis_index("head")
    zc = h // 2
    on_first = h % 2 == 0
    parts = [y]
    for d in range(1, ring):
        perm = [(i, ((i // 2 + d) % ring) * 2 + i % 2) for i in range(n)]
        parts.append(lax.ppermute(y, "head", perm))
    stacked = jnp.stack(parts, 0)
    in_order = jnp.concatenate(
        [lax.dynamic_index_in_dim(stacked, (zc - zz) % ring, 0, keepdims=False) for zz in range(ring)], 1
    )
    got = lax.ppermute(in_order, "head", [(i, i ^ 1) for i in range(n)])
    pieces = []
    for z in range(ring):
        mine_z = in_order[:, z * width : (z + 1) * width]
        got_z = got[:, z * width : (z + 1) * width]
        pieces.append(jnp.where(on_first, mine_z, got_z))
        pieces.append(jnp.where(on_first, got_z, mine_z))
    return jnp.concatenate(pieces, 1)


def on_device(
    hidden_in,
    dec_query,
    dec_key,
    dec_value,
    pre_query,
    pre_key,
    pre_value,
    cache_key,
    cache_value,
    group_of,
    cache_length,
    stretch_start,
    row_owner,
    out_weight,
    norm_gain,
    gate_weight,
    up_weight,
    down_weight,
):
    factor = 1.0 / math.sqrt(HD)
    width_here = dec_query.shape[1]
    req_count = lax.axis_size("req")
    head_count = lax.axis_size("head")
    me = lax.axis_index("req")
    groups_here = cache_key.shape[0]
    length_cache = cache_key.shape[1]
    per_home = dec_query.shape[0]
    members = group_of[:, 0]
    total_reqs = members.shape[0]

    holder_of = members // groups_here
    holder_hot = (holder_of[:, None] == jnp.arange(req_count, dtype=jnp.int32)[None, :]).astype(jnp.int32)
    rank_all = rank_within(holder_hot.reshape(req_count, per_home, req_count), 1).reshape(total_reqs)
    slot_of = (jnp.arange(total_reqs, dtype=jnp.int32) // per_home) * per_home + rank_all

    my_holder = lax.dynamic_slice_in_dim(holder_of, me * per_home, per_home)
    my_rank = lax.dynamic_slice_in_dim(rank_all, me * per_home, per_home)
    my_slot = my_holder * per_home + my_rank
    packer = (
        my_slot[None, :] == jnp.arange(req_count * per_home, dtype=jnp.int32)[:, None]
    ).astype(jnp.bfloat16)
    outgoing_q = jnp.dot(packer, dec_query, preferred_element_type=jnp.float32).astype(jnp.bfloat16)
    arrived_q = lax.all_to_all(outgoing_q, "req", split_axis=0, concat_axis=0, tiled=True)

    first_group = me * groups_here
    wanted = first_group + jnp.arange(groups_here, dtype=jnp.int32)
    belongs = (members[None, :] == wanted[:, None]).astype(jnp.int32)
    ranking = jnp.cumsum(belongs, axis=1) - 1
    places = jnp.arange(CAP, dtype=jnp.int32)
    chosen = ((belongs[:, None, :] == 1) & (ranking[:, None, :] == places[None, :, None])).reshape(
        groups_here * CAP, total_reqs
    )
    chosen_slot = jnp.sum(jnp.where(chosen, slot_of[None, :], 0), axis=1)
    chosen_any = jnp.any(chosen, axis=1)
    chooser = chosen_any[:, None] & (
        chosen_slot[:, None] == jnp.arange(req_count * per_home, dtype=jnp.int32)[None, :]
    )
    picked = jnp.dot(
        chooser.astype(jnp.bfloat16), arrived_q, preferred_element_type=jnp.float32
    ).astype(jnp.bfloat16)
    heads_here = width_here // HD
    head_mask = (jnp.arange(width_here) // HD)[None, :] == jnp.arange(heads_here)[:, None]
    positions = jnp.arange(length_cache)
    results = []
    pad_cols = 128
    for group_pos in range(groups_here):
        q_rows = picked[group_pos * CAP : (group_pos + 1) * CAP]
        q_stack = jnp.where(head_mask[:, None, :], q_rows[None], 0).reshape(heads_here * CAP, width_here)
        cache_scores = lax.dot_general(
            q_stack, cache_key[group_pos], (((1,), (1,)), ((), ())), preferred_element_type=jnp.float32
        ) * factor
        valid = (positions < cache_length[group_pos])[None, :]
        cache_scores = jnp.where(valid, cache_scores, -jnp.inf)
        highest = jnp.max(cache_scores, axis=-1, keepdims=True)
        raised = jnp.exp(cache_scores - highest)
        total = jnp.sum(raised, axis=-1, keepdims=True)
        weights = (raised / total).astype(jnp.bfloat16)
        mixed = jnp.dot(weights, cache_value[group_pos], preferred_element_type=jnp.float32)
        blended = jnp.sum(
            jnp.where(head_mask[:, None, :], mixed.reshape(heads_here, CAP, width_here), 0.0), axis=0
        )
        spread = (highest + jnp.log(total)).reshape(heads_here, CAP).T
        spread_hi = spread.astype(jnp.bfloat16)
        spread_lo = (spread - spread_hi.astype(jnp.float32)).astype(jnp.bfloat16)
        tail = jnp.zeros((CAP, pad_cols - 2 * heads_here), jnp.bfloat16)
        results.append(
            jnp.concatenate([blended.astype(jnp.bfloat16), spread_hi, spread_lo, tail], axis=1)
        )
    stacked = jnp.concatenate(results, axis=0)
    going_back = jnp.dot(
        chooser.astype(jnp.bfloat16).T, stacked, preferred_element_type=jnp.float32
    ).astype(jnp.bfloat16)
    came_back = lax.all_to_all(going_back, "req", split_axis=0, concat_axis=0, tiled=True)
    dec_back = jnp.dot(packer.T, came_back, preferred_element_type=jnp.float32)
    cache_mix = dec_back[:, :width_here]
    cache_spread = (
        dec_back[:, width_here : width_here + heads_here]
        + dec_back[:, width_here + heads_here : width_here + 2 * heads_here]
    )
    own_prod = dec_query.astype(jnp.float32) * dec_key.astype(jnp.float32)
    own_scores = jnp.sum(jnp.where(head_mask[:, None, :], own_prod[None], 0.0), axis=-1).T * factor
    top = jnp.maximum(cache_spread, own_scores)
    part_cache = jnp.exp(cache_spread - top)
    part_own = jnp.exp(own_scores - top)
    share_own = part_own / (part_cache + part_own)
    share_cols = jnp.sum(jnp.where(head_mask[:, None, :], share_own.T[:, :, None], 0.0), axis=0)
    dec_out = (
        (1.0 - share_cols) * cache_mix + share_cols * dec_value.astype(jnp.float32)
    ).astype(jnp.bfloat16)

    stretch_len = pre_query.shape[0]
    row_numbers = jnp.arange(stretch_len)
    pre_stack = jnp.where(head_mask[:, None, :], pre_query[None], 0).reshape(heads_here * stretch_len, width_here)
    dims = (((1,), (1,)), ((), ()))
    cache_part = lax.dot_general(pre_stack, cache_key[0], dims, preferred_element_type=jnp.float32) * factor
    self_part = lax.dot_general(pre_stack, pre_key, dims, preferred_element_type=jnp.float32) * factor
    cache_part = jnp.where((positions < stretch_start[0])[None, :], cache_part, -jnp.inf)
    causal = (row_numbers[None, :] <= row_numbers[:, None])[None]
    self_part = jnp.where(causal, self_part.reshape(heads_here, stretch_len, stretch_len), -jnp.inf).reshape(
        heads_here * stretch_len, stretch_len
    )
    highest = jnp.maximum(
        jnp.max(cache_part, axis=-1, keepdims=True), jnp.max(self_part, axis=-1, keepdims=True)
    )
    raised_cache = jnp.exp(cache_part - highest)
    raised_self = jnp.exp(self_part - highest)
    total = jnp.sum(raised_cache, axis=-1, keepdims=True) + jnp.sum(raised_self, axis=-1, keepdims=True)
    pre_mixed = jnp.dot(
        (raised_cache / total).astype(jnp.bfloat16), cache_value[0], preferred_element_type=jnp.float32
    ) + jnp.dot((raised_self / total).astype(jnp.bfloat16), pre_value, preferred_element_type=jnp.float32)
    pre_out = jnp.sum(
        jnp.where(head_mask[:, None, :], pre_mixed.reshape(heads_here, stretch_len, width_here), 0.0), axis=0
    ).astype(jnp.bfloat16)
    head_me = lax.axis_index("head")
    col_start = head_me * width_here

    def project(attn_chunk, hidden_chunk):
        projected = jnp.dot(attn_chunk, out_weight, preferred_element_type=jnp.float32)
        own_cols = lax.dynamic_slice_in_dim(projected, col_start, width_here, 1) + hidden_chunk.astype(
            jnp.float32
        )
        return lax.dynamic_update_slice_in_dim(projected, own_cols, col_start, 1).astype(jnp.bfloat16)

    pre_contribution = project(pre_out, hidden_in[per_home:])
    row_count = hidden_in.shape[0]
    half = row_count // 2
    late_rows, _ = lax.optimization_barrier((pre_contribution[half - per_home :], arrived_q))
    dec_out, early_rows = lax.optimization_barrier((dec_out, pre_contribution[: half - per_home]))
    first_rows = jnp.concatenate([project(dec_out, hidden_in[:per_home]), early_rows], axis=0)

    def feed_forward(contribution):
        own_residual = pair_then_z_scatter(contribution).astype(jnp.bfloat16)
        residual = z_then_pair_gather(own_residual)
        residual_wide = residual.astype(jnp.float32)
        squares = jnp.mean(jnp.square(residual_wide), axis=-1, keepdims=True)
        normed = (residual_wide * lax.rsqrt(squares + eps_norm) * norm_gain).astype(jnp.bfloat16)
        gate_act = jnp.dot(normed, gate_weight, preferred_element_type=jnp.float32)
        up_act = jnp.dot(normed, up_weight, preferred_element_type=jnp.float32)
        hidden = (jax.nn.silu(gate_act) * up_act).astype(jnp.bfloat16)
        down_part = jnp.dot(hidden, down_weight, preferred_element_type=jnp.float32).astype(jnp.bfloat16)
        down_cols = pair_then_z_scatter(down_part)
        return (own_residual.astype(jnp.float32) + down_cols).astype(jnp.bfloat16)

    out_cols = jnp.concatenate(
        [
            feed_forward(first_rows),
            feed_forward(late_rows),
        ],
        axis=0,
    )

    slot_rows = 8 * ((2 * row_count + 8 * req_count - 1) // (8 * req_count))
    owners = row_owner[:, 0]
    onehot_owner = (owners[:, None] == jnp.arange(req_count, dtype=jnp.int32)[None, :]).astype(
        jnp.int32
    )
    before = rank_within(onehot_owner, 0)
    target = owners * slot_rows + before
    placing = (
        target[None, :] == jnp.arange(req_count * slot_rows, dtype=jnp.int32)[:, None]
    ).astype(jnp.bfloat16)
    outgoing = jnp.dot(placing, out_cols, preferred_element_type=jnp.float32).astype(jnp.bfloat16)
    arrived = lax.all_to_all(outgoing, "req", split_axis=0, concat_axis=0, tiled=True)
    return lax.all_to_all(arrived, "head", split_axis=0, concat_axis=1, tiled=True)


def solution(mesh):
    placed = (
        P("req", "head"),
        P("req", "head"),
        P("req", "head"),
        P("req", "head"),
        P("req", "head"),
        P("req", "head"),
        P("req", "head"),
        P("req", None, "head"),
        P("req", None, "head"),
        P(),
        P("req"),
        P("req"),
        P("req", None),
        P("head", None),
        P(),
        P(None, "head"),
        P(None, "head"),
        P("head", None),
    )
    return jax.shard_map(
        on_device, mesh=mesh, in_specs=placed, out_specs=P(("req", "head"), None), check_vma=False
    )
```

```python
import math

import jax
import jax.numpy as jnp
from jax import lax
from jax.sharding import PartitionSpec as P

HD = 96
CAP = 48


eps_norm = 1e-05


def rank_within(onehot, axis):
    return jnp.sum((jnp.cumsum(onehot, axis=axis) - 1) * onehot, axis=-1)


def pair_then_z_scatter(x):
    rows, cols = x.shape
    n = lax.axis_size("head")
    ring = n // 2
    width = cols // n
    half = cols // 2
    h = lax.axis_index("head")
    zc = h // 2
    on_first = h % 2 == 0
    mine = jnp.where(on_first, x[:, :half], x[:, half:])
    other = jnp.where(on_first, x[:, half:], x[:, :half])
    got = lax.ppermute(other, "head", [(i, i ^ 1) for i in range(n)])
    pair_sum = (mine.astype(jnp.float32) + got.astype(jnp.float32)).astype(jnp.bfloat16)
    acc = lax.dynamic_slice_in_dim(pair_sum, zc * width, width, 1).astype(jnp.float32)
    for d in range(1, ring):
        perm = [(i, ((i // 2 + d) % ring) * 2 + i % 2) for i in range(n)]
        piece = lax.dynamic_slice_in_dim(pair_sum, ((zc + d) % ring) * width, width, 1)
        acc = acc + lax.ppermute(piece, "head", perm).astype(jnp.float32)
    return acc


def z_then_pair_gather(y):
    rows, width = y.shape
    n = lax.axis_size("head")
    ring = n // 2
    h = lax.axis_index("head")
    zc = h // 2
    on_first = h % 2 == 0
    parts = [y]
    for d in range(1, ring):
        perm = [(i, ((i // 2 + d) % ring) * 2 + i % 2) for i in range(n)]
        parts.append(lax.ppermute(y, "head", perm))
    stacked = jnp.stack(parts, 0)
    in_order = jnp.concatenate(
        [lax.dynamic_index_in_dim(stacked, (zc - zz) % ring, 0, keepdims=False) for zz in range(ring)], 1
    )
    got = lax.ppermute(in_order, "head", [(i, i ^ 1) for i in range(n)])
    return jnp.where(
        on_first, jnp.concatenate([in_order, got], 1), jnp.concatenate([got, in_order], 1)
    )


def on_device(
    hidden_in,
    dec_query,
    dec_key,
    dec_value,
    pre_query,
    pre_key,
    pre_value,
    cache_key,
    cache_value,
    group_of,
    cache_length,
    stretch_start,
    row_owner,
    out_weight,
    norm_gain,
    gate_weight,
    up_weight,
    down_weight,
):
    factor = 1.0 / math.sqrt(HD)
    width_here = dec_query.shape[1]
    req_count = lax.axis_size("req")
    head_count = lax.axis_size("head")
    me = lax.axis_index("req")
    groups_here = cache_key.shape[0]
    length_cache = cache_key.shape[1]
    per_home = dec_query.shape[0]
    members = group_of[:, 0]
    total_reqs = members.shape[0]

    holder_of = members // groups_here
    holder_hot = (holder_of[:, None] == jnp.arange(req_count, dtype=jnp.int32)[None, :]).astype(jnp.int32)
    rank_all = rank_within(holder_hot.reshape(req_count, per_home, req_count), 1).reshape(total_reqs)
    slot_of = (jnp.arange(total_reqs, dtype=jnp.int32) // per_home) * per_home + rank_all

    my_holder = lax.dynamic_slice_in_dim(holder_of, me * per_home, per_home)
    my_rank = lax.dynamic_slice_in_dim(rank_all, me * per_home, per_home)
    my_slot = my_holder * per_home + my_rank
    packer = (
        my_slot[None, :] == jnp.arange(req_count * per_home, dtype=jnp.int32)[:, None]
    ).astype(jnp.bfloat16)
    outgoing_q = jnp.dot(packer, dec_query, preferred_element_type=jnp.float32).astype(jnp.bfloat16)
    arrived_q = lax.all_to_all(outgoing_q, "req", split_axis=0, concat_axis=0, tiled=True)

    first_group = me * groups_here
    wanted = first_group + jnp.arange(groups_here, dtype=jnp.int32)
    belongs = (members[None, :] == wanted[:, None]).astype(jnp.int32)
    ranking = jnp.cumsum(belongs, axis=1) - 1
    places = jnp.arange(CAP, dtype=jnp.int32)
    chosen = ((belongs[:, None, :] == 1) & (ranking[:, None, :] == places[None, :, None])).reshape(
        groups_here * CAP, total_reqs
    )
    chosen_slot = jnp.sum(jnp.where(chosen, slot_of[None, :], 0), axis=1)
    chosen_any = jnp.any(chosen, axis=1)
    chooser = chosen_any[:, None] & (
        chosen_slot[:, None] == jnp.arange(req_count * per_home, dtype=jnp.int32)[None, :]
    )
    picked = jnp.dot(
        chooser.astype(jnp.bfloat16), arrived_q, preferred_element_type=jnp.float32
    ).astype(jnp.bfloat16)
    heads_here = width_here // HD
    head_mask = (jnp.arange(width_here) // HD)[None, :] == jnp.arange(heads_here)[:, None]
    positions = jnp.arange(length_cache)
    results = []
    pad_cols = 128
    for group_pos in range(groups_here):
        q_rows = picked[group_pos * CAP : (group_pos + 1) * CAP]
        q_stack = jnp.where(head_mask[:, None, :], q_rows[None], 0).reshape(heads_here * CAP, width_here)
        cache_scores = lax.dot_general(
            q_stack, cache_key[group_pos], (((1,), (1,)), ((), ())), preferred_element_type=jnp.float32
        ) * factor
        valid = (positions < cache_length[group_pos])[None, :]
        cache_scores = jnp.where(valid, cache_scores, -jnp.inf)
        highest = jnp.max(cache_scores, axis=-1, keepdims=True)
        raised = jnp.exp(cache_scores - highest)
        total = jnp.sum(raised, axis=-1, keepdims=True)
        weights = (raised / total).astype(jnp.bfloat16)
        mixed = jnp.dot(weights, cache_value[group_pos], preferred_element_type=jnp.float32)
        blended = jnp.sum(
            jnp.where(head_mask[:, None, :], mixed.reshape(heads_here, CAP, width_here), 0.0), axis=0
        )
        spread = (highest + jnp.log(total)).reshape(heads_here, CAP).T
        spread_hi = spread.astype(jnp.bfloat16)
        spread_lo = (spread - spread_hi.astype(jnp.float32)).astype(jnp.bfloat16)
        tail = jnp.zeros((CAP, pad_cols - 2 * heads_here), jnp.bfloat16)
        results.append(
            jnp.concatenate([blended.astype(jnp.bfloat16), spread_hi, spread_lo, tail], axis=1)
        )
    stacked = jnp.concatenate(results, axis=0)
    going_back = jnp.dot(
        chooser.astype(jnp.bfloat16).T, stacked, preferred_element_type=jnp.float32
    ).astype(jnp.bfloat16)
    came_back = lax.all_to_all(going_back, "req", split_axis=0, concat_axis=0, tiled=True)
    dec_back = jnp.dot(packer.T, came_back, preferred_element_type=jnp.float32)
    cache_mix = dec_back[:, :width_here]
    cache_spread = (
        dec_back[:, width_here : width_here + heads_here]
        + dec_back[:, width_here + heads_here : width_here + 2 * heads_here]
    )
    own_prod = dec_query.astype(jnp.float32) * dec_key.astype(jnp.float32)
    own_scores = jnp.sum(jnp.where(head_mask[:, None, :], own_prod[None], 0.0), axis=-1).T * factor
    top = jnp.maximum(cache_spread, own_scores)
    part_cache = jnp.exp(cache_spread - top)
    part_own = jnp.exp(own_scores - top)
    share_own = part_own / (part_cache + part_own)
    share_cols = jnp.sum(jnp.where(head_mask[:, None, :], share_own.T[:, :, None], 0.0), axis=0)
    dec_out = (
        (1.0 - share_cols) * cache_mix + share_cols * dec_value.astype(jnp.float32)
    ).astype(jnp.bfloat16)

    stretch_len = pre_query.shape[0]
    row_numbers = jnp.arange(stretch_len)
    pre_stack = jnp.where(head_mask[:, None, :], pre_query[None], 0).reshape(heads_here * stretch_len, width_here)
    dims = (((1,), (1,)), ((), ()))
    cache_part = lax.dot_general(pre_stack, cache_key[0], dims, preferred_element_type=jnp.float32) * factor
    self_part = lax.dot_general(pre_stack, pre_key, dims, preferred_element_type=jnp.float32) * factor
    cache_part = jnp.where((positions < stretch_start[0])[None, :], cache_part, -jnp.inf)
    causal = (row_numbers[None, :] <= row_numbers[:, None])[None]
    self_part = jnp.where(causal, self_part.reshape(heads_here, stretch_len, stretch_len), -jnp.inf).reshape(
        heads_here * stretch_len, stretch_len
    )
    highest = jnp.maximum(
        jnp.max(cache_part, axis=-1, keepdims=True), jnp.max(self_part, axis=-1, keepdims=True)
    )
    raised_cache = jnp.exp(cache_part - highest)
    raised_self = jnp.exp(self_part - highest)
    total = jnp.sum(raised_cache, axis=-1, keepdims=True) + jnp.sum(raised_self, axis=-1, keepdims=True)
    pre_mixed = jnp.dot(
        (raised_cache / total).astype(jnp.bfloat16), cache_value[0], preferred_element_type=jnp.float32
    ) + jnp.dot((raised_self / total).astype(jnp.bfloat16), pre_value, preferred_element_type=jnp.float32)
    pre_out = jnp.sum(
        jnp.where(head_mask[:, None, :], pre_mixed.reshape(heads_here, stretch_len, width_here), 0.0), axis=0
    ).astype(jnp.bfloat16)
    dec_out, pre_out = lax.optimization_barrier((dec_out, pre_out))
    attn_rows = jnp.concatenate([dec_out, pre_out], axis=0)
    head_me = lax.axis_index("head")
    col_start = head_me * width_here

    def feed_forward(attn_chunk, hidden_chunk):
        projected = jnp.dot(attn_chunk, out_weight, preferred_element_type=jnp.float32)
        own_cols = lax.dynamic_slice_in_dim(projected, col_start, width_here, 1) + hidden_chunk.astype(
            jnp.float32
        )
        contribution = lax.dynamic_update_slice_in_dim(projected, own_cols, col_start, 1)
        own_residual = pair_then_z_scatter(contribution.astype(jnp.bfloat16)).astype(jnp.bfloat16)
        residual = z_then_pair_gather(own_residual)
        residual_wide = residual.astype(jnp.float32)
        squares = jnp.mean(jnp.square(residual_wide), axis=-1, keepdims=True)
        normed = (residual_wide * lax.rsqrt(squares + eps_norm) * norm_gain).astype(jnp.bfloat16)
        gate_act = jnp.dot(normed, gate_weight, preferred_element_type=jnp.float32)
        up_act = jnp.dot(normed, up_weight, preferred_element_type=jnp.float32)
        hidden = (jax.nn.silu(gate_act) * up_act).astype(jnp.bfloat16)
        down_part = jnp.dot(hidden, down_weight, preferred_element_type=jnp.float32).astype(jnp.bfloat16)
        down_cols = pair_then_z_scatter(down_part)
        return (own_residual.astype(jnp.float32) + down_cols).astype(jnp.bfloat16)

    row_count = hidden_in.shape[0]
    half = row_count // 2
    out_cols = jnp.concatenate(
        [
            feed_forward(attn_rows[:half], hidden_in[:half]),
            feed_forward(attn_rows[half:], hidden_in[half:]),
        ],
        axis=0,
    )

    slot_rows = 8 * ((2 * row_count + 8 * req_count - 1) // (8 * req_count))
    owners = row_owner[:, 0]
    onehot_owner = (owners[:, None] == jnp.arange(req_count, dtype=jnp.int32)[None, :]).astype(
        jnp.int32
    )
    before = rank_within(onehot_owner, 0)
    target = owners * slot_rows + before
    placing = (
        target[None, :] == jnp.arange(req_count * slot_rows, dtype=jnp.int32)[:, None]
    ).astype(jnp.bfloat16)
    outgoing = jnp.dot(placing, out_cols, preferred_element_type=jnp.float32).astype(jnp.bfloat16)
    arrived = lax.all_to_all(outgoing, "req", split_axis=0, concat_axis=0, tiled=True)
    routed = lax.all_to_all(arrived, "head", split_axis=0, concat_axis=1, tiled=True)
    ring = head_count // 2
    return jnp.concatenate(
        [
            routed[:, ((b % ring) * 2 + b // ring) * width_here : ((b % ring) * 2 + b // ring + 1) * width_here]
            for b in range(head_count)
        ],
        axis=1,
    )


def solution(mesh):
    placed = (
        P("req", "head"),
        P("req", "head"),
        P("req", "head"),
        P("req", "head"),
        P("req", "head"),
        P("req", "head"),
        P("req", "head"),
        P("req", None, "head"),
        P("req", None, "head"),
        P(),
        P("req"),
        P("req"),
        P("req", None),
        P("head", None),
        P(),
        P(None, "head"),
        P(None, "head"),
        P("head", None),
    )
    return jax.shard_map(
        on_device, mesh=mesh, in_specs=placed, out_specs=P(("req", "head"), None), check_vma=False
    )
```

```python
import math

import jax
import jax.numpy as jnp
from jax import lax
from jax.sharding import PartitionSpec as P

HD = 96
CAP = 48


eps_norm = 1e-05


def rank_within(onehot, axis):
    return jnp.sum((jnp.cumsum(onehot, axis=axis) - 1) * onehot, axis=-1)


def pair_then_z_scatter(x):
    rows, cols = x.shape
    n = lax.axis_size("head")
    ring = n // 2
    width = cols // n
    half = cols // 2
    h = lax.axis_index("head")
    zc = h // 2
    on_first = h % 2 == 0
    mine = jnp.where(on_first, x[:, :half], x[:, half:])
    other = jnp.where(on_first, x[:, half:], x[:, :half])
    got = lax.ppermute(other, "head", [(i, i ^ 1) for i in range(n)])
    pair_sum = (mine.astype(jnp.float32) + got.astype(jnp.float32)).astype(jnp.bfloat16)
    acc = lax.dynamic_slice_in_dim(pair_sum, zc * width, width, 1).astype(jnp.float32)
    for d in range(1, ring):
        perm = [(i, ((i // 2 + d) % ring) * 2 + i % 2) for i in range(n)]
        piece = lax.dynamic_slice_in_dim(pair_sum, ((zc + d) % ring) * width, width, 1)
        acc = acc + lax.ppermute(piece, "head", perm).astype(jnp.float32)
    return acc


def z_then_pair_gather(y):
    rows, width = y.shape
    n = lax.axis_size("head")
    ring = n // 2
    h = lax.axis_index("head")
    zc = h // 2
    on_first = h % 2 == 0
    parts = [y]
    for d in range(1, ring):
        perm = [(i, ((i // 2 + d) % ring) * 2 + i % 2) for i in range(n)]
        parts.append(lax.ppermute(y, "head", perm))
    stacked = jnp.stack(parts, 0)
    in_order = jnp.concatenate(
        [lax.dynamic_index_in_dim(stacked, (zc - zz) % ring, 0, keepdims=False) for zz in range(ring)], 1
    )
    got = lax.ppermute(in_order, "head", [(i, i ^ 1) for i in range(n)])
    return jnp.where(
        on_first, jnp.concatenate([in_order, got], 1), jnp.concatenate([got, in_order], 1)
    )


def on_device(
    hidden_in,
    dec_query,
    dec_key,
    dec_value,
    pre_query,
    pre_key,
    pre_value,
    cache_key,
    cache_value,
    group_of,
    cache_length,
    stretch_start,
    row_owner,
    out_weight,
    norm_gain,
    gate_weight,
    up_weight,
    down_weight,
):
    factor = 1.0 / math.sqrt(HD)
    width_here = dec_query.shape[1]
    req_count = lax.axis_size("req")
    head_count = lax.axis_size("head")
    me = lax.axis_index("req")
    groups_here = cache_key.shape[0]
    length_cache = cache_key.shape[1]
    per_home = dec_query.shape[0]
    members = group_of[:, 0]
    total_reqs = members.shape[0]

    holder_of = members // groups_here
    holder_hot = (holder_of[:, None] == jnp.arange(req_count, dtype=jnp.int32)[None, :]).astype(jnp.int32)
    rank_all = rank_within(holder_hot.reshape(req_count, per_home, req_count), 1).reshape(total_reqs)
    slot_of = (jnp.arange(total_reqs, dtype=jnp.int32) // per_home) * per_home + rank_all

    my_holder = lax.dynamic_slice_in_dim(holder_of, me * per_home, per_home)
    my_rank = lax.dynamic_slice_in_dim(rank_all, me * per_home, per_home)
    my_slot = my_holder * per_home + my_rank
    packer = (
        my_slot[None, :] == jnp.arange(req_count * per_home, dtype=jnp.int32)[:, None]
    ).astype(jnp.bfloat16)
    outgoing_q = jnp.dot(packer, dec_query, preferred_element_type=jnp.float32).astype(jnp.bfloat16)
    arrived_q = lax.all_to_all(outgoing_q, "req", split_axis=0, concat_axis=0, tiled=True)

    first_group = me * groups_here
    wanted = first_group + jnp.arange(groups_here, dtype=jnp.int32)
    belongs = (members[None, :] == wanted[:, None]).astype(jnp.int32)
    ranking = jnp.cumsum(belongs, axis=1) - 1
    places = jnp.arange(CAP, dtype=jnp.int32)
    chosen = ((belongs[:, None, :] == 1) & (ranking[:, None, :] == places[None, :, None])).reshape(
        groups_here * CAP, total_reqs
    )
    chosen_slot = jnp.sum(jnp.where(chosen, slot_of[None, :], 0), axis=1)
    chosen_any = jnp.any(chosen, axis=1)
    chooser = chosen_any[:, None] & (
        chosen_slot[:, None] == jnp.arange(req_count * per_home, dtype=jnp.int32)[None, :]
    )
    picked = jnp.dot(
        chooser.astype(jnp.bfloat16), arrived_q, preferred_element_type=jnp.float32
    ).astype(jnp.bfloat16)
    heads_here = width_here // HD
    head_mask = (jnp.arange(width_here) // HD)[None, :] == jnp.arange(heads_here)[:, None]
    positions = jnp.arange(length_cache)
    results = []
    pad_cols = 128
    for group_pos in range(groups_here):
        q_rows = picked[group_pos * CAP : (group_pos + 1) * CAP]
        q_stack = jnp.where(head_mask[:, None, :], q_rows[None], 0).reshape(heads_here * CAP, width_here)
        cache_scores = lax.dot_general(
            q_stack, cache_key[group_pos], (((1,), (1,)), ((), ())), preferred_element_type=jnp.float32
        ) * factor
        valid = (positions < cache_length[group_pos])[None, :]
        cache_scores = jnp.where(valid, cache_scores, -jnp.inf)
        highest = jnp.max(cache_scores, axis=-1, keepdims=True)
        raised = jnp.exp(cache_scores - highest)
        total = jnp.sum(raised, axis=-1, keepdims=True)
        weights = (raised / total).astype(jnp.bfloat16)
        mixed = jnp.dot(weights, cache_value[group_pos], preferred_element_type=jnp.float32)
        blended = jnp.sum(
            jnp.where(head_mask[:, None, :], mixed.reshape(heads_here, CAP, width_here), 0.0), axis=0
        )
        spread = (highest + jnp.log(total)).reshape(heads_here, CAP).T
        spread_hi = spread.astype(jnp.bfloat16)
        spread_lo = (spread - spread_hi.astype(jnp.float32)).astype(jnp.bfloat16)
        tail = jnp.zeros((CAP, pad_cols - 2 * heads_here), jnp.bfloat16)
        results.append(
            jnp.concatenate([blended.astype(jnp.bfloat16), spread_hi, spread_lo, tail], axis=1)
        )
    stacked = jnp.concatenate(results, axis=0)
    going_back = jnp.dot(
        chooser.astype(jnp.bfloat16).T, stacked, preferred_element_type=jnp.float32
    ).astype(jnp.bfloat16)
    came_back = lax.all_to_all(going_back, "req", split_axis=0, concat_axis=0, tiled=True)
    dec_back = jnp.dot(packer.T, came_back, preferred_element_type=jnp.float32)
    cache_mix = dec_back[:, :width_here]
    cache_spread = (
        dec_back[:, width_here : width_here + heads_here]
        + dec_back[:, width_here + heads_here : width_here + 2 * heads_here]
    )
    own_prod = dec_query.astype(jnp.float32) * dec_key.astype(jnp.float32)
    own_scores = jnp.sum(jnp.where(head_mask[:, None, :], own_prod[None], 0.0), axis=-1).T * factor
    top = jnp.maximum(cache_spread, own_scores)
    part_cache = jnp.exp(cache_spread - top)
    part_own = jnp.exp(own_scores - top)
    share_own = part_own / (part_cache + part_own)
    share_cols = jnp.sum(jnp.where(head_mask[:, None, :], share_own.T[:, :, None], 0.0), axis=0)
    dec_out = (
        (1.0 - share_cols) * cache_mix + share_cols * dec_value.astype(jnp.float32)
    ).astype(jnp.bfloat16)

    stretch_len = pre_query.shape[0]
    row_numbers = jnp.arange(stretch_len)
    pre_stack = jnp.where(head_mask[:, None, :], pre_query[None], 0).reshape(heads_here * stretch_len, width_here)
    dims = (((1,), (1,)), ((), ()))
    cache_part = lax.dot_general(pre_stack, cache_key[0], dims, preferred_element_type=jnp.float32) * factor
    self_part = lax.dot_general(pre_stack, pre_key, dims, preferred_element_type=jnp.float32) * factor
    cache_part = jnp.where((positions < stretch_start[0])[None, :], cache_part, -jnp.inf)
    causal = (row_numbers[None, :] <= row_numbers[:, None])[None]
    self_part = jnp.where(causal, self_part.reshape(heads_here, stretch_len, stretch_len), -jnp.inf).reshape(
        heads_here * stretch_len, stretch_len
    )
    highest = jnp.maximum(
        jnp.max(cache_part, axis=-1, keepdims=True), jnp.max(self_part, axis=-1, keepdims=True)
    )
    raised_cache = jnp.exp(cache_part - highest)
    raised_self = jnp.exp(self_part - highest)
    total = jnp.sum(raised_cache, axis=-1, keepdims=True) + jnp.sum(raised_self, axis=-1, keepdims=True)
    pre_mixed = jnp.dot(
        (raised_cache / total).astype(jnp.bfloat16), cache_value[0], preferred_element_type=jnp.float32
    ) + jnp.dot((raised_self / total).astype(jnp.bfloat16), pre_value, preferred_element_type=jnp.float32)
    pre_out = jnp.sum(
        jnp.where(head_mask[:, None, :], pre_mixed.reshape(heads_here, stretch_len, width_here), 0.0), axis=0
    ).astype(jnp.bfloat16)
    dec_out, pre_out = lax.optimization_barrier((dec_out, pre_out))
    attn_rows = jnp.concatenate([dec_out, pre_out], axis=0)
    head_me = lax.axis_index("head")
    col_start = head_me * width_here

    def feed_forward(attn_chunk, hidden_chunk):
        projected = jnp.dot(attn_chunk, out_weight, preferred_element_type=jnp.float32)
        own_cols = lax.dynamic_slice_in_dim(projected, col_start, width_here, 1) + hidden_chunk.astype(
            jnp.float32
        )
        contribution = lax.dynamic_update_slice_in_dim(projected, own_cols, col_start, 1)
        own_residual = pair_then_z_scatter(contribution.astype(jnp.bfloat16)).astype(jnp.bfloat16)
        residual = z_then_pair_gather(own_residual)
        residual_wide = residual.astype(jnp.float32)
        squares = jnp.mean(jnp.square(residual_wide), axis=-1, keepdims=True)
        normed = (residual_wide * lax.rsqrt(squares + eps_norm) * norm_gain).astype(jnp.bfloat16)
        gate_act = jnp.dot(normed, gate_weight, preferred_element_type=jnp.float32)
        up_act = jnp.dot(normed, up_weight, preferred_element_type=jnp.float32)
        hidden = (jax.nn.silu(gate_act) * up_act).astype(jnp.bfloat16)
        down_part = jnp.dot(hidden, down_weight, preferred_element_type=jnp.float32).astype(jnp.bfloat16)
        down_cols = pair_then_z_scatter(down_part)
        return (own_residual.astype(jnp.float32) + down_cols).astype(jnp.bfloat16)

    row_count = hidden_in.shape[0]
    cut = 8 * ((row_count + 23) // 24)
    bounds = [0, cut, 2 * cut, row_count]
    out_cols = jnp.concatenate(
        [feed_forward(attn_rows[bounds[i] : bounds[i + 1]], hidden_in[bounds[i] : bounds[i + 1]]) for i in range(3)], axis=0
    )

    slot_rows = 8 * ((2 * row_count + 8 * req_count - 1) // (8 * req_count))
    owners = row_owner[:, 0]
    onehot_owner = (owners[:, None] == jnp.arange(req_count, dtype=jnp.int32)[None, :]).astype(
        jnp.int32
    )
    before = rank_within(onehot_owner, 0)
    target = owners * slot_rows + before
    placing = (
        target[None, :] == jnp.arange(req_count * slot_rows, dtype=jnp.int32)[:, None]
    ).astype(jnp.bfloat16)
    outgoing = jnp.dot(placing, out_cols, preferred_element_type=jnp.float32).astype(jnp.bfloat16)
    arrived = lax.all_to_all(outgoing, "req", split_axis=0, concat_axis=0, tiled=True)
    routed = lax.all_to_all(arrived, "head", split_axis=0, concat_axis=1, tiled=True)
    ring = head_count // 2
    return jnp.concatenate(
        [
            routed[:, ((b % ring) * 2 + b // ring) * width_here : ((b % ring) * 2 + b // ring + 1) * width_here]
            for b in range(head_count)
        ],
        axis=1,
    )


def solution(mesh):
    placed = (
        P("req", "head"),
        P("req", "head"),
        P("req", "head"),
        P("req", "head"),
        P("req", "head"),
        P("req", "head"),
        P("req", "head"),
        P("req", None, "head"),
        P("req", None, "head"),
        P(),
        P("req"),
        P("req"),
        P("req", None),
        P("head", None),
        P(),
        P(None, "head"),
        P(None, "head"),
        P("head", None),
    )
    return jax.shard_map(
        on_device, mesh=mesh, in_specs=placed, out_specs=P(("req", "head"), None), check_vma=False
    )
```

```python
import math

import jax
import jax.numpy as jnp
from jax import lax
from jax.sharding import PartitionSpec as P

HD = 96
CAP = 48


eps_norm = 1e-05


def rank_within(onehot, axis):
    return jnp.sum((jnp.cumsum(onehot, axis=axis) - 1) * onehot, axis=-1)


def pair_then_z_scatter(x):
    rows, cols = x.shape
    n = lax.axis_size("head")
    ring = n // 2
    width = cols // n
    half = cols // 2
    h = lax.axis_index("head")
    zc = h // 2
    on_first = h % 2 == 0
    mine = jnp.where(on_first, x[:, :half], x[:, half:])
    other = jnp.where(on_first, x[:, half:], x[:, :half])
    got = lax.ppermute(other, "head", [(i, i ^ 1) for i in range(n)])
    pair_sum = (mine.astype(jnp.float32) + got.astype(jnp.float32)).astype(jnp.bfloat16)
    acc = lax.dynamic_slice_in_dim(pair_sum, zc * width, width, 1).astype(jnp.float32)
    for d in range(1, ring):
        perm = [(i, ((i // 2 + d) % ring) * 2 + i % 2) for i in range(n)]
        piece = lax.dynamic_slice_in_dim(pair_sum, ((zc + d) % ring) * width, width, 1)
        acc = acc + lax.ppermute(piece, "head", perm).astype(jnp.float32)
    return acc


def z_then_pair_gather(y):
    rows, width = y.shape
    n = lax.axis_size("head")
    ring = n // 2
    h = lax.axis_index("head")
    zc = h // 2
    on_first = h % 2 == 0
    parts = [y]
    for d in range(1, ring):
        perm = [(i, ((i // 2 + d) % ring) * 2 + i % 2) for i in range(n)]
        parts.append(lax.ppermute(y, "head", perm))
    stacked = jnp.stack(parts, 0)
    in_order = jnp.concatenate(
        [lax.dynamic_index_in_dim(stacked, (zc - zz) % ring, 0, keepdims=False) for zz in range(ring)], 1
    )
    got = lax.ppermute(in_order, "head", [(i, i ^ 1) for i in range(n)])
    return jnp.where(
        on_first, jnp.concatenate([in_order, got], 1), jnp.concatenate([got, in_order], 1)
    )


def on_device(
    hidden_in,
    dec_query,
    dec_key,
    dec_value,
    pre_query,
    pre_key,
    pre_value,
    cache_key,
    cache_value,
    group_of,
    cache_length,
    stretch_start,
    row_owner,
    out_weight,
    norm_gain,
    gate_weight,
    up_weight,
    down_weight,
):
    factor = 1.0 / math.sqrt(HD)
    width_here = dec_query.shape[1]
    req_count = lax.axis_size("req")
    head_count = lax.axis_size("head")
    me = lax.axis_index("req")
    groups_here = cache_key.shape[0]
    length_cache = cache_key.shape[1]
    per_home = dec_query.shape[0]
    members = group_of[:, 0]
    total_reqs = members.shape[0]

    holder_of = members // groups_here
    holder_hot = (holder_of[:, None] == jnp.arange(req_count, dtype=jnp.int32)[None, :]).astype(jnp.int32)
    rank_all = rank_within(holder_hot.reshape(req_count, per_home, req_count), 1).reshape(total_reqs)
    slot_of = (jnp.arange(total_reqs, dtype=jnp.int32) // per_home) * per_home + rank_all

    my_holder = lax.dynamic_slice_in_dim(holder_of, me * per_home, per_home)
    my_rank = lax.dynamic_slice_in_dim(rank_all, me * per_home, per_home)
    my_slot = my_holder * per_home + my_rank
    packer = (
        my_slot[None, :] == jnp.arange(req_count * per_home, dtype=jnp.int32)[:, None]
    ).astype(jnp.bfloat16)
    outgoing_q = jnp.dot(packer, dec_query, preferred_element_type=jnp.float32).astype(jnp.bfloat16)
    arrived_q = lax.all_to_all(outgoing_q, "req", split_axis=0, concat_axis=0, tiled=True)

    first_group = me * groups_here
    wanted = first_group + jnp.arange(groups_here, dtype=jnp.int32)
    belongs = (members[None, :] == wanted[:, None]).astype(jnp.int32)
    ranking = jnp.cumsum(belongs, axis=1) - 1
    places = jnp.arange(CAP, dtype=jnp.int32)
    chosen = ((belongs[:, None, :] == 1) & (ranking[:, None, :] == places[None, :, None])).reshape(
        groups_here * CAP, total_reqs
    )
    chosen_slot = jnp.sum(jnp.where(chosen, slot_of[None, :], 0), axis=1)
    chosen_any = jnp.any(chosen, axis=1)
    chooser = chosen_any[:, None] & (
        chosen_slot[:, None] == jnp.arange(req_count * per_home, dtype=jnp.int32)[None, :]
    )
    picked = jnp.dot(
        chooser.astype(jnp.bfloat16), arrived_q, preferred_element_type=jnp.float32
    ).astype(jnp.bfloat16)
    heads_here = width_here // HD
    head_mask = (jnp.arange(width_here) // HD)[None, :] == jnp.arange(heads_here)[:, None]
    positions = jnp.arange(length_cache)
    results = []
    pad_cols = 128
    for group_pos in range(groups_here):
        q_rows = picked[group_pos * CAP : (group_pos + 1) * CAP]
        q_stack = jnp.where(head_mask[:, None, :], q_rows[None], 0).reshape(heads_here * CAP, width_here)
        cache_scores = lax.dot_general(
            q_stack, cache_key[group_pos], (((1,), (1,)), ((), ())), preferred_element_type=jnp.float32
        ) * factor
        valid = (positions < cache_length[group_pos])[None, :]
        cache_scores = jnp.where(valid, cache_scores, -jnp.inf)
        highest = jnp.max(cache_scores, axis=-1, keepdims=True)
        raised = jnp.exp(cache_scores - highest)
        total = jnp.sum(raised, axis=-1, keepdims=True)
        weights = (raised / total).astype(jnp.bfloat16)
        mixed = jnp.dot(weights, cache_value[group_pos], preferred_element_type=jnp.float32)
        blended = jnp.sum(
            jnp.where(head_mask[:, None, :], mixed.reshape(heads_here, CAP, width_here), 0.0), axis=0
        )
        spread = (highest + jnp.log(total)).reshape(heads_here, CAP).T
        spread_hi = spread.astype(jnp.bfloat16)
        spread_lo = (spread - spread_hi.astype(jnp.float32)).astype(jnp.bfloat16)
        tail = jnp.zeros((CAP, pad_cols - 2 * heads_here), jnp.bfloat16)
        results.append(
            jnp.concatenate([blended.astype(jnp.bfloat16), spread_hi, spread_lo, tail], axis=1)
        )
    stacked = jnp.concatenate(results, axis=0)
    going_back = jnp.dot(
        chooser.astype(jnp.bfloat16).T, stacked, preferred_element_type=jnp.float32
    ).astype(jnp.bfloat16)
    came_back = lax.all_to_all(going_back, "req", split_axis=0, concat_axis=0, tiled=True)
    dec_back = jnp.dot(packer.T, came_back, preferred_element_type=jnp.float32)
    cache_mix = dec_back[:, :width_here]
    cache_spread = (
        dec_back[:, width_here : width_here + heads_here]
        + dec_back[:, width_here + heads_here : width_here + 2 * heads_here]
    )
    own_prod = dec_query.astype(jnp.float32) * dec_key.astype(jnp.float32)
    own_scores = jnp.sum(jnp.where(head_mask[:, None, :], own_prod[None], 0.0), axis=-1).T * factor
    top = jnp.maximum(cache_spread, own_scores)
    part_cache = jnp.exp(cache_spread - top)
    part_own = jnp.exp(own_scores - top)
    share_own = part_own / (part_cache + part_own)
    share_cols = jnp.sum(jnp.where(head_mask[:, None, :], share_own.T[:, :, None], 0.0), axis=0)
    dec_out = (
        (1.0 - share_cols) * cache_mix + share_cols * dec_value.astype(jnp.float32)
    ).astype(jnp.bfloat16)

    stretch_len = pre_query.shape[0]
    row_numbers = jnp.arange(stretch_len)
    pre_stack = jnp.where(head_mask[:, None, :], pre_query[None], 0).reshape(heads_here * stretch_len, width_here)
    dims = (((1,), (1,)), ((), ()))
    cache_part = lax.dot_general(pre_stack, cache_key[0], dims, preferred_element_type=jnp.float32) * factor
    self_part = lax.dot_general(pre_stack, pre_key, dims, preferred_element_type=jnp.float32) * factor
    cache_part = jnp.where((positions < stretch_start[0])[None, :], cache_part, -jnp.inf)
    causal = (row_numbers[None, :] <= row_numbers[:, None])[None]
    self_part = jnp.where(causal, self_part.reshape(heads_here, stretch_len, stretch_len), -jnp.inf).reshape(
        heads_here * stretch_len, stretch_len
    )
    highest = jnp.maximum(
        jnp.max(cache_part, axis=-1, keepdims=True), jnp.max(self_part, axis=-1, keepdims=True)
    )
    raised_cache = jnp.exp(cache_part - highest)
    raised_self = jnp.exp(self_part - highest)
    total = jnp.sum(raised_cache, axis=-1, keepdims=True) + jnp.sum(raised_self, axis=-1, keepdims=True)
    pre_mixed = jnp.dot(
        (raised_cache / total).astype(jnp.bfloat16), cache_value[0], preferred_element_type=jnp.float32
    ) + jnp.dot((raised_self / total).astype(jnp.bfloat16), pre_value, preferred_element_type=jnp.float32)
    pre_out = jnp.sum(
        jnp.where(head_mask[:, None, :], pre_mixed.reshape(heads_here, stretch_len, width_here), 0.0), axis=0
    ).astype(jnp.bfloat16)
    dec_out, pre_out = lax.optimization_barrier((dec_out, pre_out))
    attn_rows = jnp.concatenate([dec_out, pre_out], axis=0)
    head_me = lax.axis_index("head")
    col_start = head_me * width_here

    def feed_forward(attn_chunk, hidden_chunk, after=None):
        if after is not None:
            attn_chunk, _ = lax.optimization_barrier((attn_chunk, after))
        projected = jnp.dot(attn_chunk, out_weight, preferred_element_type=jnp.float32)
        own_cols = lax.dynamic_slice_in_dim(projected, col_start, width_here, 1) + hidden_chunk.astype(
            jnp.float32
        )
        contribution = lax.dynamic_update_slice_in_dim(projected, own_cols, col_start, 1)
        own_residual = pair_then_z_scatter(contribution.astype(jnp.bfloat16)).astype(jnp.bfloat16)
        residual = z_then_pair_gather(own_residual)
        residual_wide = residual.astype(jnp.float32)
        squares = jnp.mean(jnp.square(residual_wide), axis=-1, keepdims=True)
        normed = (residual_wide * lax.rsqrt(squares + eps_norm) * norm_gain).astype(jnp.bfloat16)
        gate_act = jnp.dot(normed, gate_weight, preferred_element_type=jnp.float32)
        up_act = jnp.dot(normed, up_weight, preferred_element_type=jnp.float32)
        hidden = (jax.nn.silu(gate_act) * up_act).astype(jnp.bfloat16)
        down_part = jnp.dot(hidden, down_weight, preferred_element_type=jnp.float32).astype(jnp.bfloat16)
        down_cols = pair_then_z_scatter(down_part)
        return (own_residual.astype(jnp.float32) + down_cols).astype(jnp.bfloat16), residual

    row_count = hidden_in.shape[0]
    half = row_count // 2
    first_cols, first_residual = feed_forward(attn_rows[:half], hidden_in[:half])
    second_cols, _ = feed_forward(attn_rows[half:], hidden_in[half:], after=first_residual)
    out_cols = jnp.concatenate([first_cols, second_cols], axis=0)

    slot_rows = 8 * ((2 * row_count + 8 * req_count - 1) // (8 * req_count))
    owners = row_owner[:, 0]
    onehot_owner = (owners[:, None] == jnp.arange(req_count, dtype=jnp.int32)[None, :]).astype(
        jnp.int32
    )
    before = rank_within(onehot_owner, 0)
    target = owners * slot_rows + before
    placing = (
        target[None, :] == jnp.arange(req_count * slot_rows, dtype=jnp.int32)[:, None]
    ).astype(jnp.bfloat16)
    outgoing = jnp.dot(placing, out_cols, preferred_element_type=jnp.float32).astype(jnp.bfloat16)
    arrived = lax.all_to_all(outgoing, "req", split_axis=0, concat_axis=0, tiled=True)
    routed = lax.all_to_all(arrived, "head", split_axis=0, concat_axis=1, tiled=True)
    ring = head_count // 2
    return jnp.concatenate(
        [
            routed[:, ((b % ring) * 2 + b // ring) * width_here : ((b % ring) * 2 + b // ring + 1) * width_here]
            for b in range(head_count)
        ],
        axis=1,
    )


def solution(mesh):
    placed = (
        P("req", "head"),
        P("req", "head"),
        P("req", "head"),
        P("req", "head"),
        P("req", "head"),
        P("req", "head"),
        P("req", "head"),
        P("req", None, "head"),
        P("req", None, "head"),
        P(),
        P("req"),
        P("req"),
        P("req", None),
        P("head", None),
        P(),
        P(None, "head"),
        P(None, "head"),
        P("head", None),
    )
    return jax.shard_map(
        on_device, mesh=mesh, in_specs=placed, out_specs=P(("req", "head"), None), check_vma=False
    )
```

```python
import math

import jax
import jax.numpy as jnp
from jax import lax
from jax.sharding import PartitionSpec as P

HD = 96
CAP = 48


eps_norm = 1e-05


def rank_within(onehot, axis):
    return jnp.sum((jnp.cumsum(onehot, axis=axis) - 1) * onehot, axis=-1)


def pair_then_z_scatter(x):
    rows, cols = x.shape
    n = lax.axis_size("head")
    ring = n // 2
    width = cols // n
    h = lax.axis_index("head")
    zc = h // 2
    on_first = h % 2 == 0
    even = jnp.concatenate([x[:, (2 * z) * width : (2 * z + 1) * width] for z in range(ring)], 1)
    odd = jnp.concatenate([x[:, (2 * z + 1) * width : (2 * z + 2) * width] for z in range(ring)], 1)
    mine = jnp.where(on_first, even, odd)
    other = jnp.where(on_first, odd, even)
    got = lax.ppermute(other, "head", [(i, i ^ 1) for i in range(n)])
    pair_sum = (mine.astype(jnp.float32) + got.astype(jnp.float32)).astype(jnp.bfloat16)
    acc = lax.dynamic_slice_in_dim(pair_sum, zc * width, width, 1).astype(jnp.float32)
    for d in range(1, ring):
        perm = [(i, ((i // 2 + d) % ring) * 2 + i % 2) for i in range(n)]
        piece = lax.dynamic_slice_in_dim(pair_sum, ((zc + d) % ring) * width, width, 1)
        acc = acc + lax.ppermute(piece, "head", perm).astype(jnp.float32)
    return acc


def z_then_pair_gather(y):
    rows, width = y.shape
    n = lax.axis_size("head")
    ring = n // 2
    h = lax.axis_index("head")
    zc = h // 2
    on_first = h % 2 == 0
    parts = [y]
    for d in range(1, ring):
        perm = [(i, ((i // 2 + d) % ring) * 2 + i % 2) for i in range(n)]
        parts.append(lax.ppermute(y, "head", perm))
    stacked = jnp.stack(parts, 0)
    in_order = jnp.concatenate(
        [lax.dynamic_index_in_dim(stacked, (zc - zz) % ring, 0, keepdims=False) for zz in range(ring)], 1
    )
    got = lax.ppermute(in_order, "head", [(i, i ^ 1) for i in range(n)])
    pieces = []
    for z in range(ring):
        mine_z = in_order[:, z * width : (z + 1) * width]
        got_z = got[:, z * width : (z + 1) * width]
        pieces.append(jnp.where(on_first, mine_z, got_z))
        pieces.append(jnp.where(on_first, got_z, mine_z))
    return jnp.concatenate(pieces, 1)


def on_device(
    hidden_in,
    dec_query,
    dec_key,
    dec_value,
    pre_query,
    pre_key,
    pre_value,
    cache_key,
    cache_value,
    group_of,
    cache_length,
    stretch_start,
    row_owner,
    out_weight,
    norm_gain,
    gate_weight,
    up_weight,
    down_weight,
):
    factor = 1.0 / math.sqrt(HD)
    width_here = dec_query.shape[1]
    req_count = lax.axis_size("req")
    head_count = lax.axis_size("head")
    me = lax.axis_index("req")
    groups_here = cache_key.shape[0]
    length_cache = cache_key.shape[1]
    per_home = dec_query.shape[0]
    members = group_of[:, 0]
    total_reqs = members.shape[0]

    holder_of = members // groups_here
    holder_hot = (holder_of[:, None] == jnp.arange(req_count, dtype=jnp.int32)[None, :]).astype(jnp.int32)
    rank_all = rank_within(holder_hot.reshape(req_count, per_home, req_count), 1).reshape(total_reqs)
    slot_of = (jnp.arange(total_reqs, dtype=jnp.int32) // per_home) * per_home + rank_all

    my_holder = lax.dynamic_slice_in_dim(holder_of, me * per_home, per_home)
    my_rank = lax.dynamic_slice_in_dim(rank_all, me * per_home, per_home)
    my_slot = my_holder * per_home + my_rank
    packer = (
        my_slot[None, :] == jnp.arange(req_count * per_home, dtype=jnp.int32)[:, None]
    ).astype(jnp.bfloat16)
    outgoing_q = jnp.dot(packer, dec_query, preferred_element_type=jnp.float32).astype(jnp.bfloat16)
    arrived_q = lax.all_to_all(outgoing_q, "req", split_axis=0, concat_axis=0, tiled=True)

    first_group = me * groups_here
    wanted = first_group + jnp.arange(groups_here, dtype=jnp.int32)
    belongs = (members[None, :] == wanted[:, None]).astype(jnp.int32)
    ranking = jnp.cumsum(belongs, axis=1) - 1
    places = jnp.arange(CAP, dtype=jnp.int32)
    chosen = ((belongs[:, None, :] == 1) & (ranking[:, None, :] == places[None, :, None])).reshape(
        groups_here * CAP, total_reqs
    )
    chosen_slot = jnp.sum(jnp.where(chosen, slot_of[None, :], 0), axis=1)
    chosen_any = jnp.any(chosen, axis=1)
    chooser = chosen_any[:, None] & (
        chosen_slot[:, None] == jnp.arange(req_count * per_home, dtype=jnp.int32)[None, :]
    )
    picked = jnp.dot(
        chooser.astype(jnp.bfloat16), arrived_q, preferred_element_type=jnp.float32
    ).astype(jnp.bfloat16)
    heads_here = width_here // HD
    head_mask = (jnp.arange(width_here) // HD)[None, :] == jnp.arange(heads_here)[:, None]
    positions = jnp.arange(length_cache)
    results = []
    pad_cols = 128
    for group_pos in range(groups_here):
        q_rows = picked[group_pos * CAP : (group_pos + 1) * CAP]
        q_stack = jnp.where(head_mask[:, None, :], q_rows[None], 0).reshape(heads_here * CAP, width_here)
        cache_scores = lax.dot_general(
            q_stack, cache_key[group_pos], (((1,), (1,)), ((), ())), preferred_element_type=jnp.float32
        ) * factor
        valid = (positions < cache_length[group_pos])[None, :]
        cache_scores = jnp.where(valid, cache_scores, -jnp.inf)
        highest = jnp.max(cache_scores, axis=-1, keepdims=True)
        raised = jnp.exp(cache_scores - highest)
        total = jnp.sum(raised, axis=-1, keepdims=True)
        weights = (raised / total).astype(jnp.bfloat16)
        mixed = jnp.dot(weights, cache_value[group_pos], preferred_element_type=jnp.float32)
        blended = jnp.sum(
            jnp.where(head_mask[:, None, :], mixed.reshape(heads_here, CAP, width_here), 0.0), axis=0
        )
        spread = (highest + jnp.log(total)).reshape(heads_here, CAP).T
        spread_hi = spread.astype(jnp.bfloat16)
        spread_lo = (spread - spread_hi.astype(jnp.float32)).astype(jnp.bfloat16)
        tail = jnp.zeros((CAP, pad_cols - 2 * heads_here), jnp.bfloat16)
        results.append(
            jnp.concatenate([blended.astype(jnp.bfloat16), spread_hi, spread_lo, tail], axis=1)
        )
    stacked = jnp.concatenate(results, axis=0)
    going_back = jnp.dot(
        chooser.astype(jnp.bfloat16).T, stacked, preferred_element_type=jnp.float32
    ).astype(jnp.bfloat16)
    came_back = lax.all_to_all(going_back, "req", split_axis=0, concat_axis=0, tiled=True)
    dec_back = jnp.dot(packer.T, came_back, preferred_element_type=jnp.float32)
    cache_mix = dec_back[:, :width_here]
    cache_spread = (
        dec_back[:, width_here : width_here + heads_here]
        + dec_back[:, width_here + heads_here : width_here + 2 * heads_here]
    )
    own_prod = dec_query.astype(jnp.float32) * dec_key.astype(jnp.float32)
    own_scores = jnp.sum(jnp.where(head_mask[:, None, :], own_prod[None], 0.0), axis=-1).T * factor
    top = jnp.maximum(cache_spread, own_scores)
    part_cache = jnp.exp(cache_spread - top)
    part_own = jnp.exp(own_scores - top)
    share_own = part_own / (part_cache + part_own)
    share_cols = jnp.sum(jnp.where(head_mask[:, None, :], share_own.T[:, :, None], 0.0), axis=0)
    dec_out = (
        (1.0 - share_cols) * cache_mix + share_cols * dec_value.astype(jnp.float32)
    ).astype(jnp.bfloat16)

    stretch_len = pre_query.shape[0]
    row_numbers = jnp.arange(stretch_len)
    pre_stack = jnp.where(head_mask[:, None, :], pre_query[None], 0).reshape(heads_here * stretch_len, width_here)
    dims = (((1,), (1,)), ((), ()))
    cache_part = lax.dot_general(pre_stack, cache_key[0], dims, preferred_element_type=jnp.float32) * factor
    self_part = lax.dot_general(pre_stack, pre_key, dims, preferred_element_type=jnp.float32) * factor
    cache_part = jnp.where((positions < stretch_start[0])[None, :], cache_part, -jnp.inf)
    causal = (row_numbers[None, :] <= row_numbers[:, None])[None]
    self_part = jnp.where(causal, self_part.reshape(heads_here, stretch_len, stretch_len), -jnp.inf).reshape(
        heads_here * stretch_len, stretch_len
    )
    highest = jnp.maximum(
        jnp.max(cache_part, axis=-1, keepdims=True), jnp.max(self_part, axis=-1, keepdims=True)
    )
    raised_cache = jnp.exp(cache_part - highest)
    raised_self = jnp.exp(self_part - highest)
    total = jnp.sum(raised_cache, axis=-1, keepdims=True) + jnp.sum(raised_self, axis=-1, keepdims=True)
    pre_mixed = jnp.dot(
        (raised_cache / total).astype(jnp.bfloat16), cache_value[0], preferred_element_type=jnp.float32
    ) + jnp.dot((raised_self / total).astype(jnp.bfloat16), pre_value, preferred_element_type=jnp.float32)
    pre_out = jnp.sum(
        jnp.where(head_mask[:, None, :], pre_mixed.reshape(heads_here, stretch_len, width_here), 0.0), axis=0
    ).astype(jnp.bfloat16)
    row_count = hidden_in.shape[0]
    half = row_count // 2
    late_attn, _ = lax.optimization_barrier((pre_out[half - per_home :], going_back))
    dec_out, early_pre = lax.optimization_barrier((dec_out, pre_out[: half - per_home]))
    early_attn = jnp.concatenate([dec_out, early_pre], axis=0)
    head_me = lax.axis_index("head")
    col_start = head_me * width_here

    def feed_forward(attn_chunk, hidden_chunk):
        projected = jnp.dot(attn_chunk, out_weight, preferred_element_type=jnp.float32)
        own_cols = lax.dynamic_slice_in_dim(projected, col_start, width_here, 1) + hidden_chunk.astype(
            jnp.float32
        )
        contribution = lax.dynamic_update_slice_in_dim(projected, own_cols, col_start, 1)
        own_residual = pair_then_z_scatter(contribution.astype(jnp.bfloat16)).astype(jnp.bfloat16)
        residual = z_then_pair_gather(own_residual)
        residual_wide = residual.astype(jnp.float32)
        squares = jnp.mean(jnp.square(residual_wide), axis=-1, keepdims=True)
        normed = (residual_wide * lax.rsqrt(squares + eps_norm) * norm_gain).astype(jnp.bfloat16)
        gate_act = jnp.dot(normed, gate_weight, preferred_element_type=jnp.float32)
        up_act = jnp.dot(normed, up_weight, preferred_element_type=jnp.float32)
        hidden = (jax.nn.silu(gate_act) * up_act).astype(jnp.bfloat16)
        down_part = jnp.dot(hidden, down_weight, preferred_element_type=jnp.float32).astype(jnp.bfloat16)
        down_cols = pair_then_z_scatter(down_part)
        return (own_residual.astype(jnp.float32) + down_cols).astype(jnp.bfloat16)

    out_cols = jnp.concatenate(
        [
            feed_forward(early_attn, hidden_in[:half]),
            feed_forward(late_attn, hidden_in[half:]),
        ],
        axis=0,
    )

    slot_rows = 8 * ((2 * row_count + 8 * req_count - 1) // (8 * req_count))
    owners = row_owner[:, 0]
    onehot_owner = (owners[:, None] == jnp.arange(req_count, dtype=jnp.int32)[None, :]).astype(
        jnp.int32
    )
    before = rank_within(onehot_owner, 0)
    target = owners * slot_rows + before
    placing = (
        target[None, :] == jnp.arange(req_count * slot_rows, dtype=jnp.int32)[:, None]
    ).astype(jnp.bfloat16)
    outgoing = jnp.dot(placing, out_cols, preferred_element_type=jnp.float32).astype(jnp.bfloat16)
    arrived = lax.all_to_all(outgoing, "req", split_axis=0, concat_axis=0, tiled=True)
    return lax.all_to_all(arrived, "head", split_axis=0, concat_axis=1, tiled=True)


def solution(mesh):
    placed = (
        P("req", "head"),
        P("req", "head"),
        P("req", "head"),
        P("req", "head"),
        P("req", "head"),
        P("req", "head"),
        P("req", "head"),
        P("req", None, "head"),
        P("req", None, "head"),
        P(),
        P("req"),
        P("req"),
        P("req", None),
        P("head", None),
        P(),
        P(None, "head"),
        P(None, "head"),
        P("head", None),
    )
    return jax.shard_map(
        on_device, mesh=mesh, in_specs=placed, out_specs=P(("req", "head"), None), check_vma=False
    )
```

```python
import math

import jax
import jax.numpy as jnp
from jax import lax
from jax.sharding import PartitionSpec as P

HD = 96
CAP = 48


eps_norm = 1e-05


def rank_within(onehot, axis):
    return jnp.sum((jnp.cumsum(onehot, axis=axis) - 1) * onehot, axis=-1)


def pair_then_z_scatter(x):
    rows, cols = x.shape
    n = lax.axis_size("head")
    ring = n // 2
    width = cols // n
    h = lax.axis_index("head")
    zc = h // 2
    on_first = h % 2 == 0
    even = jnp.concatenate([x[:, (2 * z) * width : (2 * z + 1) * width] for z in range(ring)], 1)
    odd = jnp.concatenate([x[:, (2 * z + 1) * width : (2 * z + 2) * width] for z in range(ring)], 1)
    mine = jnp.where(on_first, even, odd)
    other = jnp.where(on_first, odd, even)
    got = lax.ppermute(other, "head", [(i, i ^ 1) for i in range(n)])
    pair_sum = (mine.astype(jnp.float32) + got.astype(jnp.float32)).astype(jnp.bfloat16)
    acc = lax.dynamic_slice_in_dim(pair_sum, zc * width, width, 1).astype(jnp.float32)
    for d in range(1, ring):
        perm = [(i, ((i // 2 + d) % ring) * 2 + i % 2) for i in range(n)]
        piece = lax.dynamic_slice_in_dim(pair_sum, ((zc + d) % ring) * width, width, 1)
        acc = acc + lax.ppermute(piece, "head", perm).astype(jnp.float32)
    return acc


def z_then_pair_gather(y):
    rows, width = y.shape
    n = lax.axis_size("head")
    ring = n // 2
    h = lax.axis_index("head")
    zc = h // 2
    on_first = h % 2 == 0
    parts = [y]
    for d in range(1, ring):
        perm = [(i, ((i // 2 + d) % ring) * 2 + i % 2) for i in range(n)]
        parts.append(lax.ppermute(y, "head", perm))
    stacked = jnp.stack(parts, 0)
    in_order = jnp.concatenate(
        [lax.dynamic_index_in_dim(stacked, (zc - zz) % ring, 0, keepdims=False) for zz in range(ring)], 1
    )
    got = lax.ppermute(in_order, "head", [(i, i ^ 1) for i in range(n)])
    pieces = []
    for z in range(ring):
        mine_z = in_order[:, z * width : (z + 1) * width]
        got_z = got[:, z * width : (z + 1) * width]
        pieces.append(jnp.where(on_first, mine_z, got_z))
        pieces.append(jnp.where(on_first, got_z, mine_z))
    return jnp.concatenate(pieces, 1)


def on_device(
    hidden_in,
    dec_query,
    dec_key,
    dec_value,
    pre_query,
    pre_key,
    pre_value,
    cache_key,
    cache_value,
    group_of,
    cache_length,
    stretch_start,
    row_owner,
    out_weight,
    norm_gain,
    gate_weight,
    up_weight,
    down_weight,
):
    factor = 1.0 / math.sqrt(HD)
    width_here = dec_query.shape[1]
    req_count = lax.axis_size("req")
    head_count = lax.axis_size("head")
    me = lax.axis_index("req")
    groups_here = cache_key.shape[0]
    length_cache = cache_key.shape[1]
    per_home = dec_query.shape[0]
    members = group_of[:, 0]
    total_reqs = members.shape[0]

    holder_of = members // groups_here
    holder_hot = (holder_of[:, None] == jnp.arange(req_count, dtype=jnp.int32)[None, :]).astype(jnp.int32)
    rank_all = rank_within(holder_hot.reshape(req_count, per_home, req_count), 1).reshape(total_reqs)
    slot_of = (jnp.arange(total_reqs, dtype=jnp.int32) // per_home) * per_home + rank_all

    my_holder = lax.dynamic_slice_in_dim(holder_of, me * per_home, per_home)
    my_rank = lax.dynamic_slice_in_dim(rank_all, me * per_home, per_home)
    my_slot = my_holder * per_home + my_rank
    packer = (
        my_slot[None, :] == jnp.arange(req_count * per_home, dtype=jnp.int32)[:, None]
    ).astype(jnp.bfloat16)
    outgoing_q = jnp.dot(packer, dec_query, preferred_element_type=jnp.float32).astype(jnp.bfloat16)
    arrived_q = lax.all_to_all(outgoing_q, "req", split_axis=0, concat_axis=0, tiled=True)

    first_group = me * groups_here
    wanted = first_group + jnp.arange(groups_here, dtype=jnp.int32)
    belongs = (members[None, :] == wanted[:, None]).astype(jnp.int32)
    ranking = jnp.cumsum(belongs, axis=1) - 1
    places = jnp.arange(CAP, dtype=jnp.int32)
    chosen = ((belongs[:, None, :] == 1) & (ranking[:, None, :] == places[None, :, None])).reshape(
        groups_here * CAP, total_reqs
    )
    chosen_slot = jnp.sum(jnp.where(chosen, slot_of[None, :], 0), axis=1)
    chosen_any = jnp.any(chosen, axis=1)
    chooser = chosen_any[:, None] & (
        chosen_slot[:, None] == jnp.arange(req_count * per_home, dtype=jnp.int32)[None, :]
    )
    picked = jnp.dot(
        chooser.astype(jnp.bfloat16), arrived_q, preferred_element_type=jnp.float32
    ).astype(jnp.bfloat16)
    heads_here = width_here // HD
    head_mask = (jnp.arange(width_here) // HD)[None, :] == jnp.arange(heads_here)[:, None]
    positions = jnp.arange(length_cache)
    results = []
    pad_cols = 128
    for group_pos in range(groups_here):
        q_rows = picked[group_pos * CAP : (group_pos + 1) * CAP]
        q_stack = jnp.where(head_mask[:, None, :], q_rows[None], 0).reshape(heads_here * CAP, width_here)
        cache_scores = lax.dot_general(
            q_stack, cache_key[group_pos], (((1,), (1,)), ((), ())), preferred_element_type=jnp.float32
        ) * factor
        valid = (positions < cache_length[group_pos])[None, :]
        cache_scores = jnp.where(valid, cache_scores, -jnp.inf)
        highest = jnp.max(cache_scores, axis=-1, keepdims=True)
        raised = jnp.exp(cache_scores - highest)
        total = jnp.sum(raised, axis=-1, keepdims=True)
        weights = (raised / total).astype(jnp.bfloat16)
        mixed = jnp.dot(weights, cache_value[group_pos], preferred_element_type=jnp.float32)
        blended = jnp.sum(
            jnp.where(head_mask[:, None, :], mixed.reshape(heads_here, CAP, width_here), 0.0), axis=0
        )
        spread = (highest + jnp.log(total)).reshape(heads_here, CAP).T
        spread_hi = spread.astype(jnp.bfloat16)
        spread_lo = (spread - spread_hi.astype(jnp.float32)).astype(jnp.bfloat16)
        tail = jnp.zeros((CAP, pad_cols - 2 * heads_here), jnp.bfloat16)
        results.append(
            jnp.concatenate([blended.astype(jnp.bfloat16), spread_hi, spread_lo, tail], axis=1)
        )
    stacked = jnp.concatenate(results, axis=0)
    going_back = jnp.dot(
        chooser.astype(jnp.bfloat16).T, stacked, preferred_element_type=jnp.float32
    ).astype(jnp.bfloat16)
    came_back = lax.all_to_all(going_back, "req", split_axis=0, concat_axis=0, tiled=True)
    dec_back = jnp.dot(packer.T, came_back, preferred_element_type=jnp.float32)
    cache_mix = dec_back[:, :width_here]
    cache_spread = (
        dec_back[:, width_here : width_here + heads_here]
        + dec_back[:, width_here + heads_here : width_here + 2 * heads_here]
    )
    own_prod = dec_query.astype(jnp.float32) * dec_key.astype(jnp.float32)
    own_scores = jnp.sum(jnp.where(head_mask[:, None, :], own_prod[None], 0.0), axis=-1).T * factor
    top = jnp.maximum(cache_spread, own_scores)
    part_cache = jnp.exp(cache_spread - top)
    part_own = jnp.exp(own_scores - top)
    share_own = part_own / (part_cache + part_own)
    share_cols = jnp.sum(jnp.where(head_mask[:, None, :], share_own.T[:, :, None], 0.0), axis=0)
    dec_out = (
        (1.0 - share_cols) * cache_mix + share_cols * dec_value.astype(jnp.float32)
    ).astype(jnp.bfloat16)

    stretch_len = pre_query.shape[0]
    row_numbers = jnp.arange(stretch_len)
    pre_stack = jnp.where(head_mask[:, None, :], pre_query[None], 0).reshape(heads_here * stretch_len, width_here)
    dims = (((1,), (1,)), ((), ()))
    cache_part = lax.dot_general(pre_stack, cache_key[0], dims, preferred_element_type=jnp.float32) * factor
    self_part = lax.dot_general(pre_stack, pre_key, dims, preferred_element_type=jnp.float32) * factor
    cache_part = jnp.where((positions < stretch_start[0])[None, :], cache_part, -jnp.inf)
    causal = (row_numbers[None, :] <= row_numbers[:, None])[None]
    self_part = jnp.where(causal, self_part.reshape(heads_here, stretch_len, stretch_len), -jnp.inf).reshape(
        heads_here * stretch_len, stretch_len
    )
    highest = jnp.maximum(
        jnp.max(cache_part, axis=-1, keepdims=True), jnp.max(self_part, axis=-1, keepdims=True)
    )
    raised_cache = jnp.exp(cache_part - highest)
    raised_self = jnp.exp(self_part - highest)
    total = jnp.sum(raised_cache, axis=-1, keepdims=True) + jnp.sum(raised_self, axis=-1, keepdims=True)
    pre_mixed = jnp.dot(
        (raised_cache / total).astype(jnp.bfloat16), cache_value[0], preferred_element_type=jnp.float32
    ) + jnp.dot((raised_self / total).astype(jnp.bfloat16), pre_value, preferred_element_type=jnp.float32)
    pre_out = jnp.sum(
        jnp.where(head_mask[:, None, :], pre_mixed.reshape(heads_here, stretch_len, width_here), 0.0), axis=0
    ).astype(jnp.bfloat16)
    row_count = hidden_in.shape[0]
    half = 8 * ((row_count // 3 + 7) // 8)
    late_attn, _ = lax.optimization_barrier((pre_out[half - per_home :], going_back))
    dec_out, early_pre = lax.optimization_barrier((dec_out, pre_out[: half - per_home]))
    early_attn = jnp.concatenate([dec_out, early_pre], axis=0)
    head_me = lax.axis_index("head")
    col_start = head_me * width_here

    def feed_forward(attn_chunk, hidden_chunk):
        projected = jnp.dot(attn_chunk, out_weight, preferred_element_type=jnp.float32)
        own_cols = lax.dynamic_slice_in_dim(projected, col_start, width_here, 1) + hidden_chunk.astype(
            jnp.float32
        )
        contribution = lax.dynamic_update_slice_in_dim(projected, own_cols, col_start, 1)
        own_residual = pair_then_z_scatter(contribution.astype(jnp.bfloat16)).astype(jnp.bfloat16)
        residual = z_then_pair_gather(own_residual)
        residual_wide = residual.astype(jnp.float32)
        squares = jnp.mean(jnp.square(residual_wide), axis=-1, keepdims=True)
        normed = (residual_wide * lax.rsqrt(squares + eps_norm) * norm_gain).astype(jnp.bfloat16)
        gate_act = jnp.dot(normed, gate_weight, preferred_element_type=jnp.float32)
        up_act = jnp.dot(normed, up_weight, preferred_element_type=jnp.float32)
        hidden = (jax.nn.silu(gate_act) * up_act).astype(jnp.bfloat16)
        down_part = jnp.dot(hidden, down_weight, preferred_element_type=jnp.float32).astype(jnp.bfloat16)
        down_cols = pair_then_z_scatter(down_part)
        return (own_residual.astype(jnp.float32) + down_cols).astype(jnp.bfloat16)

    out_cols = jnp.concatenate(
        [
            feed_forward(early_attn, hidden_in[:half]),
            feed_forward(late_attn, hidden_in[half:]),
        ],
        axis=0,
    )

    slot_rows = 8 * ((2 * row_count + 8 * req_count - 1) // (8 * req_count))
    owners = row_owner[:, 0]
    onehot_owner = (owners[:, None] == jnp.arange(req_count, dtype=jnp.int32)[None, :]).astype(
        jnp.int32
    )
    before = rank_within(onehot_owner, 0)
    target = owners * slot_rows + before
    placing = (
        target[None, :] == jnp.arange(req_count * slot_rows, dtype=jnp.int32)[:, None]
    ).astype(jnp.bfloat16)
    outgoing = jnp.dot(placing, out_cols, preferred_element_type=jnp.float32).astype(jnp.bfloat16)
    arrived = lax.all_to_all(outgoing, "req", split_axis=0, concat_axis=0, tiled=True)
    return lax.all_to_all(arrived, "head", split_axis=0, concat_axis=1, tiled=True)


def solution(mesh):
    placed = (
        P("req", "head"),
        P("req", "head"),
        P("req", "head"),
        P("req", "head"),
        P("req", "head"),
        P("req", "head"),
        P("req", "head"),
        P("req", None, "head"),
        P("req", None, "head"),
        P(),
        P("req"),
        P("req"),
        P("req", None),
        P("head", None),
        P(),
        P(None, "head"),
        P(None, "head"),
        P("head", None),
    )
    return jax.shard_map(
        on_device, mesh=mesh, in_specs=placed, out_specs=P(("req", "head"), None), check_vma=False
    )
```

```python
import math

import jax
import jax.numpy as jnp
from jax import lax
from jax.sharding import PartitionSpec as P

HD = 96
CAP = 48


eps_norm = 1e-05


def rank_within(onehot, axis):
    return jnp.sum((jnp.cumsum(onehot, axis=axis) - 1) * onehot, axis=-1)


def pair_then_z_scatter(x):
    rows, cols = x.shape
    n = lax.axis_size("head")
    ring = n // 2
    width = cols // n
    h = lax.axis_index("head")
    zc = h // 2
    on_first = h % 2 == 0
    even = jnp.concatenate([x[:, (2 * z) * width : (2 * z + 1) * width] for z in range(ring)], 1)
    odd = jnp.concatenate([x[:, (2 * z + 1) * width : (2 * z + 2) * width] for z in range(ring)], 1)
    mine = jnp.where(on_first, even, odd)
    other = jnp.where(on_first, odd, even)
    got = lax.ppermute(other, "head", [(i, i ^ 1) for i in range(n)])
    pair_sum = (mine.astype(jnp.float32) + got.astype(jnp.float32)).astype(jnp.bfloat16)
    acc = lax.dynamic_slice_in_dim(pair_sum, zc * width, width, 1).astype(jnp.float32)
    for d in range(1, ring):
        perm = [(i, ((i // 2 + d) % ring) * 2 + i % 2) for i in range(n)]
        piece = lax.dynamic_slice_in_dim(pair_sum, ((zc + d) % ring) * width, width, 1)
        acc = acc + lax.ppermute(piece, "head", perm).astype(jnp.float32)
    return acc


def z_then_pair_gather(y):
    rows, width = y.shape
    n = lax.axis_size("head")
    ring = n // 2
    h = lax.axis_index("head")
    zc = h // 2
    on_first = h % 2 == 0
    parts = [y]
    for d in range(1, ring):
        perm = [(i, ((i // 2 + d) % ring) * 2 + i % 2) for i in range(n)]
        parts.append(lax.ppermute(y, "head", perm))
    stacked = jnp.stack(parts, 0)
    in_order = jnp.concatenate(
        [lax.dynamic_index_in_dim(stacked, (zc - zz) % ring, 0, keepdims=False) for zz in range(ring)], 1
    )
    got = lax.ppermute(in_order, "head", [(i, i ^ 1) for i in range(n)])
    pieces = []
    for z in range(ring):
        mine_z = in_order[:, z * width : (z + 1) * width]
        got_z = got[:, z * width : (z + 1) * width]
        pieces.append(jnp.where(on_first, mine_z, got_z))
        pieces.append(jnp.where(on_first, got_z, mine_z))
    return jnp.concatenate(pieces, 1)


def on_device(
    hidden_in,
    dec_query,
    dec_key,
    dec_value,
    pre_query,
    pre_key,
    pre_value,
    cache_key,
    cache_value,
    group_of,
    cache_length,
    stretch_start,
    row_owner,
    out_weight,
    norm_gain,
    gate_weight,
    up_weight,
    down_weight,
):
    factor = 1.0 / math.sqrt(HD)
    width_here = dec_query.shape[1]
    req_count = lax.axis_size("req")
    head_count = lax.axis_size("head")
    me = lax.axis_index("req")
    groups_here = cache_key.shape[0]
    length_cache = cache_key.shape[1]
    per_home = dec_query.shape[0]
    members = group_of[:, 0]
    total_reqs = members.shape[0]

    holder_of = members // groups_here
    holder_hot = (holder_of[:, None] == jnp.arange(req_count, dtype=jnp.int32)[None, :]).astype(jnp.int32)
    rank_all = rank_within(holder_hot.reshape(req_count, per_home, req_count), 1).reshape(total_reqs)
    slot_of = (jnp.arange(total_reqs, dtype=jnp.int32) // per_home) * per_home + rank_all

    my_holder = lax.dynamic_slice_in_dim(holder_of, me * per_home, per_home)
    my_rank = lax.dynamic_slice_in_dim(rank_all, me * per_home, per_home)
    my_slot = my_holder * per_home + my_rank
    packer = (
        my_slot[None, :] == jnp.arange(req_count * per_home, dtype=jnp.int32)[:, None]
    ).astype(jnp.bfloat16)
    outgoing_q = jnp.dot(packer, dec_query, preferred_element_type=jnp.float32).astype(jnp.bfloat16)
    arrived_q = lax.all_to_all(outgoing_q, "req", split_axis=0, concat_axis=0, tiled=True)

    first_group = me * groups_here
    wanted = first_group + jnp.arange(groups_here, dtype=jnp.int32)
    belongs = (members[None, :] == wanted[:, None]).astype(jnp.int32)
    ranking = jnp.cumsum(belongs, axis=1) - 1
    places = jnp.arange(CAP, dtype=jnp.int32)
    chosen = ((belongs[:, None, :] == 1) & (ranking[:, None, :] == places[None, :, None])).reshape(
        groups_here * CAP, total_reqs
    )
    chosen_slot = jnp.sum(jnp.where(chosen, slot_of[None, :], 0), axis=1)
    chosen_any = jnp.any(chosen, axis=1)
    chooser = chosen_any[:, None] & (
        chosen_slot[:, None] == jnp.arange(req_count * per_home, dtype=jnp.int32)[None, :]
    )
    picked = jnp.dot(
        chooser.astype(jnp.bfloat16), arrived_q, preferred_element_type=jnp.float32
    ).astype(jnp.bfloat16)
    heads_here = width_here // HD
    head_mask = (jnp.arange(width_here) // HD)[None, :] == jnp.arange(heads_here)[:, None]
    positions = jnp.arange(length_cache)
    results = []
    pad_cols = 128
    for group_pos in range(groups_here):
        q_rows = picked[group_pos * CAP : (group_pos + 1) * CAP]
        q_stack = jnp.where(head_mask[:, None, :], q_rows[None], 0).reshape(heads_here * CAP, width_here)
        cache_scores = lax.dot_general(
            q_stack, cache_key[group_pos], (((1,), (1,)), ((), ())), preferred_element_type=jnp.float32
        ) * factor
        valid = (positions < cache_length[group_pos])[None, :]
        cache_scores = jnp.where(valid, cache_scores, -jnp.inf)
        highest = jnp.max(cache_scores, axis=-1, keepdims=True)
        raised = jnp.exp(cache_scores - highest)
        total = jnp.sum(raised, axis=-1, keepdims=True)
        weights = (raised / total).astype(jnp.bfloat16)
        mixed = jnp.dot(weights, cache_value[group_pos], preferred_element_type=jnp.float32)
        blended = jnp.sum(
            jnp.where(head_mask[:, None, :], mixed.reshape(heads_here, CAP, width_here), 0.0), axis=0
        )
        spread = (highest + jnp.log(total)).reshape(heads_here, CAP).T
        spread_hi = spread.astype(jnp.bfloat16)
        spread_lo = (spread - spread_hi.astype(jnp.float32)).astype(jnp.bfloat16)
        tail = jnp.zeros((CAP, pad_cols - 2 * heads_here), jnp.bfloat16)
        results.append(
            jnp.concatenate([blended.astype(jnp.bfloat16), spread_hi, spread_lo, tail], axis=1)
        )
    stacked = jnp.concatenate(results, axis=0)
    going_back = jnp.dot(
        chooser.astype(jnp.bfloat16).T, stacked, preferred_element_type=jnp.float32
    ).astype(jnp.bfloat16)
    came_back = lax.all_to_all(going_back, "req", split_axis=0, concat_axis=0, tiled=True)
    dec_back = jnp.dot(packer.T, came_back, preferred_element_type=jnp.float32)
    cache_mix = dec_back[:, :width_here]
    cache_spread = (
        dec_back[:, width_here : width_here + heads_here]
        + dec_back[:, width_here + heads_here : width_here + 2 * heads_here]
    )
    own_prod = dec_query.astype(jnp.float32) * dec_key.astype(jnp.float32)
    own_scores = jnp.sum(jnp.where(head_mask[:, None, :], own_prod[None], 0.0), axis=-1).T * factor
    top = jnp.maximum(cache_spread, own_scores)
    part_cache = jnp.exp(cache_spread - top)
    part_own = jnp.exp(own_scores - top)
    share_own = part_own / (part_cache + part_own)
    share_cols = jnp.sum(jnp.where(head_mask[:, None, :], share_own.T[:, :, None], 0.0), axis=0)
    dec_out = (
        (1.0 - share_cols) * cache_mix + share_cols * dec_value.astype(jnp.float32)
    ).astype(jnp.bfloat16)

    stretch_len = pre_query.shape[0]
    row_numbers = jnp.arange(stretch_len)
    pre_stack = jnp.where(head_mask[:, None, :], pre_query[None], 0).reshape(heads_here * stretch_len, width_here)
    dims = (((1,), (1,)), ((), ()))
    cache_part = lax.dot_general(pre_stack, cache_key[0], dims, preferred_element_type=jnp.float32) * factor
    self_part = lax.dot_general(pre_stack, pre_key, dims, preferred_element_type=jnp.float32) * factor
    cache_part = jnp.where((positions < stretch_start[0])[None, :], cache_part, -jnp.inf)
    causal = (row_numbers[None, :] <= row_numbers[:, None])[None]
    self_part = jnp.where(causal, self_part.reshape(heads_here, stretch_len, stretch_len), -jnp.inf).reshape(
        heads_here * stretch_len, stretch_len
    )
    highest = jnp.maximum(
        jnp.max(cache_part, axis=-1, keepdims=True), jnp.max(self_part, axis=-1, keepdims=True)
    )
    raised_cache = jnp.exp(cache_part - highest)
    raised_self = jnp.exp(self_part - highest)
    total = jnp.sum(raised_cache, axis=-1, keepdims=True) + jnp.sum(raised_self, axis=-1, keepdims=True)
    pre_mixed = jnp.dot(
        (raised_cache / total).astype(jnp.bfloat16), cache_value[0], preferred_element_type=jnp.float32
    ) + jnp.dot((raised_self / total).astype(jnp.bfloat16), pre_value, preferred_element_type=jnp.float32)
    pre_out = jnp.sum(
        jnp.where(head_mask[:, None, :], pre_mixed.reshape(heads_here, stretch_len, width_here), 0.0), axis=0
    ).astype(jnp.bfloat16)
    row_count = hidden_in.shape[0]
    half = row_count - 8 * ((row_count // 3 + 7) // 8)
    late_attn, _ = lax.optimization_barrier((pre_out[half - per_home :], going_back))
    dec_out, early_pre = lax.optimization_barrier((dec_out, pre_out[: half - per_home]))
    early_attn = jnp.concatenate([dec_out, early_pre], axis=0)
    head_me = lax.axis_index("head")
    col_start = head_me * width_here

    def feed_forward(attn_chunk, hidden_chunk):
        projected = jnp.dot(attn_chunk, out_weight, preferred_element_type=jnp.float32)
        own_cols = lax.dynamic_slice_in_dim(projected, col_start, width_here, 1) + hidden_chunk.astype(
            jnp.float32
        )
        contribution = lax.dynamic_update_slice_in_dim(projected, own_cols, col_start, 1)
        own_residual = pair_then_z_scatter(contribution.astype(jnp.bfloat16)).astype(jnp.bfloat16)
        residual = z_then_pair_gather(own_residual)
        residual_wide = residual.astype(jnp.float32)
        squares = jnp.mean(jnp.square(residual_wide), axis=-1, keepdims=True)
        normed = (residual_wide * lax.rsqrt(squares + eps_norm) * norm_gain).astype(jnp.bfloat16)
        gate_act = jnp.dot(normed, gate_weight, preferred_element_type=jnp.float32)
        up_act = jnp.dot(normed, up_weight, preferred_element_type=jnp.float32)
        hidden = (jax.nn.silu(gate_act) * up_act).astype(jnp.bfloat16)
        down_part = jnp.dot(hidden, down_weight, preferred_element_type=jnp.float32).astype(jnp.bfloat16)
        down_cols = pair_then_z_scatter(down_part)
        return (own_residual.astype(jnp.float32) + down_cols).astype(jnp.bfloat16)

    out_cols = jnp.concatenate(
        [
            feed_forward(early_attn, hidden_in[:half]),
            feed_forward(late_attn, hidden_in[half:]),
        ],
        axis=0,
    )

    slot_rows = 8 * ((2 * row_count + 8 * req_count - 1) // (8 * req_count))
    owners = row_owner[:, 0]
    onehot_owner = (owners[:, None] == jnp.arange(req_count, dtype=jnp.int32)[None, :]).astype(
        jnp.int32
    )
    before = rank_within(onehot_owner, 0)
    target = owners * slot_rows + before
    placing = (
        target[None, :] == jnp.arange(req_count * slot_rows, dtype=jnp.int32)[:, None]
    ).astype(jnp.bfloat16)
    outgoing = jnp.dot(placing, out_cols, preferred_element_type=jnp.float32).astype(jnp.bfloat16)
    arrived = lax.all_to_all(outgoing, "req", split_axis=0, concat_axis=0, tiled=True)
    return lax.all_to_all(arrived, "head", split_axis=0, concat_axis=1, tiled=True)


def solution(mesh):
    placed = (
        P("req", "head"),
        P("req", "head"),
        P("req", "head"),
        P("req", "head"),
        P("req", "head"),
        P("req", "head"),
        P("req", "head"),
        P("req", None, "head"),
        P("req", None, "head"),
        P(),
        P("req"),
        P("req"),
        P("req", None),
        P("head", None),
        P(),
        P(None, "head"),
        P(None, "head"),
        P("head", None),
    )
    return jax.shard_map(
        on_device, mesh=mesh, in_specs=placed, out_specs=P(("req", "head"), None), check_vma=False
    )
```
